128 devices in a mesh: ctx: 16 (over y_lo, z, core), head: 8 (over x, y_hi).
Axes of the slice: x: 4, y: 4 (y_hi: 2, y_lo: 2; y = y_hi * 2 + y_lo), z: 4, core: 2. Of those that a mesh axis runs over, the one named last changes fastest.
Arguments:
- hidden_in: bfloat16 [4096, 8192], P('ctx', 'head'), may hold values from -90 to 90
- query_rows: bfloat16 [4096, 8192], P('ctx', 'head'), may hold values from -5 to 5
- key_rows: bfloat16 [4096, 1024], P('ctx', 'head'), may hold values from -5 to 5
- value_rows: bfloat16 [4096, 1024], P('ctx', 'head'), may hold values from -6 to 6
- out_weight: bfloat16 [8192, 8192], P('head'), may hold values from -0.0625 to 0.0625
- grad_out: bfloat16 [4096, 8192], P('ctx', 'head'), may hold values from -6 to 6
- answer_mask: int32 [4096], P('ctx'), may hold values 0 or 1
Outputs:
- grad_query: bfloat16 [4096, 8192], P('ctx', 'head')
- grad_key: bfloat16 [4096, 1024], P('ctx', 'head')
- grad_value: bfloat16 [4096, 1024], P('ctx', 'head')
- fisher_q: float32 [16, 64], P('ctx', 'head')
- fisher_o: float32 [16, 64], P('ctx', 'head')
The draws below stay inside these ranges and needn't reach their ends.
All inputs are finite; a program needn't handle non-finite values. No bound on the sum of `answer_mask` on one device may be relied on, other than what follows from the above.
Results may differ from the reference program's by a relative error of at most 0.019.
Values may be sent and summed in bfloat16 or wider, within the bound.
No kernel may reach another device: no remote copies, remote signals or barrier semaphores. Data moves between devices by JAX's collectives and lax.ppermute only.
A program may use at most 128 MiB of HBM per device.

```python
import jax
import jax.numpy as jnp
from jax import lax

D = 8192
HEADS = 64
KVH = 8
HD = 128
TOK_DEV = 256
TOKENS = 4096


def draw_hidden_in(key, part):
    column = jnp.arange(D, dtype=jnp.float32) / (D - 1)
    factor = jax.random.uniform(jax.random.fold_in(key, 31), (D,), jnp.float32, 0.7, 1.4)
    column_scale = jnp.exp(column * jnp.log(10.0)) * factor
    base = jax.random.truncated_normal(jax.random.fold_in(key, 33), -6.0, 6.0, (TOKENS, D), jnp.float32)
    return (base * column_scale[None, :]).astype(jnp.bfloat16)


def drawn_pair(key):
    width_q = HEADS * HD
    width_k = KVH * HD
    queries = jax.random.truncated_normal(jax.random.fold_in(key, 21), -5.0, 5.0, (TOKENS, width_q), jnp.float32)
    key_table = jax.random.truncated_normal(jax.random.fold_in(key, 22), -5.0, 5.0, (TOKENS, width_k), jnp.float32)
    return (queries, key_table)


def draw_query_rows(key, part):
    return drawn_pair(key)[0].astype(jnp.bfloat16)


def draw_key_rows(key, part):
    return drawn_pair(key)[1].astype(jnp.bfloat16)


def touch_ends(drawn, key, low, top_value):
    extent = drawn.shape
    index_at = [jax.random.randint(jax.random.fold_in(key, axis), (), 0, extent[axis]) for axis in range(len(extent))]
    drawn = drawn.at[tuple(index_at)].set(low)
    longest = extent.index(max(extent))
    index_at[longest] = (index_at[longest] + 1) % extent[longest]
    return drawn.at[tuple(index_at)].set(top_value)


def shard_levels(own_key, extent, shards, low, top_value):
    def one(axis_at, blocks):
        steps = jax.random.uniform(jax.random.fold_in(jax.random.fold_in(own_key, 6), axis_at), (blocks,), jnp.float32, low / len(shards), top_value / len(shards))
        return jnp.repeat(jnp.exp(steps), extent[axis_at] // blocks).reshape((-1,) + (1,) * (len(extent) - axis_at - 1))

    factor_of = one(*shards[0])
    for cut in shards[1:]:
        factor_of = factor_of * one(*cut)
    return factor_of


def noise(stream_key, dims, spread, bound, shards=(), kind=jnp.bfloat16):
    factor_of = shard_levels(stream_key, dims, shards, -0.22, 0.18) if shards else 1.0
    result = jax.random.normal(stream_key, dims, jnp.float32) * spread * factor_of
    return jnp.minimum(jnp.maximum(result, -bound), bound).astype(kind)


def setup_inputs(seed: int = 0) -> dict:
    seeds = jax.random.split(jax.random.key(seed), 8)
    hidden_in = draw_hidden_in(jax.random.fold_in(seeds[7], 71), 0)
    query_rows = draw_query_rows(jax.random.fold_in(seeds[7], 71), 0)
    key_rows = draw_key_rows(jax.random.fold_in(seeds[7], 71), 0)
    value_rows = noise(seeds[3], (TOKENS, KVH * HD), 1.0, 6.0, ((0, 16), (1, 8)))
    out_weight = noise(seeds[4], (HEADS * HD, D), D ** -0.5, 0.0625, ((0, 8),))
    grad_out = noise(seeds[5], (TOKENS, D), 1.0, 6.0, ((0, 16), (1, 8)))
    answer_mask = touch_ends((jax.random.randint(seeds[6], (TOKENS,), 0, 4) < 1).astype(jnp.int32), jax.random.fold_in(seeds[6], 1), 0, 1)
    return {"hidden_in": hidden_in, "query_rows": query_rows, "key_rows": key_rows, "value_rows": value_rows, "out_weight": out_weight, "grad_out": grad_out, "answer_mask": answer_mask}


NEGATIVE = -1e30
EPSILON = 1e-6


def span_fisher(left_side, right_side):
    def span_squares(operands):
        product = jnp.dot(operands[0].T, operands[1], preferred_element_type=jnp.float32)
        return jnp.sum((product * product).reshape(product.shape[0], HEADS, HD), axis=(0, 2))
    squares = lax.map(span_squares, (left_side, right_side))
    return jnp.log(squares / (D * HD * TOK_DEV) + EPSILON)


def reference(hidden_in, query_rows, key_rows, value_rows, out_weight, grad_out, answer_mask):
    tokens = query_rows.shape[0]
    group_size = HEADS // KVH
    scaling = HD ** -0.5
    loss_weight = 0.25 + answer_mask.astype(jnp.float32)
    weighted = (grad_out.astype(jnp.float32) * loss_weight[:, None]).astype(jnp.bfloat16)
    grad_attended = jnp.dot(weighted, out_weight.T, preferred_element_type=jnp.float32).astype(jnp.bfloat16)
    query_heads = query_rows.reshape(tokens, KVH, group_size, HD).transpose(1, 0, 2, 3)
    key_heads = key_rows.reshape(tokens, KVH, HD).transpose(1, 0, 2)
    value_heads = value_rows.reshape(tokens, KVH, HD).transpose(1, 0, 2)
    grad_heads = grad_attended.reshape(tokens, KVH, group_size, HD).transpose(1, 0, 2, 3)
    positions = jnp.arange(tokens, dtype=jnp.int32)
    causal = positions[:, None] >= positions[None, :]

    def one_group(operands):
        query_group = operands[0].astype(jnp.float32)
        key_group = operands[1].astype(jnp.float32)
        value_group = operands[2].astype(jnp.float32)
        grad_group = operands[3].astype(jnp.float32)
        scores = jnp.einsum("tgd,kd->tgk", query_group, key_group) * scaling
        scores = jnp.where(causal[:, None, :], scores, NEGATIVE)
        row_max = jnp.max(scores, axis=-1, keepdims=True)
        log_total = row_max + jnp.log(jnp.sum(jnp.exp(scores - row_max), axis=-1, keepdims=True))
        softmax = jnp.exp(scores - log_total)
        rounded = softmax.astype(jnp.bfloat16)
        attended = jnp.einsum("tgk,kd->tgd", rounded.astype(jnp.float32), value_group).astype(jnp.bfloat16)
        row_dot = jnp.sum(grad_group * attended.astype(jnp.float32), axis=-1, keepdims=True)
        grad_prob = jnp.einsum("tgd,kd->tgk", grad_group, value_group)
        grad_score = (softmax * (grad_prob - row_dot) * scaling).astype(jnp.bfloat16)
        grad_query = jnp.einsum("tgk,kd->tgd", grad_score.astype(jnp.float32), key_group).astype(jnp.bfloat16)
        grad_key = jnp.einsum("tgk,tgd->kd", grad_score.astype(jnp.float32), query_group).astype(jnp.bfloat16)
        grad_value = jnp.einsum("tgk,tgd->kd", rounded.astype(jnp.float32), grad_group).astype(jnp.bfloat16)
        return attended, grad_query, grad_key, grad_value

    attended, grad_query, grad_key, grad_value = lax.map(one_group, (query_heads, key_heads, value_heads, grad_heads))
    attended = attended.transpose(1, 0, 2, 3).reshape(tokens, HEADS * HD)
    grad_query = grad_query.transpose(1, 0, 2, 3).reshape(tokens, HEADS * HD)
    grad_key = grad_key.transpose(1, 0, 2).reshape(tokens, KVH * HD)
    grad_value = grad_value.transpose(1, 0, 2).reshape(tokens, KVH * HD)
    span_count = tokens // TOK_DEV
    fisher_q = span_fisher(hidden_in.reshape(span_count, TOK_DEV, D), grad_query.reshape(span_count, TOK_DEV, HEADS * HD))
    fisher_o = span_fisher(weighted.reshape(span_count, TOK_DEV, D), attended.reshape(span_count, TOK_DEV, HEADS * HD))
    return grad_query, grad_key, grad_value, fisher_q, fisher_o
```

```python
import math

import jax
import jax.numpy as jnp
from jax import lax
from jax.sharding import PartitionSpec as P

D = 8192
HEADS = 64
KVH = 8
HD = 128


NEGATIVE = -1e30
EPSILON = 1e-06


def block_scores(query_group, key_block, scaling, row_pos, col_pos):
    scores = (
        jnp.einsum("tgd,kd->tgk", query_group, key_block, preferred_element_type=jnp.float32)
        * scaling
    )
    return jnp.where(row_pos[:, None, None] >= col_pos[None, None, :], scores, NEGATIVE)


def head_squares(left_side, right_side, head_dim):
    product = lax.dot_general(
        left_side, right_side, (((0,), (0,)), ((), ())), preferred_element_type=jnp.float32
    )
    shaped = (product * product).reshape(
        product.shape[0], right_side.shape[1] // head_dim, head_dim
    )
    return jnp.sum(shaped, axis=(0, 2))


def gram_pair_squares(left_gram, right_side, head_dim):
    rows = right_side.shape[0]
    right_heads = right_side.reshape(rows, right_side.shape[1] // head_dim, head_dim)
    right_gram = jnp.einsum(
        "ihd,jhd->hij", right_heads, right_heads, preferred_element_type=jnp.float32
    )
    return jnp.sum(right_gram * left_gram[None], axis=(1, 2))


def gram_squares(left_side, right_side, head_dim):
    left_gram = lax.dot_general(
        left_side, left_side, (((1,), (1,)), ((), ())), preferred_element_type=jnp.float32
    )
    return gram_pair_squares(left_gram, right_side, head_dim)


def body(hidden_in, query_rows, key_rows, value_rows, out_weight, grad_out, answer_mask):
    tok_dev = query_rows.shape[0]
    head_dim = HD
    group_size = HEADS // KVH
    local_groups = key_rows.shape[1] // head_dim
    scaling = head_dim ** (-0.5)
    own_index = lax.axis_index("ctx")
    first_row = own_index * tok_dev
    loss_weight = 0.25 + answer_mask.astype(jnp.float32)
    weighted = (grad_out.astype(jnp.float32) * loss_weight[:, None]).astype(jnp.bfloat16)
    hidden_gram = lax.psum(
        lax.dot_general(
            hidden_in, hidden_in, (((1,), (1,)), ((), ())), preferred_element_type=jnp.float32
        ),
        "head",
    )
    pair_all = lax.all_gather(
        jnp.concatenate([key_rows, value_rows], axis=1), "ctx", axis=0, tiled=True
    )
    kv_width = key_rows.shape[1]
    keys_all, values_all = (pair_all[:, :kv_width], pair_all[:, kv_width:])
    tokens = keys_all.shape[0]
    block_rows = math.gcd(512, tokens)

    def fetch(table, block_number):
        return lax.dynamic_slice_in_dim(table, block_number * block_rows, block_rows, 0)

    def column_pos(block_number):
        return block_number * block_rows + jnp.arange(block_rows, dtype=jnp.int32)

    buffer = jnp.zeros((tokens, 2 * local_groups * head_dim), jnp.float32)
    rows = query_rows.shape[0]
    row_pos = first_row + jnp.arange(rows, dtype=jnp.int32)
    needed = (first_row + rows - 1) // block_rows + 1
    query_heads = query_rows.reshape(rows, local_groups, group_size, head_dim)
    log_totals = []
    shared_head = 0
    query_group = query_heads[:, shared_head]

    def stats_step(block_number, carried):
        running_max, running_sum = carried
        key_block = fetch(keys_all, block_number)
        scores = block_scores(query_group, key_block, scaling, row_pos, column_pos(block_number))
        new_max = jnp.maximum(running_max, jnp.max(scores, axis=-1))
        running_sum = running_sum * jnp.exp(running_max - new_max) + jnp.sum(
            jnp.exp(scores - new_max[..., None]), axis=-1
        )
        return (new_max, running_sum)

    start_max = jnp.full((rows, group_size), NEGATIVE, jnp.float32)
    start_sum = jnp.zeros((rows, group_size), jnp.float32)
    running_max, running_sum = lax.fori_loop(0, needed, stats_step, (start_max, start_sum))
    log_total = running_max + jnp.log(running_sum)

    def value_step(block_number, accumulated):
        key_block = fetch(keys_all, block_number)
        value_block = fetch(values_all, block_number)
        scores = block_scores(query_group, key_block, scaling, row_pos, column_pos(block_number))
        rounded = jnp.exp(scores - log_total[..., None]).astype(jnp.bfloat16)
        return accumulated + jnp.einsum(
            "tgk,kd->tgd", rounded, value_block, preferred_element_type=jnp.float32
        )

    accumulated = lax.fori_loop(
        0, needed, value_step, jnp.zeros((rows, group_size, head_dim), jnp.float32)
    )
    log_totals.append(log_total)
    attended_list = [accumulated.astype(jnp.bfloat16)]
    attended_part = jnp.stack(attended_list, axis=1).reshape(
        rows, local_groups * group_size * head_dim
    )
    log_totals, attended = (log_totals, attended_part)
    piece_part = lax.all_gather(weighted, "head", axis=1, tiled=True)
    grad_sum = lax.dot_general(
        piece_part, out_weight, (((1,), (1,)), ((), ())), preferred_element_type=jnp.float32
    )
    grad_sum, squares_out = (grad_sum, gram_squares(piece_part, attended, head_dim))
    grad_attended, squares_out = (grad_sum.astype(jnp.bfloat16), squares_out)
    backward_buffer = buffer
    rows = query_rows.shape[0]
    backward_row_pos = first_row + jnp.arange(rows, dtype=jnp.int32)
    needed = (first_row + rows - 1) // block_rows + 1
    query_heads = query_rows.reshape(rows, local_groups, group_size, head_dim)
    grad_heads = grad_attended.reshape(rows, local_groups, group_size, head_dim)
    attended_heads = attended.reshape(rows, local_groups, group_size, head_dim)
    shared_head = 0
    backward_query_group = query_heads[:, shared_head]
    grad_group = grad_heads[:, shared_head]
    backward_log_total = log_totals[shared_head]
    row_dot = jnp.sum(
        grad_group.astype(jnp.float32) * attended_heads[:, shared_head].astype(jnp.float32), axis=-1
    )
    key_column = jnp.int32(shared_head * head_dim)
    value_column = jnp.int32((local_groups + shared_head) * head_dim)

    def back_step(block_number, carried):
        query_sum, buffer_now = carried
        key_block = fetch(keys_all, block_number)
        value_block = fetch(values_all, block_number)
        scores = block_scores(
            backward_query_group, key_block, scaling, backward_row_pos, column_pos(block_number)
        )
        softmax = jnp.exp(scores - backward_log_total[..., None])
        rounded = softmax.astype(jnp.bfloat16)
        grad_prob = jnp.einsum(
            "tgd,kd->tgk", grad_group, value_block, preferred_element_type=jnp.float32
        )
        grad_score = (softmax * (grad_prob - row_dot[..., None]) * scaling).astype(jnp.bfloat16)
        query_sum = query_sum + jnp.einsum(
            "tgk,kd->tgd", grad_score, key_block, preferred_element_type=jnp.float32
        )
        key_part = jnp.einsum(
            "tgk,tgd->kd", grad_score, backward_query_group, preferred_element_type=jnp.float32
        )
        value_part = jnp.einsum(
            "tgk,tgd->kd", rounded, grad_group, preferred_element_type=jnp.float32
        )
        row_start = (block_number * block_rows).astype(jnp.int32)
        old_key = lax.dynamic_slice(buffer_now, (row_start, key_column), (block_rows, head_dim))
        buffer_now = lax.dynamic_update_slice(
            buffer_now, old_key + key_part, (row_start, key_column)
        )
        old_value = lax.dynamic_slice(buffer_now, (row_start, value_column), (block_rows, head_dim))
        buffer_now = lax.dynamic_update_slice(
            buffer_now, old_value + value_part, (row_start, value_column)
        )
        return (query_sum, buffer_now)

    start_query = jnp.zeros((rows, group_size, head_dim), jnp.float32)
    query_sum, backward_buffer = lax.fori_loop(0, needed, back_step, (start_query, backward_buffer))
    query_grads = [query_sum.astype(jnp.bfloat16)]
    grad_query_part = jnp.stack(query_grads, axis=1).reshape(
        rows, local_groups * group_size * head_dim
    )
    key_sums = lax.psum_scatter(
        backward_buffer.astype(jnp.bfloat16), "ctx", scatter_dimension=0, tiled=True
    ).astype(jnp.float32)
    grad_key = key_sums[:, : local_groups * head_dim].astype(jnp.bfloat16)
    grad_value = key_sums[:, local_groups * head_dim :].astype(jnp.bfloat16)
    squares_query = gram_pair_squares(hidden_gram, grad_query_part, head_dim)
    normal_size = D * head_dim * tok_dev
    fisher_q = jnp.log(squares_query / normal_size + EPSILON).reshape(1, -1)
    fisher_o = jnp.log(squares_out / normal_size + EPSILON).reshape(1, -1)
    return (grad_query_part, grad_key, grad_value, fisher_q, fisher_o)


def solution(mesh):
    return jax.shard_map(
        body,
        mesh=mesh,
        in_specs=(
            P("ctx", "head"),
            P("ctx", "head"),
            P("ctx", "head"),
            P("ctx", "head"),
            P("head", None),
            P("ctx", "head"),
            P("ctx"),
        ),
        out_specs=(
            P("ctx", "head"),
            P("ctx", "head"),
            P("ctx", "head"),
            P("ctx", "head"),
            P("ctx", "head"),
        ),
        check_vma=False,
    )
```

```python
import math

import jax
import jax.numpy as jnp
from jax import lax
from jax.sharding import PartitionSpec as P

D = 8192
HEADS = 64
KVH = 8
HD = 128


NEGATIVE = -1e30
EPSILON = 1e-06


def block_scores(query_group, key_block, scaling, row_pos, col_pos):
    scores = (
        jnp.einsum("tgd,kd->tgk", query_group, key_block, preferred_element_type=jnp.float32)
        * scaling
    )
    return jnp.where(row_pos[:, None, None] >= col_pos[None, None, :], scores, NEGATIVE)


def head_squares(left_side, right_side, head_dim):
    product = lax.dot_general(
        left_side, right_side, (((0,), (0,)), ((), ())), preferred_element_type=jnp.float32
    )
    shaped = (product * product).reshape(
        product.shape[0], right_side.shape[1] // head_dim, head_dim
    )
    return jnp.sum(shaped, axis=(0, 2))


def butterfly_sum(value, axis_name):
    size = lax.axis_size(axis_name)
    stride = 1
    while stride < size:
        pairs = [(i, i ^ stride) for i in range(size)]
        value = value + lax.ppermute(value, axis_name, pairs)
        stride *= 2
    return value


def gram_pair_squares(left_gram, right_side, head_dim):
    rows = right_side.shape[0]
    right_heads = right_side.reshape(rows, right_side.shape[1] // head_dim, head_dim)
    right_gram = jnp.einsum(
        "ihd,jhd->hij", right_heads, right_heads, preferred_element_type=jnp.float32
    )
    return jnp.sum(right_gram * left_gram[None], axis=(1, 2))


def gram_squares(left_side, right_side, head_dim):
    left_gram = lax.dot_general(
        left_side, left_side, (((1,), (1,)), ((), ())), preferred_element_type=jnp.float32
    )
    return gram_pair_squares(left_gram, right_side, head_dim)


def body(hidden_in, query_rows, key_rows, value_rows, out_weight, grad_out, answer_mask):
    tok_dev = query_rows.shape[0]
    head_dim = HD
    group_size = HEADS // KVH
    local_groups = key_rows.shape[1] // head_dim
    scaling = head_dim ** (-0.5)
    own_index = lax.axis_index("ctx")
    first_row = own_index * tok_dev
    loss_weight = 0.25 + answer_mask.astype(jnp.float32)
    weighted = (grad_out.astype(jnp.float32) * loss_weight[:, None]).astype(jnp.bfloat16)
    hidden_gram = butterfly_sum(
        lax.dot_general(
            hidden_in, hidden_in, (((1,), (1,)), ((), ())), preferred_element_type=jnp.float32
        ),
        "head",
    )
    pair_all = lax.all_gather(
        jnp.concatenate([key_rows, value_rows], axis=1), "ctx", axis=0, tiled=True
    )
    kv_width = key_rows.shape[1]
    keys_all, values_all = (pair_all[:, :kv_width], pair_all[:, kv_width:])
    tokens = keys_all.shape[0]
    block_rows = math.gcd(512, tokens)

    def fetch(table, block_number):
        return lax.dynamic_slice_in_dim(table, block_number * block_rows, block_rows, 0)

    def column_pos(block_number):
        return block_number * block_rows + jnp.arange(block_rows, dtype=jnp.int32)

    buffer = jnp.zeros((tokens, 2 * local_groups * head_dim), jnp.float32)
    rows = query_rows.shape[0]
    row_pos = first_row + jnp.arange(rows, dtype=jnp.int32)
    needed = (first_row + rows - 1) // block_rows + 1
    query_heads = query_rows.reshape(rows, local_groups, group_size, head_dim)
    log_totals = []
    shared_head = 0
    query_group = query_heads[:, shared_head]

    def stats_step(block_number, carried):
        running_max, running_sum = carried
        key_block = fetch(keys_all, block_number)
        scores = block_scores(query_group, key_block, scaling, row_pos, column_pos(block_number))
        new_max = jnp.maximum(running_max, jnp.max(scores, axis=-1))
        running_sum = running_sum * jnp.exp(running_max - new_max) + jnp.sum(
            jnp.exp(scores - new_max[..., None]), axis=-1
        )
        return (new_max, running_sum)

    start_max = jnp.full((rows, group_size), NEGATIVE, jnp.float32)
    start_sum = jnp.zeros((rows, group_size), jnp.float32)
    running_max, running_sum = lax.fori_loop(0, needed, stats_step, (start_max, start_sum))
    log_total = running_max + jnp.log(running_sum)

    def value_step(block_number, accumulated):
        key_block = fetch(keys_all, block_number)
        value_block = fetch(values_all, block_number)
        scores = block_scores(query_group, key_block, scaling, row_pos, column_pos(block_number))
        rounded = jnp.exp(scores - log_total[..., None]).astype(jnp.bfloat16)
        return accumulated + jnp.einsum(
            "tgk,kd->tgd", rounded, value_block, preferred_element_type=jnp.float32
        )

    accumulated = lax.fori_loop(
        0, needed, value_step, jnp.zeros((rows, group_size, head_dim), jnp.float32)
    )
    log_totals.append(log_total)
    attended_list = [accumulated.astype(jnp.bfloat16)]
    attended_part = jnp.stack(attended_list, axis=1).reshape(
        rows, local_groups * group_size * head_dim
    )
    log_totals, attended = (log_totals, attended_part)
    piece_part = lax.all_gather(weighted, "head", axis=1, tiled=True)
    grad_sum = lax.dot_general(
        piece_part, out_weight, (((1,), (1,)), ((), ())), preferred_element_type=jnp.float32
    )
    grad_sum, squares_out = (grad_sum, gram_squares(piece_part, attended, head_dim))
    grad_attended, squares_out = (grad_sum.astype(jnp.bfloat16), squares_out)
    backward_buffer = buffer
    rows = query_rows.shape[0]
    backward_row_pos = first_row + jnp.arange(rows, dtype=jnp.int32)
    needed = (first_row + rows - 1) // block_rows + 1
    query_heads = query_rows.reshape(rows, local_groups, group_size, head_dim)
    grad_heads = grad_attended.reshape(rows, local_groups, group_size, head_dim)
    attended_heads = attended.reshape(rows, local_groups, group_size, head_dim)
    shared_head = 0
    backward_query_group = query_heads[:, shared_head]
    grad_group = grad_heads[:, shared_head]
    backward_log_total = log_totals[shared_head]
    row_dot = jnp.sum(
        grad_group.astype(jnp.float32) * attended_heads[:, shared_head].astype(jnp.float32), axis=-1
    )
    key_column = jnp.int32(shared_head * head_dim)
    value_column = jnp.int32((local_groups + shared_head) * head_dim)

    def back_step(block_number, carried):
        query_sum, buffer_now = carried
        key_block = fetch(keys_all, block_number)
        value_block = fetch(values_all, block_number)
        scores = block_scores(
            backward_query_group, key_block, scaling, backward_row_pos, column_pos(block_number)
        )
        softmax = jnp.exp(scores - backward_log_total[..., None])
        rounded = softmax.astype(jnp.bfloat16)
        grad_prob = jnp.einsum(
            "tgd,kd->tgk", grad_group, value_block, preferred_element_type=jnp.float32
        )
        grad_score = (softmax * (grad_prob - row_dot[..., None]) * scaling).astype(jnp.bfloat16)
        query_sum = query_sum + jnp.einsum(
            "tgk,kd->tgd", grad_score, key_block, preferred_element_type=jnp.float32
        )
        key_part = jnp.einsum(
            "tgk,tgd->kd", grad_score, backward_query_group, preferred_element_type=jnp.float32
        )
        value_part = jnp.einsum(
            "tgk,tgd->kd", rounded, grad_group, preferred_element_type=jnp.float32
        )
        row_start = (block_number * block_rows).astype(jnp.int32)
        old_key = lax.dynamic_slice(buffer_now, (row_start, key_column), (block_rows, head_dim))
        buffer_now = lax.dynamic_update_slice(
            buffer_now, old_key + key_part, (row_start, key_column)
        )
        old_value = lax.dynamic_slice(buffer_now, (row_start, value_column), (block_rows, head_dim))
        buffer_now = lax.dynamic_update_slice(
            buffer_now, old_value + value_part, (row_start, value_column)
        )
        return (query_sum, buffer_now)

    start_query = jnp.zeros((rows, group_size, head_dim), jnp.float32)
    query_sum, backward_buffer = lax.fori_loop(0, needed, back_step, (start_query, backward_buffer))
    query_grads = [query_sum.astype(jnp.bfloat16)]
    grad_query_part = jnp.stack(query_grads, axis=1).reshape(
        rows, local_groups * group_size * head_dim
    )
    key_sums = lax.psum_scatter(
        backward_buffer.astype(jnp.bfloat16), "ctx", scatter_dimension=0, tiled=True
    ).astype(jnp.float32)
    grad_key = key_sums[:, : local_groups * head_dim].astype(jnp.bfloat16)
    grad_value = key_sums[:, local_groups * head_dim :].astype(jnp.bfloat16)
    squares_query = gram_pair_squares(hidden_gram, grad_query_part, head_dim)
    normal_size = D * head_dim * tok_dev
    fisher_q = jnp.log(squares_query / normal_size + EPSILON).reshape(1, -1)
    fisher_o = jnp.log(squares_out / normal_size + EPSILON).reshape(1, -1)
    return (grad_query_part, grad_key, grad_value, fisher_q, fisher_o)


def solution(mesh):
    return jax.shard_map(
        body,
        mesh=mesh,
        in_specs=(
            P("ctx", "head"),
            P("ctx", "head"),
            P("ctx", "head"),
            P("ctx", "head"),
            P("head", None),
            P("ctx", "head"),
            P("ctx"),
        ),
        out_specs=(
            P("ctx", "head"),
            P("ctx", "head"),
            P("ctx", "head"),
            P("ctx", "head"),
            P("ctx", "head"),
        ),
        check_vma=False,
    )
```

```python
import math

import jax
import jax.numpy as jnp
from jax import lax
from jax.experimental import pallas as pl
from jax.experimental.pallas import tpu as pltpu
from jax.sharding import PartitionSpec as P

D = 8192
HEADS = 64
KVH = 8
HD = 128


NEGATIVE = -1e30
EPSILON = 1e-06


def block_scores(query_group, key_block, scaling, row_pos, col_pos):
    scores = (
        jnp.einsum("tgd,kd->tgk", query_group, key_block, preferred_element_type=jnp.float32)
        * scaling
    )
    return jnp.where(row_pos[:, None, None] >= col_pos[None, None, :], scores, NEGATIVE)


def head_squares(left_side, right_side, head_dim):
    product = lax.dot_general(
        left_side, right_side, (((0,), (0,)), ((), ())), preferred_element_type=jnp.float32
    )
    shaped = (product * product).reshape(
        product.shape[0], right_side.shape[1] // head_dim, head_dim
    )
    return jnp.sum(shaped, axis=(0, 2))


def flash_backward(query_rows, grad_attended, keys_all, values_all, log_total, row_dot, first_row, head_dim, block_rows):
    rows, width = query_rows.shape
    heads = width // head_dim
    tokens = keys_all.shape[0]
    blocks = tokens // block_rows
    scaling = head_dim ** (-0.5)
    needed = (first_row + rows - 1) // block_rows + 1
    scalars = jnp.stack([needed, first_row]).astype(jnp.int32)

    def kernel(scalar_ref, q_ref, do_ref, k_ref, v_ref, lt_ref, rd_ref, dq_ref, dkv_ref, dq_acc):
        j = pl.program_id(0)

        @pl.when(j == 0)
        def _():
            dq_acc[...] = jnp.zeros_like(dq_acc)

        @pl.when(j < scalar_ref[0])
        def _():
            k = k_ref[...]
            v = v_ref[...]
            row_pos = scalar_ref[1] + lax.broadcasted_iota(jnp.int32, (rows, block_rows), 0)
            col_pos = j * block_rows + lax.broadcasted_iota(jnp.int32, (rows, block_rows), 1)
            keep = row_pos >= col_pos
            dk = jnp.zeros((block_rows, head_dim), jnp.float32)
            dv = jnp.zeros((block_rows, head_dim), jnp.float32)
            for h in range(heads):
                cols = slice(h * head_dim, (h + 1) * head_dim)
                q = q_ref[:, cols]
                do = do_ref[:, cols]
                s = lax.dot_general(q, k, (((1,), (1,)), ((), ())), preferred_element_type=jnp.float32) * scaling
                s = jnp.where(keep, s, NEGATIVE)
                p = jnp.exp(s - lt_ref[:, h : h + 1])
                dp = lax.dot_general(do, v, (((1,), (1,)), ((), ())), preferred_element_type=jnp.float32)
                ds = (p * (dp - rd_ref[:, h : h + 1]) * scaling).astype(jnp.bfloat16)
                dq_acc[:, cols] += jnp.dot(ds, k, preferred_element_type=jnp.float32)
                dk += lax.dot_general(ds, q, (((0,), (0,)), ((), ())), preferred_element_type=jnp.float32)
                dv += lax.dot_general(p.astype(jnp.bfloat16), do, (((0,), (0,)), ((), ())), preferred_element_type=jnp.float32)
            dkv_ref[:, :head_dim] = dk.astype(dkv_ref.dtype)
            dkv_ref[:, head_dim:] = dv.astype(dkv_ref.dtype)

        @pl.when(j >= scalar_ref[0])
        def _():
            dkv_ref[...] = jnp.zeros_like(dkv_ref)

        @pl.when(j == blocks - 1)
        def _():
            dq_ref[...] = dq_acc[...].astype(dq_ref.dtype)

    def kv_map(j, s):
        return (jnp.minimum(j, s[0] - 1), 0)

    full = lambda j, s: (0, 0)
    grid_spec = pltpu.PrefetchScalarGridSpec(
        num_scalar_prefetch=1,
        grid=(blocks,),
        in_specs=[
            pl.BlockSpec((rows, width), full),
            pl.BlockSpec((rows, width), full),
            pl.BlockSpec((block_rows, head_dim), kv_map),
            pl.BlockSpec((block_rows, head_dim), kv_map),
            pl.BlockSpec((rows, heads), full),
            pl.BlockSpec((rows, heads), full),
        ],
        out_specs=[
            pl.BlockSpec((rows, width), full),
            pl.BlockSpec((block_rows, 2 * head_dim), lambda j, s: (j, 0)),
        ],
        scratch_shapes=[pltpu.VMEM((rows, width), jnp.float32)],
    )
    return pl.pallas_call(
        kernel,
        grid_spec=grid_spec,
        out_shape=[
            jax.ShapeDtypeStruct((rows, width), jnp.bfloat16),
            jax.ShapeDtypeStruct((tokens, 2 * head_dim), jnp.bfloat16),
        ],
        compiler_params=pltpu.CompilerParams(dimension_semantics=("arbitrary",)),
    )(scalars, query_rows, grad_attended, keys_all, values_all, log_total, row_dot)


def butterfly_sum(value, axis_name):
    size = lax.axis_size(axis_name)
    stride = 1
    while stride < size:
        pairs = [(i, i ^ stride) for i in range(size)]
        value = value + lax.ppermute(value, axis_name, pairs)
        stride *= 2
    return value


def gram_pair_squares(left_gram, right_side, head_dim):
    rows = right_side.shape[0]
    right_heads = right_side.reshape(rows, right_side.shape[1] // head_dim, head_dim)
    right_gram = jnp.einsum(
        "ihd,jhd->hij", right_heads, right_heads, preferred_element_type=jnp.float32
    )
    return jnp.sum(right_gram * left_gram[None], axis=(1, 2))


def gram_squares(left_side, right_side, head_dim):
    left_gram = lax.dot_general(
        left_side, left_side, (((1,), (1,)), ((), ())), preferred_element_type=jnp.float32
    )
    return gram_pair_squares(left_gram, right_side, head_dim)


def body(hidden_in, query_rows, key_rows, value_rows, out_weight, grad_out, answer_mask):
    tok_dev = query_rows.shape[0]
    head_dim = HD
    group_size = HEADS // KVH
    local_groups = key_rows.shape[1] // head_dim
    scaling = head_dim ** (-0.5)
    own_index = lax.axis_index("ctx")
    first_row = own_index * tok_dev
    loss_weight = 0.25 + answer_mask.astype(jnp.float32)
    weighted = (grad_out.astype(jnp.float32) * loss_weight[:, None]).astype(jnp.bfloat16)
    hidden_gram = butterfly_sum(
        lax.dot_general(
            hidden_in, hidden_in, (((1,), (1,)), ((), ())), preferred_element_type=jnp.float32
        ),
        "head",
    )
    pair_all = lax.all_gather(
        jnp.concatenate([key_rows, value_rows], axis=1), "ctx", axis=0, tiled=True
    )
    kv_width = key_rows.shape[1]
    keys_all, values_all = (pair_all[:, :kv_width], pair_all[:, kv_width:])
    tokens = keys_all.shape[0]
    block_rows = math.gcd(512, tokens)

    def fetch(table, block_number):
        return lax.dynamic_slice_in_dim(table, block_number * block_rows, block_rows, 0)

    def column_pos(block_number):
        return block_number * block_rows + jnp.arange(block_rows, dtype=jnp.int32)

    buffer = jnp.zeros((tokens, 2 * local_groups * head_dim), jnp.float32)
    rows = query_rows.shape[0]
    row_pos = first_row + jnp.arange(rows, dtype=jnp.int32)
    needed = (first_row + rows - 1) // block_rows + 1
    query_heads = query_rows.reshape(rows, local_groups, group_size, head_dim)
    log_totals = []
    shared_head = 0
    query_group = query_heads[:, shared_head]

    def stats_step(block_number, carried):
        running_max, running_sum = carried
        key_block = fetch(keys_all, block_number)
        scores = block_scores(query_group, key_block, scaling, row_pos, column_pos(block_number))
        new_max = jnp.maximum(running_max, jnp.max(scores, axis=-1))
        running_sum = running_sum * jnp.exp(running_max - new_max) + jnp.sum(
            jnp.exp(scores - new_max[..., None]), axis=-1
        )
        return (new_max, running_sum)

    start_max = jnp.full((rows, group_size), NEGATIVE, jnp.float32)
    start_sum = jnp.zeros((rows, group_size), jnp.float32)
    running_max, running_sum = lax.fori_loop(0, needed, stats_step, (start_max, start_sum))
    log_total = running_max + jnp.log(running_sum)

    def value_step(block_number, accumulated):
        key_block = fetch(keys_all, block_number)
        value_block = fetch(values_all, block_number)
        scores = block_scores(query_group, key_block, scaling, row_pos, column_pos(block_number))
        rounded = jnp.exp(scores - log_total[..., None]).astype(jnp.bfloat16)
        return accumulated + jnp.einsum(
            "tgk,kd->tgd", rounded, value_block, preferred_element_type=jnp.float32
        )

    accumulated = lax.fori_loop(
        0, needed, value_step, jnp.zeros((rows, group_size, head_dim), jnp.float32)
    )
    log_totals.append(log_total)
    attended_list = [accumulated.astype(jnp.bfloat16)]
    attended_part = jnp.stack(attended_list, axis=1).reshape(
        rows, local_groups * group_size * head_dim
    )
    log_totals, attended = (log_totals, attended_part)
    piece_part = lax.all_gather(weighted, "head", axis=1, tiled=True)
    grad_sum = lax.dot_general(
        piece_part, out_weight, (((1,), (1,)), ((), ())), preferred_element_type=jnp.float32
    )
    grad_sum, squares_out = (grad_sum, gram_squares(piece_part, attended, head_dim))
    grad_attended, squares_out = (grad_sum.astype(jnp.bfloat16), squares_out)
    backward_buffer = buffer
    rows = query_rows.shape[0]
    backward_row_pos = first_row + jnp.arange(rows, dtype=jnp.int32)
    needed = (first_row + rows - 1) // block_rows + 1
    query_heads = query_rows.reshape(rows, local_groups, group_size, head_dim)
    grad_heads = grad_attended.reshape(rows, local_groups, group_size, head_dim)
    attended_heads = attended.reshape(rows, local_groups, group_size, head_dim)
    shared_head = 0
    backward_query_group = query_heads[:, shared_head]
    grad_group = grad_heads[:, shared_head]
    backward_log_total = log_totals[shared_head]
    row_dot = jnp.sum(
        grad_group.astype(jnp.float32) * attended_heads[:, shared_head].astype(jnp.float32), axis=-1
    )
    grad_query_part, backward_buffer = flash_backward(
        backward_query_group.reshape(rows, group_size * head_dim),
        grad_group.reshape(rows, group_size * head_dim),
        keys_all,
        values_all,
        backward_log_total,
        row_dot,
        first_row,
        head_dim,
        block_rows,
    )
    key_sums = lax.psum_scatter(
        backward_buffer, "ctx", scatter_dimension=0, tiled=True
    ).astype(jnp.float32)
    grad_key = key_sums[:, : local_groups * head_dim].astype(jnp.bfloat16)
    grad_value = key_sums[:, local_groups * head_dim :].astype(jnp.bfloat16)
    squares_query = gram_pair_squares(hidden_gram, grad_query_part, head_dim)
    normal_size = D * head_dim * tok_dev
    fisher_q = jnp.log(squares_query / normal_size + EPSILON).reshape(1, -1)
    fisher_o = jnp.log(squares_out / normal_size + EPSILON).reshape(1, -1)
    return (grad_query_part, grad_key, grad_value, fisher_q, fisher_o)


def solution(mesh):
    return jax.shard_map(
        body,
        mesh=mesh,
        in_specs=(
            P("ctx", "head"),
            P("ctx", "head"),
            P("ctx", "head"),
            P("ctx", "head"),
            P("head", None),
            P("ctx", "head"),
            P("ctx"),
        ),
        out_specs=(
            P("ctx", "head"),
            P("ctx", "head"),
            P("ctx", "head"),
            P("ctx", "head"),
            P("ctx", "head"),
        ),
        check_vma=False,
    )
```

```python
import math

import jax
import jax.numpy as jnp
from jax import lax
from jax.experimental import pallas as pl
from jax.experimental.pallas import tpu as pltpu
from jax.sharding import PartitionSpec as P

D = 8192
HEADS = 64
KVH = 8
HD = 128


NEGATIVE = -1e30
EPSILON = 1e-06


def block_scores(query_group, key_block, scaling, row_pos, col_pos):
    scores = (
        jnp.einsum("tgd,kd->tgk", query_group, key_block, preferred_element_type=jnp.float32)
        * scaling
    )
    return jnp.where(row_pos[:, None, None] >= col_pos[None, None, :], scores, NEGATIVE)


def head_squares(left_side, right_side, head_dim):
    product = lax.dot_general(
        left_side, right_side, (((0,), (0,)), ((), ())), preferred_element_type=jnp.float32
    )
    shaped = (product * product).reshape(
        product.shape[0], right_side.shape[1] // head_dim, head_dim
    )
    return jnp.sum(shaped, axis=(0, 2))


def flash_backward(query_rows, grad_attended, keys_all, values_all, log_total, row_dot, first_row, head_dim, block_rows):
    rows, width = query_rows.shape
    heads = width // head_dim
    tokens = keys_all.shape[0]
    blocks = tokens // block_rows
    scaling = head_dim ** (-0.5)
    needed = (first_row + rows - 1) // block_rows + 1
    scalars = jnp.stack([needed, first_row]).astype(jnp.int32)

    def kernel(scalar_ref, q_ref, do_ref, k_ref, v_ref, lt_ref, rd_ref, dq_ref, dkv_ref, dq_acc):
        j = pl.program_id(0)

        @pl.when(j == 0)
        def _():
            dq_acc[...] = jnp.zeros_like(dq_acc)

        @pl.when(j < scalar_ref[0])
        def _():
            k = k_ref[...]
            v = v_ref[...]
            row_pos = scalar_ref[1] + lax.broadcasted_iota(jnp.int32, (rows, block_rows), 0)
            col_pos = j * block_rows + lax.broadcasted_iota(jnp.int32, (rows, block_rows), 1)
            keep = row_pos >= col_pos
            dk = jnp.zeros((block_rows, head_dim), jnp.float32)
            dv = jnp.zeros((block_rows, head_dim), jnp.float32)
            for h in range(heads):
                cols = slice(h * head_dim, (h + 1) * head_dim)
                q = q_ref[:, cols]
                do = do_ref[:, cols]
                s = lax.dot_general(q, k, (((1,), (1,)), ((), ())), preferred_element_type=jnp.float32) * scaling
                s = jnp.where(keep, s, NEGATIVE)
                p = jnp.exp(s - lt_ref[:, h : h + 1])
                dp = lax.dot_general(do, v, (((1,), (1,)), ((), ())), preferred_element_type=jnp.float32)
                ds = (p * (dp - rd_ref[:, h : h + 1]) * scaling).astype(jnp.bfloat16)
                dq_acc[:, cols] += jnp.dot(ds, k, preferred_element_type=jnp.float32)
                dk += lax.dot_general(ds, q, (((0,), (0,)), ((), ())), preferred_element_type=jnp.float32)
                dv += lax.dot_general(p.astype(jnp.bfloat16), do, (((0,), (0,)), ((), ())), preferred_element_type=jnp.float32)
            dkv_ref[:, :head_dim] = dk.astype(dkv_ref.dtype)
            dkv_ref[:, head_dim:] = dv.astype(dkv_ref.dtype)

        @pl.when(j >= scalar_ref[0])
        def _():
            dkv_ref[...] = jnp.zeros_like(dkv_ref)

        @pl.when(j == blocks - 1)
        def _():
            dq_ref[...] = dq_acc[...].astype(dq_ref.dtype)

    def kv_map(j, s):
        return (jnp.minimum(j, s[0] - 1), 0)

    full = lambda j, s: (0, 0)
    grid_spec = pltpu.PrefetchScalarGridSpec(
        num_scalar_prefetch=1,
        grid=(blocks,),
        in_specs=[
            pl.BlockSpec((rows, width), full),
            pl.BlockSpec((rows, width), full),
            pl.BlockSpec((block_rows, head_dim), kv_map),
            pl.BlockSpec((block_rows, head_dim), kv_map),
            pl.BlockSpec((rows, heads), full),
            pl.BlockSpec((rows, heads), full),
        ],
        out_specs=[
            pl.BlockSpec((rows, width), full),
            pl.BlockSpec((block_rows, 2 * head_dim), lambda j, s: (j, 0)),
        ],
        scratch_shapes=[pltpu.VMEM((rows, width), jnp.float32)],
    )
    return pl.pallas_call(
        kernel,
        grid_spec=grid_spec,
        out_shape=[
            jax.ShapeDtypeStruct((rows, width), jnp.bfloat16),
            jax.ShapeDtypeStruct((tokens, 2 * head_dim), jnp.bfloat16),
        ],
        compiler_params=pltpu.CompilerParams(dimension_semantics=("arbitrary",)),
    )(scalars, query_rows, grad_attended, keys_all, values_all, log_total, row_dot)


def butterfly_gather(value, axis_name):
    size = lax.axis_size(axis_name)
    own = lax.axis_index(axis_name)
    held = value[None]
    stride = size // 2
    bits = 0
    while stride >= 1:
        pairs = [(i, i ^ stride) for i in range(size)]
        other = lax.ppermute(held, axis_name, pairs)
        low = (own & stride) == 0
        held = jnp.where(
            low, jnp.concatenate([held, other], 0), jnp.concatenate([other, held], 0)
        )
        stride //= 2
        bits += 1
    held = held.reshape((2,) * bits + value.shape)
    held = held.transpose(tuple(range(bits))[::-1] + tuple(range(bits, bits + value.ndim)))
    return held.reshape((size * value.shape[0],) + value.shape[1:])


def butterfly_sum(value, axis_name):
    size = lax.axis_size(axis_name)
    stride = 1
    while stride < size:
        pairs = [(i, i ^ stride) for i in range(size)]
        value = value + lax.ppermute(value, axis_name, pairs)
        stride *= 2
    return value


def gram_pair_squares(left_gram, right_side, head_dim):
    rows = right_side.shape[0]
    right_heads = right_side.reshape(rows, right_side.shape[1] // head_dim, head_dim)
    right_gram = jnp.einsum(
        "ihd,jhd->hij", right_heads, right_heads, preferred_element_type=jnp.float32
    )
    return jnp.sum(right_gram * left_gram[None], axis=(1, 2))


def gram_squares(left_side, right_side, head_dim):
    left_gram = lax.dot_general(
        left_side, left_side, (((1,), (1,)), ((), ())), preferred_element_type=jnp.float32
    )
    return gram_pair_squares(left_gram, right_side, head_dim)


def body(hidden_in, query_rows, key_rows, value_rows, out_weight, grad_out, answer_mask):
    tok_dev = query_rows.shape[0]
    head_dim = HD
    group_size = HEADS // KVH
    local_groups = key_rows.shape[1] // head_dim
    scaling = head_dim ** (-0.5)
    own_index = lax.axis_index("ctx")
    first_row = own_index * tok_dev
    loss_weight = 0.25 + answer_mask.astype(jnp.float32)
    weighted = (grad_out.astype(jnp.float32) * loss_weight[:, None]).astype(jnp.bfloat16)
    hidden_gram = butterfly_sum(
        lax.dot_general(
            hidden_in, hidden_in, (((1,), (1,)), ((), ())), preferred_element_type=jnp.float32
        ),
        "head",
    )
    piece_part = lax.all_gather(weighted, "head", axis=1, tiled=True)
    pair, _ = lax.optimization_barrier(
        (jnp.concatenate([key_rows, value_rows], axis=1), weighted)
    )
    pair_all = butterfly_gather(pair, "ctx")
    kv_width = key_rows.shape[1]
    keys_all, values_all = (pair_all[:, :kv_width], pair_all[:, kv_width:])
    tokens = keys_all.shape[0]
    block_rows = math.gcd(512, tokens)

    def fetch(table, block_number):
        return lax.dynamic_slice_in_dim(table, block_number * block_rows, block_rows, 0)

    def column_pos(block_number):
        return block_number * block_rows + jnp.arange(block_rows, dtype=jnp.int32)

    buffer = jnp.zeros((tokens, 2 * local_groups * head_dim), jnp.float32)
    rows = query_rows.shape[0]
    row_pos = first_row + jnp.arange(rows, dtype=jnp.int32)
    needed = (first_row + rows - 1) // block_rows + 1
    query_heads = query_rows.reshape(rows, local_groups, group_size, head_dim)
    log_totals = []
    shared_head = 0
    query_group = query_heads[:, shared_head]

    def stats_step(block_number, carried):
        running_max, running_sum = carried
        key_block = fetch(keys_all, block_number)
        scores = block_scores(query_group, key_block, scaling, row_pos, column_pos(block_number))
        new_max = jnp.maximum(running_max, jnp.max(scores, axis=-1))
        running_sum = running_sum * jnp.exp(running_max - new_max) + jnp.sum(
            jnp.exp(scores - new_max[..., None]), axis=-1
        )
        return (new_max, running_sum)

    start_max = jnp.full((rows, group_size), NEGATIVE, jnp.float32)
    start_sum = jnp.zeros((rows, group_size), jnp.float32)
    running_max, running_sum = lax.fori_loop(0, needed, stats_step, (start_max, start_sum))
    log_total = running_max + jnp.log(running_sum)

    def value_step(block_number, accumulated):
        key_block = fetch(keys_all, block_number)
        value_block = fetch(values_all, block_number)
        scores = block_scores(query_group, key_block, scaling, row_pos, column_pos(block_number))
        rounded = jnp.exp(scores - log_total[..., None]).astype(jnp.bfloat16)
        return accumulated + jnp.einsum(
            "tgk,kd->tgd", rounded, value_block, preferred_element_type=jnp.float32
        )

    accumulated = lax.fori_loop(
        0, needed, value_step, jnp.zeros((rows, group_size, head_dim), jnp.float32)
    )
    log_totals.append(log_total)
    attended_list = [accumulated.astype(jnp.bfloat16)]
    attended_part = jnp.stack(attended_list, axis=1).reshape(
        rows, local_groups * group_size * head_dim
    )
    log_totals, attended = (log_totals, attended_part)
    grad_sum = lax.dot_general(
        piece_part, out_weight, (((1,), (1,)), ((), ())), preferred_element_type=jnp.float32
    )
    grad_sum, squares_out = (grad_sum, gram_squares(piece_part, attended, head_dim))
    grad_attended, squares_out = (grad_sum.astype(jnp.bfloat16), squares_out)
    backward_buffer = buffer
    rows = query_rows.shape[0]
    backward_row_pos = first_row + jnp.arange(rows, dtype=jnp.int32)
    needed = (first_row + rows - 1) // block_rows + 1
    query_heads = query_rows.reshape(rows, local_groups, group_size, head_dim)
    grad_heads = grad_attended.reshape(rows, local_groups, group_size, head_dim)
    attended_heads = attended.reshape(rows, local_groups, group_size, head_dim)
    shared_head = 0
    backward_query_group = query_heads[:, shared_head]
    grad_group = grad_heads[:, shared_head]
    backward_log_total = log_totals[shared_head]
    row_dot = jnp.sum(
        grad_group.astype(jnp.float32) * attended_heads[:, shared_head].astype(jnp.float32), axis=-1
    )
    grad_query_part, backward_buffer = flash_backward(
        backward_query_group.reshape(rows, group_size * head_dim),
        grad_group.reshape(rows, group_size * head_dim),
        keys_all,
        values_all,
        backward_log_total,
        row_dot,
        first_row,
        head_dim,
        block_rows,
    )
    key_sums = lax.psum_scatter(
        backward_buffer, "ctx", scatter_dimension=0, tiled=True
    ).astype(jnp.float32)
    grad_key = key_sums[:, : local_groups * head_dim].astype(jnp.bfloat16)
    grad_value = key_sums[:, local_groups * head_dim :].astype(jnp.bfloat16)
    squares_query = gram_pair_squares(hidden_gram, grad_query_part, head_dim)
    normal_size = D * head_dim * tok_dev
    fisher_q = jnp.log(squares_query / normal_size + EPSILON).reshape(1, -1)
    fisher_o = jnp.log(squares_out / normal_size + EPSILON).reshape(1, -1)
    return (grad_query_part, grad_key, grad_value, fisher_q, fisher_o)


def solution(mesh):
    return jax.shard_map(
        body,
        mesh=mesh,
        in_specs=(
            P("ctx", "head"),
            P("ctx", "head"),
            P("ctx", "head"),
            P("ctx", "head"),
            P("head", None),
            P("ctx", "head"),
            P("ctx"),
        ),
        out_specs=(
            P("ctx", "head"),
            P("ctx", "head"),
            P("ctx", "head"),
            P("ctx", "head"),
            P("ctx", "head"),
        ),
        check_vma=False,
    )
```

```python
import math

import jax
import jax.numpy as jnp
from jax import lax
from jax.experimental import pallas as pl
from jax.experimental.pallas import tpu as pltpu
from jax.sharding import PartitionSpec as P

D = 8192
HEADS = 64
KVH = 8
HD = 128


NEGATIVE = -1e30
EPSILON = 1e-06


def block_scores(query_group, key_block, scaling, row_pos, col_pos):
    scores = (
        jnp.einsum("tgd,kd->tgk", query_group, key_block, preferred_element_type=jnp.float32)
        * scaling
    )
    return jnp.where(row_pos[:, None, None] >= col_pos[None, None, :], scores, NEGATIVE)


def head_squares(left_side, right_side, head_dim):
    product = lax.dot_general(
        left_side, right_side, (((0,), (0,)), ((), ())), preferred_element_type=jnp.float32
    )
    shaped = (product * product).reshape(
        product.shape[0], right_side.shape[1] // head_dim, head_dim
    )
    return jnp.sum(shaped, axis=(0, 2))


def flash_backward(query_rows, grad_attended, keys_all, values_all, log_total, row_dot, first_row, head_dim, block_rows):
    rows, width = query_rows.shape
    heads = width // head_dim
    tokens = keys_all.shape[0]
    blocks = tokens // block_rows
    scaling = head_dim ** (-0.5)
    needed = (first_row + rows - 1) // block_rows + 1
    scalars = jnp.stack([needed, first_row]).astype(jnp.int32)

    def kernel(scalar_ref, q_ref, do_ref, k_ref, v_ref, lt_ref, rd_ref, dq_ref, dkv_ref, dq_acc):
        j = pl.program_id(0)

        @pl.when(j == 0)
        def _():
            dq_acc[...] = jnp.zeros_like(dq_acc)

        @pl.when(j < scalar_ref[0])
        def _():
            k = k_ref[...]
            v = v_ref[...]
            row_pos = scalar_ref[1] + lax.broadcasted_iota(jnp.int32, (rows, block_rows), 0)
            col_pos = j * block_rows + lax.broadcasted_iota(jnp.int32, (rows, block_rows), 1)
            keep = row_pos >= col_pos
            dk = jnp.zeros((block_rows, head_dim), jnp.float32)
            dv = jnp.zeros((block_rows, head_dim), jnp.float32)
            for h in range(heads):
                cols = slice(h * head_dim, (h + 1) * head_dim)
                q = q_ref[:, cols]
                do = do_ref[:, cols]
                s = lax.dot_general(q, k, (((1,), (1,)), ((), ())), preferred_element_type=jnp.float32) * scaling
                s = jnp.where(keep, s, NEGATIVE)
                p = jnp.exp(s - lt_ref[:, h : h + 1])
                dp = lax.dot_general(do, v, (((1,), (1,)), ((), ())), preferred_element_type=jnp.float32)
                ds = (p * (dp - rd_ref[:, h : h + 1]) * scaling).astype(jnp.bfloat16)
                dq_acc[:, cols] += jnp.dot(ds, k, preferred_element_type=jnp.float32)
                dk += lax.dot_general(ds, q, (((0,), (0,)), ((), ())), preferred_element_type=jnp.float32)
                dv += lax.dot_general(p.astype(jnp.bfloat16), do, (((0,), (0,)), ((), ())), preferred_element_type=jnp.float32)
            dkv_ref[:, :head_dim] = dk.astype(dkv_ref.dtype)
            dkv_ref[:, head_dim:] = dv.astype(dkv_ref.dtype)

        @pl.when(j >= scalar_ref[0])
        def _():
            dkv_ref[...] = jnp.zeros_like(dkv_ref)

        @pl.when(j == blocks - 1)
        def _():
            dq_ref[...] = dq_acc[...].astype(dq_ref.dtype)

    def kv_map(j, s):
        return (jnp.minimum(j, s[0] - 1), 0)

    full = lambda j, s: (0, 0)
    grid_spec = pltpu.PrefetchScalarGridSpec(
        num_scalar_prefetch=1,
        grid=(blocks,),
        in_specs=[
            pl.BlockSpec((rows, width), full),
            pl.BlockSpec((rows, width), full),
            pl.BlockSpec((block_rows, head_dim), kv_map),
            pl.BlockSpec((block_rows, head_dim), kv_map),
            pl.BlockSpec((rows, heads), full),
            pl.BlockSpec((rows, heads), full),
        ],
        out_specs=[
            pl.BlockSpec((rows, width), full),
            pl.BlockSpec((block_rows, 2 * head_dim), lambda j, s: (j, 0)),
        ],
        scratch_shapes=[pltpu.VMEM((rows, width), jnp.float32)],
    )
    return pl.pallas_call(
        kernel,
        grid_spec=grid_spec,
        out_shape=[
            jax.ShapeDtypeStruct((rows, width), jnp.bfloat16),
            jax.ShapeDtypeStruct((tokens, 2 * head_dim), jnp.bfloat16),
        ],
        compiler_params=pltpu.CompilerParams(dimension_semantics=("arbitrary",)),
    )(scalars, query_rows, grad_attended, keys_all, values_all, log_total, row_dot)


def butterfly_gather(value, axis_name):
    size = lax.axis_size(axis_name)
    own = lax.axis_index(axis_name)
    held = value[None]
    stride = size // 2
    bits = 0
    while stride >= 1:
        pairs = [(i, i ^ stride) for i in range(size)]
        other = lax.ppermute(held, axis_name, pairs)
        low = (own & stride) == 0
        held = jnp.where(
            low, jnp.concatenate([held, other], 0), jnp.concatenate([other, held], 0)
        )
        stride //= 2
        bits += 1
    held = held.reshape((2,) * bits + value.shape)
    held = held.transpose(tuple(range(bits))[::-1] + tuple(range(bits, bits + value.ndim)))
    return held.reshape((size * value.shape[0],) + value.shape[1:])


def causal_gather(value, axis_name):
    size = lax.axis_size(axis_name)
    own = lax.axis_index(axis_name)
    received = [value]
    for shift in range(1, size):
        pairs = [(i, i + shift) for i in range(size - shift)]
        received.append(lax.ppermute(value, axis_name, pairs))
    by_shift = jnp.stack(received[::-1], 0)
    doubled = jnp.concatenate([by_shift, by_shift], 0)
    blocks = lax.dynamic_slice_in_dim(doubled, size - 1 - own, size, 0)
    return blocks.reshape((size * value.shape[0],) + value.shape[1:])


def causal_reduce(parts, axis_name):
    size = lax.axis_size(axis_name)
    own = lax.axis_index(axis_name)
    total = lax.dynamic_index_in_dim(parts, own, 0, keepdims=False).astype(jnp.float32)
    for shift in range(1, size):
        pairs = [(i, i - shift) for i in range(shift, size)]
        sent = lax.dynamic_index_in_dim(parts, jnp.maximum(own - shift, 0), 0, keepdims=False)
        total = total + lax.ppermute(sent, axis_name, pairs).astype(jnp.float32)
    return total


def butterfly_sum(value, axis_name):
    size = lax.axis_size(axis_name)
    stride = 1
    while stride < size:
        pairs = [(i, i ^ stride) for i in range(size)]
        value = value + lax.ppermute(value, axis_name, pairs)
        stride *= 2
    return value


def gram_pair_squares(left_gram, right_side, head_dim):
    rows = right_side.shape[0]
    right_heads = right_side.reshape(rows, right_side.shape[1] // head_dim, head_dim)
    right_gram = jnp.einsum(
        "ihd,jhd->hij", right_heads, right_heads, preferred_element_type=jnp.float32
    )
    return jnp.sum(right_gram * left_gram[None], axis=(1, 2))


def gram_squares(left_side, right_side, head_dim):
    left_gram = lax.dot_general(
        left_side, left_side, (((1,), (1,)), ((), ())), preferred_element_type=jnp.float32
    )
    return gram_pair_squares(left_gram, right_side, head_dim)


def body(hidden_in, query_rows, key_rows, value_rows, out_weight, grad_out, answer_mask):
    tok_dev = query_rows.shape[0]
    head_dim = HD
    group_size = HEADS // KVH
    local_groups = key_rows.shape[1] // head_dim
    scaling = head_dim ** (-0.5)
    own_index = lax.axis_index("ctx")
    first_row = own_index * tok_dev
    loss_weight = 0.25 + answer_mask.astype(jnp.float32)
    weighted = (grad_out.astype(jnp.float32) * loss_weight[:, None]).astype(jnp.bfloat16)
    hidden_gram = butterfly_sum(
        lax.dot_general(
            hidden_in, hidden_in, (((1,), (1,)), ((), ())), preferred_element_type=jnp.float32
        ),
        "head",
    )
    piece_part = (
        lax.all_gather(grad_out, "head", axis=1, tiled=True).astype(jnp.float32)
        * loss_weight[:, None]
    ).astype(jnp.bfloat16)
    pair_all = causal_gather(jnp.concatenate([key_rows, value_rows], axis=1), "ctx")
    kv_width = key_rows.shape[1]
    keys_all, values_all = (pair_all[:, :kv_width], pair_all[:, kv_width:])
    tokens = keys_all.shape[0]
    block_rows = math.gcd(512, tokens)

    def fetch(table, block_number):
        return lax.dynamic_slice_in_dim(table, block_number * block_rows, block_rows, 0)

    def column_pos(block_number):
        return block_number * block_rows + jnp.arange(block_rows, dtype=jnp.int32)

    buffer = jnp.zeros((tokens, 2 * local_groups * head_dim), jnp.float32)
    rows = query_rows.shape[0]
    row_pos = first_row + jnp.arange(rows, dtype=jnp.int32)
    needed = (first_row + rows - 1) // block_rows + 1
    query_heads = query_rows.reshape(rows, local_groups, group_size, head_dim)
    log_totals = []
    shared_head = 0
    query_group = query_heads[:, shared_head]

    def stats_step(block_number, carried):
        running_max, running_sum = carried
        key_block = fetch(keys_all, block_number)
        scores = block_scores(query_group, key_block, scaling, row_pos, column_pos(block_number))
        new_max = jnp.maximum(running_max, jnp.max(scores, axis=-1))
        running_sum = running_sum * jnp.exp(running_max - new_max) + jnp.sum(
            jnp.exp(scores - new_max[..., None]), axis=-1
        )
        return (new_max, running_sum)

    start_max = jnp.full((rows, group_size), NEGATIVE, jnp.float32)
    start_sum = jnp.zeros((rows, group_size), jnp.float32)
    running_max, running_sum = lax.fori_loop(0, needed, stats_step, (start_max, start_sum))
    log_total = running_max + jnp.log(running_sum)

    def value_step(block_number, accumulated):
        key_block = fetch(keys_all, block_number)
        value_block = fetch(values_all, block_number)
        scores = block_scores(query_group, key_block, scaling, row_pos, column_pos(block_number))
        rounded = jnp.exp(scores - log_total[..., None]).astype(jnp.bfloat16)
        return accumulated + jnp.einsum(
            "tgk,kd->tgd", rounded, value_block, preferred_element_type=jnp.float32
        )

    accumulated = lax.fori_loop(
        0, needed, value_step, jnp.zeros((rows, group_size, head_dim), jnp.float32)
    )
    log_totals.append(log_total)
    attended_list = [accumulated.astype(jnp.bfloat16)]
    attended_part = jnp.stack(attended_list, axis=1).reshape(
        rows, local_groups * group_size * head_dim
    )
    log_totals, attended = (log_totals, attended_part)
    grad_sum = lax.dot_general(
        piece_part, out_weight, (((1,), (1,)), ((), ())), preferred_element_type=jnp.float32
    )
    grad_sum, squares_out = (grad_sum, gram_squares(piece_part, attended, head_dim))
    grad_attended, squares_out = (grad_sum.astype(jnp.bfloat16), squares_out)
    backward_buffer = buffer
    rows = query_rows.shape[0]
    backward_row_pos = first_row + jnp.arange(rows, dtype=jnp.int32)
    needed = (first_row + rows - 1) // block_rows + 1
    query_heads = query_rows.reshape(rows, local_groups, group_size, head_dim)
    grad_heads = grad_attended.reshape(rows, local_groups, group_size, head_dim)
    attended_heads = attended.reshape(rows, local_groups, group_size, head_dim)
    shared_head = 0
    backward_query_group = query_heads[:, shared_head]
    grad_group = grad_heads[:, shared_head]
    backward_log_total = log_totals[shared_head]
    row_dot = jnp.sum(
        grad_group.astype(jnp.float32) * attended_heads[:, shared_head].astype(jnp.float32), axis=-1
    )
    grad_query_part, backward_buffer = flash_backward(
        backward_query_group.reshape(rows, group_size * head_dim),
        grad_group.reshape(rows, group_size * head_dim),
        keys_all,
        values_all,
        backward_log_total,
        row_dot,
        first_row,
        head_dim,
        block_rows,
    )
    ctx_size = lax.axis_size("ctx")
    key_sums = causal_reduce(
        backward_buffer.reshape((ctx_size, tokens // ctx_size) + backward_buffer.shape[1:]), "ctx"
    )
    grad_key = key_sums[:, : local_groups * head_dim].astype(jnp.bfloat16)
    grad_value = key_sums[:, local_groups * head_dim :].astype(jnp.bfloat16)
    squares_query = gram_pair_squares(hidden_gram, grad_query_part, head_dim)
    normal_size = D * head_dim * tok_dev
    fisher_q = jnp.log(squares_query / normal_size + EPSILON).reshape(1, -1)
    fisher_o = jnp.log(squares_out / normal_size + EPSILON).reshape(1, -1)
    return (grad_query_part, grad_key, grad_value, fisher_q, fisher_o)


def solution(mesh):
    return jax.shard_map(
        body,
        mesh=mesh,
        in_specs=(
            P("ctx", "head"),
            P("ctx", "head"),
            P("ctx", "head"),
            P("ctx", "head"),
            P("head", None),
            P("ctx", "head"),
            P("ctx"),
        ),
        out_specs=(
            P("ctx", "head"),
            P("ctx", "head"),
            P("ctx", "head"),
            P("ctx", "head"),
            P("ctx", "head"),
        ),
        check_vma=False,
    )
```

```python
import math

import jax
import jax.numpy as jnp
from jax import lax
from jax.experimental import pallas as pl
from jax.experimental.pallas import tpu as pltpu
from jax.sharding import PartitionSpec as P

D = 8192
HEADS = 64
KVH = 8
HD = 128


NEGATIVE = -1e30
EPSILON = 1e-06


def block_scores(query_group, key_block, scaling, row_pos, col_pos):
    scores = (
        jnp.einsum("tgd,kd->tgk", query_group, key_block, preferred_element_type=jnp.float32)
        * scaling
    )
    return jnp.where(row_pos[:, None, None] >= col_pos[None, None, :], scores, NEGATIVE)


def head_squares(left_side, right_side, head_dim):
    product = lax.dot_general(
        left_side, right_side, (((0,), (0,)), ((), ())), preferred_element_type=jnp.float32
    )
    shaped = (product * product).reshape(
        product.shape[0], right_side.shape[1] // head_dim, head_dim
    )
    return jnp.sum(shaped, axis=(0, 2))


def flash_backward(query_rows, grad_attended, keys_all, values_all, log_total, row_dot, first_row, head_dim, block_rows):
    rows, width = query_rows.shape
    heads = width // head_dim
    tokens = keys_all.shape[0]
    blocks = tokens // block_rows
    scaling = head_dim ** (-0.5)
    needed = (first_row + rows - 1) // block_rows + 1
    scalars = jnp.stack([needed, first_row]).astype(jnp.int32)

    def kernel(scalar_ref, q_ref, do_ref, k_ref, v_ref, lt_ref, rd_ref, dq_ref, dkv_ref, dq_acc):
        j = pl.program_id(0)

        @pl.when(j == 0)
        def _():
            dq_acc[...] = jnp.zeros_like(dq_acc)

        def block(masked):
            k = k_ref[...]
            v = v_ref[...]
            row_pos = scalar_ref[1] + lax.broadcasted_iota(jnp.int32, (rows, block_rows), 0)
            col_pos = j * block_rows + lax.broadcasted_iota(jnp.int32, (rows, block_rows), 1)
            keep = row_pos >= col_pos
            dk = jnp.zeros((block_rows, head_dim), jnp.float32)
            dv = jnp.zeros((block_rows, head_dim), jnp.float32)
            for h in range(heads):
                cols = slice(h * head_dim, (h + 1) * head_dim)
                q = q_ref[:, cols]
                do = do_ref[:, cols]
                s = lax.dot_general(q, k, (((1,), (1,)), ((), ())), preferred_element_type=jnp.float32) * scaling
                if masked:
                    s = jnp.where(keep, s, NEGATIVE)
                p = jnp.exp(s - lt_ref[:, h : h + 1])
                dp = lax.dot_general(do, v, (((1,), (1,)), ((), ())), preferred_element_type=jnp.float32)
                ds = (p * (dp - rd_ref[:, h : h + 1]) * scaling).astype(jnp.bfloat16)
                dq_acc[:, cols] += jnp.dot(ds, k, preferred_element_type=jnp.float32)
                dk += lax.dot_general(ds, q, (((0,), (0,)), ((), ())), preferred_element_type=jnp.float32)
                dv += lax.dot_general(p.astype(jnp.bfloat16), do, (((0,), (0,)), ((), ())), preferred_element_type=jnp.float32)
            dkv_ref[:, :head_dim] = dk.astype(dkv_ref.dtype)
            dkv_ref[:, head_dim:] = dv.astype(dkv_ref.dtype)

        below = j * block_rows + block_rows - 1 <= scalar_ref[1]

        @pl.when(jnp.logical_and(j < scalar_ref[0], below))
        def _():
            block(False)

        @pl.when(jnp.logical_and(j < scalar_ref[0], jnp.logical_not(below)))
        def _():
            block(True)

        @pl.when(j >= scalar_ref[0])
        def _():
            dkv_ref[...] = jnp.zeros_like(dkv_ref)

        @pl.when(j == blocks - 1)
        def _():
            dq_ref[...] = dq_acc[...].astype(dq_ref.dtype)

    def kv_map(j, s):
        return (jnp.minimum(j, s[0] - 1), 0)

    full = lambda j, s: (0, 0)
    grid_spec = pltpu.PrefetchScalarGridSpec(
        num_scalar_prefetch=1,
        grid=(blocks,),
        in_specs=[
            pl.BlockSpec((rows, width), full),
            pl.BlockSpec((rows, width), full),
            pl.BlockSpec((block_rows, head_dim), kv_map),
            pl.BlockSpec((block_rows, head_dim), kv_map),
            pl.BlockSpec((rows, heads), full),
            pl.BlockSpec((rows, heads), full),
        ],
        out_specs=[
            pl.BlockSpec((rows, width), full),
            pl.BlockSpec((block_rows, 2 * head_dim), lambda j, s: (j, 0)),
        ],
        scratch_shapes=[pltpu.VMEM((rows, width), jnp.float32)],
    )
    return pl.pallas_call(
        kernel,
        grid_spec=grid_spec,
        out_shape=[
            jax.ShapeDtypeStruct((rows, width), jnp.bfloat16),
            jax.ShapeDtypeStruct((tokens, 2 * head_dim), jnp.bfloat16),
        ],
        compiler_params=pltpu.CompilerParams(dimension_semantics=("arbitrary",)),
    )(scalars, query_rows, grad_attended, keys_all, values_all, log_total, row_dot)


def butterfly_gather(value, axis_name):
    size = lax.axis_size(axis_name)
    own = lax.axis_index(axis_name)
    held = value[None]
    stride = size // 2
    bits = 0
    while stride >= 1:
        pairs = [(i, i ^ stride) for i in range(size)]
        other = lax.ppermute(held, axis_name, pairs)
        low = (own & stride) == 0
        held = jnp.where(
            low, jnp.concatenate([held, other], 0), jnp.concatenate([other, held], 0)
        )
        stride //= 2
        bits += 1
    held = held.reshape((2,) * bits + value.shape)
    held = held.transpose(tuple(range(bits))[::-1] + tuple(range(bits, bits + value.ndim)))
    return held.reshape((size * value.shape[0],) + value.shape[1:])


def causal_gather(value, axis_name):
    size = lax.axis_size(axis_name)
    own = lax.axis_index(axis_name)
    received = [value]
    for shift in range(1, size):
        pairs = [(i, i + shift) for i in range(size - shift)]
        received.append(lax.ppermute(value, axis_name, pairs))
    by_shift = jnp.stack(received[::-1], 0)
    doubled = jnp.concatenate([by_shift, by_shift], 0)
    blocks = lax.dynamic_slice_in_dim(doubled, size - 1 - own, size, 0)
    return blocks.reshape((size * value.shape[0],) + value.shape[1:])


def causal_reduce(parts, axis_name):
    size = lax.axis_size(axis_name)
    own = lax.axis_index(axis_name)
    total = lax.dynamic_index_in_dim(parts, own, 0, keepdims=False).astype(jnp.float32)
    for shift in range(1, size):
        pairs = [(i, i - shift) for i in range(shift, size)]
        sent = lax.dynamic_index_in_dim(parts, jnp.maximum(own - shift, 0), 0, keepdims=False)
        total = total + lax.ppermute(sent, axis_name, pairs).astype(jnp.float32)
    return total


def halving_reduce(parts, axis_name):
    size = lax.axis_size(axis_name)
    own = lax.axis_index(axis_name)
    held = parts.astype(jnp.float32)
    stride = 1
    while stride < size:
        halves = held.reshape((held.shape[0] // 2, 2) + held.shape[1:])
        high = (own & stride) != 0
        keep = jnp.where(high, halves[:, 1], halves[:, 0])
        send = jnp.where(high, halves[:, 0], halves[:, 1]).astype(parts.dtype)
        pairs = [(i, i ^ stride) for i in range(size)]
        held = keep + lax.ppermute(send, axis_name, pairs).astype(jnp.float32)
        stride *= 2
    return held[0]


def butterfly_sum(value, axis_name):
    size = lax.axis_size(axis_name)
    stride = 1
    while stride < size:
        pairs = [(i, i ^ stride) for i in range(size)]
        value = value + lax.ppermute(value, axis_name, pairs)
        stride *= 2
    return value


def gram_pair_squares(left_gram, right_side, head_dim):
    rows = right_side.shape[0]
    right_heads = right_side.reshape(rows, right_side.shape[1] // head_dim, head_dim)
    right_gram = jnp.einsum(
        "ihd,jhd->hij", right_heads, right_heads, preferred_element_type=jnp.float32
    )
    return jnp.sum(right_gram * left_gram[None], axis=(1, 2))


def gram_squares(left_side, right_side, head_dim):
    left_gram = lax.dot_general(
        left_side, left_side, (((1,), (1,)), ((), ())), preferred_element_type=jnp.float32
    )
    return gram_pair_squares(left_gram, right_side, head_dim)


def body(hidden_in, query_rows, key_rows, value_rows, out_weight, grad_out, answer_mask):
    tok_dev = query_rows.shape[0]
    head_dim = HD
    group_size = HEADS // KVH
    local_groups = key_rows.shape[1] // head_dim
    scaling = head_dim ** (-0.5)
    own_index = lax.axis_index("ctx")
    first_row = own_index * tok_dev
    loss_weight = 0.25 + answer_mask.astype(jnp.float32)
    weighted = (grad_out.astype(jnp.float32) * loss_weight[:, None]).astype(jnp.bfloat16)
    hidden_gram = butterfly_sum(
        lax.dot_general(
            hidden_in, hidden_in, (((1,), (1,)), ((), ())), preferred_element_type=jnp.float32
        ),
        "head",
    )
    piece_part = (
        lax.all_gather(grad_out, "head", axis=1, tiled=True).astype(jnp.float32)
        * loss_weight[:, None]
    ).astype(jnp.bfloat16)
    pair_all = causal_gather(jnp.concatenate([key_rows, value_rows], axis=1), "ctx")
    kv_width = key_rows.shape[1]
    keys_all, values_all = (pair_all[:, :kv_width], pair_all[:, kv_width:])
    tokens = keys_all.shape[0]
    block_rows = math.gcd(512, tokens)

    def fetch(table, block_number):
        return lax.dynamic_slice_in_dim(table, block_number * block_rows, block_rows, 0)

    def column_pos(block_number):
        return block_number * block_rows + jnp.arange(block_rows, dtype=jnp.int32)

    buffer = jnp.zeros((tokens, 2 * local_groups * head_dim), jnp.float32)
    rows = query_rows.shape[0]
    row_pos = first_row + jnp.arange(rows, dtype=jnp.int32)
    needed = (first_row + rows - 1) // block_rows + 1
    query_heads = query_rows.reshape(rows, local_groups, group_size, head_dim)
    log_totals = []
    shared_head = 0
    query_group = query_heads[:, shared_head]

    def stats_step(block_number, carried):
        running_max, running_sum = carried
        key_block = fetch(keys_all, block_number)
        scores = block_scores(query_group, key_block, scaling, row_pos, column_pos(block_number))
        new_max = jnp.maximum(running_max, jnp.max(scores, axis=-1))
        running_sum = running_sum * jnp.exp(running_max - new_max) + jnp.sum(
            jnp.exp(scores - new_max[..., None]), axis=-1
        )
        return (new_max, running_sum)

    start_max = jnp.full((rows, group_size), NEGATIVE, jnp.float32)
    start_sum = jnp.zeros((rows, group_size), jnp.float32)
    running_max, running_sum = lax.fori_loop(0, needed, stats_step, (start_max, start_sum))
    log_total = running_max + jnp.log(running_sum)

    def value_step(block_number, accumulated):
        key_block = fetch(keys_all, block_number)
        value_block = fetch(values_all, block_number)
        scores = block_scores(query_group, key_block, scaling, row_pos, column_pos(block_number))
        rounded = jnp.exp(scores - log_total[..., None]).astype(jnp.bfloat16)
        return accumulated + jnp.einsum(
            "tgk,kd->tgd", rounded, value_block, preferred_element_type=jnp.float32
        )

    accumulated = lax.fori_loop(
        0, needed, value_step, jnp.zeros((rows, group_size, head_dim), jnp.float32)
    )
    log_totals.append(log_total)
    attended_list = [accumulated.astype(jnp.bfloat16)]
    attended_part = jnp.stack(attended_list, axis=1).reshape(
        rows, local_groups * group_size * head_dim
    )
    log_totals, attended = (log_totals, attended_part)
    grad_sum = lax.dot_general(
        piece_part, out_weight, (((1,), (1,)), ((), ())), preferred_element_type=jnp.float32
    )
    grad_sum, squares_out = (grad_sum, gram_squares(piece_part, attended, head_dim))
    grad_attended, squares_out = (grad_sum.astype(jnp.bfloat16), squares_out)
    backward_buffer = buffer
    rows = query_rows.shape[0]
    backward_row_pos = first_row + jnp.arange(rows, dtype=jnp.int32)
    needed = (first_row + rows - 1) // block_rows + 1
    query_heads = query_rows.reshape(rows, local_groups, group_size, head_dim)
    grad_heads = grad_attended.reshape(rows, local_groups, group_size, head_dim)
    attended_heads = attended.reshape(rows, local_groups, group_size, head_dim)
    shared_head = 0
    backward_query_group = query_heads[:, shared_head]
    grad_group = grad_heads[:, shared_head]
    backward_log_total = log_totals[shared_head]
    row_dot = jnp.sum(
        grad_group.astype(jnp.float32) * attended_heads[:, shared_head].astype(jnp.float32), axis=-1
    )
    grad_query_part, backward_buffer = flash_backward(
        backward_query_group.reshape(rows, group_size * head_dim),
        grad_group.reshape(rows, group_size * head_dim),
        keys_all,
        values_all,
        backward_log_total,
        row_dot,
        first_row,
        head_dim,
        block_rows,
    )
    ctx_size = lax.axis_size("ctx")
    key_sums = halving_reduce(
        backward_buffer.reshape((ctx_size, tokens // ctx_size) + backward_buffer.shape[1:]), "ctx"
    )
    grad_key = key_sums[:, : local_groups * head_dim].astype(jnp.bfloat16)
    grad_value = key_sums[:, local_groups * head_dim :].astype(jnp.bfloat16)
    squares_query = gram_pair_squares(hidden_gram, grad_query_part, head_dim)
    normal_size = D * head_dim * tok_dev
    fisher_q = jnp.log(squares_query / normal_size + EPSILON).reshape(1, -1)
    fisher_o = jnp.log(squares_out / normal_size + EPSILON).reshape(1, -1)
    return (grad_query_part, grad_key, grad_value, fisher_q, fisher_o)


def solution(mesh):
    return jax.shard_map(
        body,
        mesh=mesh,
        in_specs=(
            P("ctx", "head"),
            P("ctx", "head"),
            P("ctx", "head"),
            P("ctx", "head"),
            P("head", None),
            P("ctx", "head"),
            P("ctx"),
        ),
        out_specs=(
            P("ctx", "head"),
            P("ctx", "head"),
            P("ctx", "head"),
            P("ctx", "head"),
            P("ctx", "head"),
        ),
        check_vma=False,
    )
```

```python
import math

import jax
import jax.numpy as jnp
from jax import lax
from jax.experimental import pallas as pl
from jax.experimental.pallas import tpu as pltpu
from jax.sharding import PartitionSpec as P

D = 8192
HEADS = 64
KVH = 8
HD = 128


NEGATIVE = -1e30
EPSILON = 1e-06


def block_scores(query_group, key_block, scaling, row_pos, col_pos):
    scores = (
        jnp.einsum("tgd,kd->tgk", query_group, key_block, preferred_element_type=jnp.float32)
        * scaling
    )
    return jnp.where(row_pos[:, None, None] >= col_pos[None, None, :], scores, NEGATIVE)


def head_squares(left_side, right_side, head_dim):
    product = lax.dot_general(
        left_side, right_side, (((0,), (0,)), ((), ())), preferred_element_type=jnp.float32
    )
    shaped = (product * product).reshape(
        product.shape[0], right_side.shape[1] // head_dim, head_dim
    )
    return jnp.sum(shaped, axis=(0, 2))


def flash_backward(query_rows, grad_attended, keys_all, values_all, log_total, row_dot, first_row, head_dim, block_rows):
    rows, width = query_rows.shape
    heads = width // head_dim
    tokens = keys_all.shape[0]
    blocks = tokens // block_rows
    scaling = head_dim ** (-0.5)
    needed = (first_row + rows - 1) // block_rows + 1
    scalars = jnp.stack([needed, first_row]).astype(jnp.int32)

    def kernel(scalar_ref, q_ref, do_ref, k_ref, v_ref, lt_ref, rd_ref, dq_ref, dkv_ref, dq_acc):
        j = pl.program_id(0)

        @pl.when(j == 0)
        def _():
            dq_acc[...] = jnp.zeros_like(dq_acc)

        def block(masked):
            k = k_ref[...]
            v = v_ref[...]
            row_pos = scalar_ref[1] + lax.broadcasted_iota(jnp.int32, (rows, block_rows), 0)
            col_pos = j * block_rows + lax.broadcasted_iota(jnp.int32, (rows, block_rows), 1)
            keep = row_pos >= col_pos
            dk = jnp.zeros((block_rows, head_dim), jnp.float32)
            dv = jnp.zeros((block_rows, head_dim), jnp.float32)
            for h in range(heads):
                cols = slice(h * head_dim, (h + 1) * head_dim)
                q = q_ref[:, cols]
                do = do_ref[:, cols]
                s = lax.dot_general(q, k, (((1,), (1,)), ((), ())), preferred_element_type=jnp.float32) * scaling
                if masked:
                    s = jnp.where(keep, s, NEGATIVE)
                p = jnp.exp(s - lt_ref[:, h : h + 1])
                dp = lax.dot_general(do, v, (((1,), (1,)), ((), ())), preferred_element_type=jnp.float32)
                ds = (p * (dp - rd_ref[:, h : h + 1]) * scaling).astype(jnp.bfloat16)
                dq_acc[:, cols] += jnp.dot(ds, k, preferred_element_type=jnp.float32)
                dk += lax.dot_general(ds, q, (((0,), (0,)), ((), ())), preferred_element_type=jnp.float32)
                dv += lax.dot_general(p.astype(jnp.bfloat16), do, (((0,), (0,)), ((), ())), preferred_element_type=jnp.float32)
            dkv_ref[:, :head_dim] = dk.astype(dkv_ref.dtype)
            dkv_ref[:, head_dim:] = dv.astype(dkv_ref.dtype)

        below = j * block_rows + block_rows - 1 <= scalar_ref[1]

        @pl.when(jnp.logical_and(j < scalar_ref[0], below))
        def _():
            block(False)

        @pl.when(jnp.logical_and(j < scalar_ref[0], jnp.logical_not(below)))
        def _():
            block(True)

        @pl.when(j >= scalar_ref[0])
        def _():
            dkv_ref[...] = jnp.zeros_like(dkv_ref)

        @pl.when(j == blocks - 1)
        def _():
            dq_ref[...] = dq_acc[...].astype(dq_ref.dtype)

    def kv_map(j, s):
        return (jnp.minimum(j, s[0] - 1), 0)

    full = lambda j, s: (0, 0)
    grid_spec = pltpu.PrefetchScalarGridSpec(
        num_scalar_prefetch=1,
        grid=(blocks,),
        in_specs=[
            pl.BlockSpec((rows, width), full),
            pl.BlockSpec((rows, width), full),
            pl.BlockSpec((block_rows, head_dim), kv_map),
            pl.BlockSpec((block_rows, head_dim), kv_map),
            pl.BlockSpec((rows, heads), full),
            pl.BlockSpec((rows, heads), full),
        ],
        out_specs=[
            pl.BlockSpec((rows, width), full),
            pl.BlockSpec((block_rows, 2 * head_dim), lambda j, s: (j, 0)),
        ],
        scratch_shapes=[pltpu.VMEM((rows, width), jnp.float32)],
    )
    return pl.pallas_call(
        kernel,
        grid_spec=grid_spec,
        out_shape=[
            jax.ShapeDtypeStruct((rows, width), jnp.bfloat16),
            jax.ShapeDtypeStruct((tokens, 2 * head_dim), jnp.bfloat16),
        ],
        compiler_params=pltpu.CompilerParams(dimension_semantics=("arbitrary",)),
    )(scalars, query_rows, grad_attended, keys_all, values_all, log_total, row_dot)


def butterfly_gather(value, axis_name):
    size = lax.axis_size(axis_name)
    own = lax.axis_index(axis_name)
    held = value[None]
    stride = size // 2
    bits = 0
    while stride >= 1:
        pairs = [(i, i ^ stride) for i in range(size)]
        other = lax.ppermute(held, axis_name, pairs)
        low = (own & stride) == 0
        held = jnp.where(
            low, jnp.concatenate([held, other], 0), jnp.concatenate([other, held], 0)
        )
        stride //= 2
        bits += 1
    held = held.reshape((2,) * bits + value.shape)
    held = held.transpose(tuple(range(bits))[::-1] + tuple(range(bits, bits + value.ndim)))
    return held.reshape((size * value.shape[0],) + value.shape[1:])


def causal_gather(value, axis_name):
    size = lax.axis_size(axis_name)
    own = lax.axis_index(axis_name)
    received = [value]
    for shift in range(1, size):
        pairs = [(i, i + shift) for i in range(size - shift)]
        received.append(lax.ppermute(value, axis_name, pairs))
    by_shift = jnp.stack(received[::-1], 0)
    doubled = jnp.concatenate([by_shift, by_shift], 0)
    blocks = lax.dynamic_slice_in_dim(doubled, size - 1 - own, size, 0)
    return blocks.reshape((size * value.shape[0],) + value.shape[1:])


def causal_reduce(parts, axis_name):
    size = lax.axis_size(axis_name)
    own = lax.axis_index(axis_name)
    total = lax.dynamic_index_in_dim(parts, own, 0, keepdims=False).astype(jnp.float32)
    for shift in range(1, size):
        pairs = [(i, i - shift) for i in range(shift, size)]
        sent = lax.dynamic_index_in_dim(parts, jnp.maximum(own - shift, 0), 0, keepdims=False)
        total = total + lax.ppermute(sent, axis_name, pairs).astype(jnp.float32)
    return total


def butterfly_sum(value, axis_name):
    size = lax.axis_size(axis_name)
    stride = 1
    while stride < size:
        pairs = [(i, i ^ stride) for i in range(size)]
        value = value + lax.ppermute(value, axis_name, pairs)
        stride *= 2
    return value


def gram_pair_squares(left_gram, right_side, head_dim):
    rows = right_side.shape[0]
    right_heads = right_side.reshape(rows, right_side.shape[1] // head_dim, head_dim)
    right_gram = jnp.einsum(
        "ihd,jhd->hij", right_heads, right_heads, preferred_element_type=jnp.float32
    )
    return jnp.sum(right_gram * left_gram[None], axis=(1, 2))


def gram_squares(left_side, right_side, head_dim):
    left_gram = lax.dot_general(
        left_side, left_side, (((1,), (1,)), ((), ())), preferred_element_type=jnp.float32
    )
    return gram_pair_squares(left_gram, right_side, head_dim)


def body(hidden_in, query_rows, key_rows, value_rows, out_weight, grad_out, answer_mask):
    tok_dev = query_rows.shape[0]
    head_dim = HD
    group_size = HEADS // KVH
    local_groups = key_rows.shape[1] // head_dim
    scaling = head_dim ** (-0.5)
    own_index = lax.axis_index("ctx")
    first_row = own_index * tok_dev
    loss_weight = 0.25 + answer_mask.astype(jnp.float32)
    weighted = (grad_out.astype(jnp.float32) * loss_weight[:, None]).astype(jnp.bfloat16)
    hidden_gram = butterfly_sum(
        lax.dot_general(
            hidden_in, hidden_in, (((1,), (1,)), ((), ())), preferred_element_type=jnp.float32
        ),
        "head",
    )
    piece_part = (
        lax.all_gather(grad_out, "head", axis=1, tiled=True).astype(jnp.float32)
        * loss_weight[:, None]
    ).astype(jnp.bfloat16)
    pair_all = causal_gather(jnp.concatenate([key_rows, value_rows], axis=1), "ctx")
    hidden_gram, pair_all = lax.optimization_barrier((hidden_gram, pair_all))
    kv_width = key_rows.shape[1]
    keys_all, values_all = (pair_all[:, :kv_width], pair_all[:, kv_width:])
    tokens = keys_all.shape[0]
    block_rows = math.gcd(512, tokens)

    def fetch(table, block_number):
        return lax.dynamic_slice_in_dim(table, block_number * block_rows, block_rows, 0)

    def column_pos(block_number):
        return block_number * block_rows + jnp.arange(block_rows, dtype=jnp.int32)

    buffer = jnp.zeros((tokens, 2 * local_groups * head_dim), jnp.float32)
    rows = query_rows.shape[0]
    row_pos = first_row + jnp.arange(rows, dtype=jnp.int32)
    needed = (first_row + rows - 1) // block_rows + 1
    query_heads = query_rows.reshape(rows, local_groups, group_size, head_dim)
    log_totals = []
    shared_head = 0
    query_group = query_heads[:, shared_head]

    def stats_step(block_number, carried):
        running_max, running_sum = carried
        key_block = fetch(keys_all, block_number)
        scores = block_scores(query_group, key_block, scaling, row_pos, column_pos(block_number))
        new_max = jnp.maximum(running_max, jnp.max(scores, axis=-1))
        running_sum = running_sum * jnp.exp(running_max - new_max) + jnp.sum(
            jnp.exp(scores - new_max[..., None]), axis=-1
        )
        return (new_max, running_sum)

    start_max = jnp.full((rows, group_size), NEGATIVE, jnp.float32)
    start_sum = jnp.zeros((rows, group_size), jnp.float32)
    running_max, running_sum = lax.fori_loop(0, needed, stats_step, (start_max, start_sum))
    log_total = running_max + jnp.log(running_sum)

    def value_step(block_number, accumulated):
        key_block = fetch(keys_all, block_number)
        value_block = fetch(values_all, block_number)
        scores = block_scores(query_group, key_block, scaling, row_pos, column_pos(block_number))
        rounded = jnp.exp(scores - log_total[..., None]).astype(jnp.bfloat16)
        return accumulated + jnp.einsum(
            "tgk,kd->tgd", rounded, value_block, preferred_element_type=jnp.float32
        )

    accumulated = lax.fori_loop(
        0, needed, value_step, jnp.zeros((rows, group_size, head_dim), jnp.float32)
    )
    log_totals.append(log_total)
    attended_list = [accumulated.astype(jnp.bfloat16)]
    attended_part = jnp.stack(attended_list, axis=1).reshape(
        rows, local_groups * group_size * head_dim
    )
    log_totals, attended = (log_totals, attended_part)
    grad_sum = lax.dot_general(
        piece_part, out_weight, (((1,), (1,)), ((), ())), preferred_element_type=jnp.float32
    )
    grad_sum, squares_out = (grad_sum, gram_squares(piece_part, attended, head_dim))
    grad_attended, squares_out = (grad_sum.astype(jnp.bfloat16), squares_out)
    backward_buffer = buffer
    rows = query_rows.shape[0]
    backward_row_pos = first_row + jnp.arange(rows, dtype=jnp.int32)
    needed = (first_row + rows - 1) // block_rows + 1
    query_heads = query_rows.reshape(rows, local_groups, group_size, head_dim)
    grad_heads = grad_attended.reshape(rows, local_groups, group_size, head_dim)
    attended_heads = attended.reshape(rows, local_groups, group_size, head_dim)
    shared_head = 0
    backward_query_group = query_heads[:, shared_head]
    grad_group = grad_heads[:, shared_head]
    backward_log_total = log_totals[shared_head]
    row_dot = jnp.sum(
        grad_group.astype(jnp.float32) * attended_heads[:, shared_head].astype(jnp.float32), axis=-1
    )
    grad_query_part, backward_buffer = flash_backward(
        backward_query_group.reshape(rows, group_size * head_dim),
        grad_group.reshape(rows, group_size * head_dim),
        keys_all,
        values_all,
        backward_log_total,
        row_dot,
        first_row,
        head_dim,
        block_rows,
    )
    ctx_size = lax.axis_size("ctx")
    key_sums = causal_reduce(
        backward_buffer.reshape((ctx_size, tokens // ctx_size) + backward_buffer.shape[1:]), "ctx"
    )
    grad_key = key_sums[:, : local_groups * head_dim].astype(jnp.bfloat16)
    grad_value = key_sums[:, local_groups * head_dim :].astype(jnp.bfloat16)
    squares_query = gram_pair_squares(hidden_gram, grad_query_part, head_dim)
    normal_size = D * head_dim * tok_dev
    fisher_q = jnp.log(squares_query / normal_size + EPSILON).reshape(1, -1)
    fisher_o = jnp.log(squares_out / normal_size + EPSILON).reshape(1, -1)
    return (grad_query_part, grad_key, grad_value, fisher_q, fisher_o)


def solution(mesh):
    return jax.shard_map(
        body,
        mesh=mesh,
        in_specs=(
            P("ctx", "head"),
            P("ctx", "head"),
            P("ctx", "head"),
            P("ctx", "head"),
            P("head", None),
            P("ctx", "head"),
            P("ctx"),
        ),
        out_specs=(
            P("ctx", "head"),
            P("ctx", "head"),
            P("ctx", "head"),
            P("ctx", "head"),
            P("ctx", "head"),
        ),
        check_vma=False,
    )
```

```python
import math

import jax
import jax.numpy as jnp
from jax import lax
from jax.experimental import pallas as pl
from jax.experimental.pallas import tpu as pltpu
from jax.sharding import PartitionSpec as P

D = 8192
HEADS = 64
KVH = 8
HD = 128


NEGATIVE = -1e30
EPSILON = 1e-06


def block_scores(query_group, key_block, scaling, row_pos, col_pos):
    scores = (
        jnp.einsum("tgd,kd->tgk", query_group, key_block, preferred_element_type=jnp.float32)
        * scaling
    )
    return jnp.where(row_pos[:, None, None] >= col_pos[None, None, :], scores, NEGATIVE)


def head_squares(left_side, right_side, head_dim):
    product = lax.dot_general(
        left_side, right_side, (((0,), (0,)), ((), ())), preferred_element_type=jnp.float32
    )
    shaped = (product * product).reshape(
        product.shape[0], right_side.shape[1] // head_dim, head_dim
    )
    return jnp.sum(shaped, axis=(0, 2))


def flash_forward(query_rows, keys_all, values_all, first_row, head_dim, block_rows):
    rows, width = query_rows.shape
    heads = width // head_dim
    tokens = keys_all.shape[0]
    blocks = tokens // block_rows
    scaling = head_dim ** (-0.5)
    needed = (first_row + rows - 1) // block_rows + 1
    scalars = jnp.stack([needed, first_row]).astype(jnp.int32)

    def kernel(scalar_ref, q_ref, k_ref, v_ref, att_ref, lt_ref, m_acc, l_acc, o_acc):
        phase = pl.program_id(0)
        j = pl.program_id(1)

        @pl.when(jnp.logical_and(phase == 0, j == 0))
        def _():
            m_acc[...] = jnp.full(m_acc.shape, NEGATIVE, jnp.float32)
            l_acc[...] = jnp.zeros_like(l_acc)
            o_acc[...] = jnp.zeros_like(o_acc)

        @pl.when(jnp.logical_and(phase == 1, j == 0))
        def _():
            lt_ref[...] = m_acc[...] + jnp.log(l_acc[...])

        def block_scores(h, k, masked):
            q = q_ref[:, h * head_dim : (h + 1) * head_dim]
            s = lax.dot_general(q, k, (((1,), (1,)), ((), ())), preferred_element_type=jnp.float32) * scaling
            if masked:
                row_pos = scalar_ref[1] + lax.broadcasted_iota(jnp.int32, (rows, block_rows), 0)
                col_pos = j * block_rows + lax.broadcasted_iota(jnp.int32, (rows, block_rows), 1)
                s = jnp.where(row_pos >= col_pos, s, NEGATIVE)
            return s

        def stats_block(masked):
            k = k_ref[...]
            for h in range(heads):
                s = block_scores(h, k, masked)
                m_old = m_acc[:, h : h + 1]
                m_new = jnp.maximum(m_old, jnp.max(s, axis=1, keepdims=True))
                l_acc[:, h : h + 1] = l_acc[:, h : h + 1] * jnp.exp(m_old - m_new) + jnp.sum(
                    jnp.exp(s - m_new), axis=1, keepdims=True
                )
                m_acc[:, h : h + 1] = m_new

        def value_block(masked):
            k = k_ref[...]
            v = v_ref[...]
            for h in range(heads):
                s = block_scores(h, k, masked)
                p = jnp.exp(s - lt_ref[:, h : h + 1]).astype(jnp.bfloat16)
                o_acc[:, h * head_dim : (h + 1) * head_dim] += jnp.dot(p, v, preferred_element_type=jnp.float32)

        active = j < scalar_ref[0]
        for phase_id, step in ((0, stats_block), (1, value_block)):

            @pl.when(jnp.logical_and(phase == phase_id, active))
            def _(step=step):
                step(True)

        @pl.when(jnp.logical_and(phase == 1, j == blocks - 1))
        def _():
            att_ref[...] = o_acc[...].astype(att_ref.dtype)

    def kv_map(p, j, s):
        return (jnp.minimum(j, s[0] - 1), 0)

    full = lambda p, j, s: (0, 0)
    grid_spec = pltpu.PrefetchScalarGridSpec(
        num_scalar_prefetch=1,
        grid=(2, blocks),
        in_specs=[
            pl.BlockSpec((rows, width), full),
            pl.BlockSpec((block_rows, head_dim), kv_map),
            pl.BlockSpec((block_rows, head_dim), kv_map),
        ],
        out_specs=[
            pl.BlockSpec((rows, width), full),
            pl.BlockSpec((rows, heads), full),
        ],
        scratch_shapes=[
            pltpu.VMEM((rows, heads), jnp.float32),
            pltpu.VMEM((rows, heads), jnp.float32),
            pltpu.VMEM((rows, width), jnp.float32),
        ],
    )
    return pl.pallas_call(
        kernel,
        grid_spec=grid_spec,
        out_shape=[
            jax.ShapeDtypeStruct((rows, width), jnp.bfloat16),
            jax.ShapeDtypeStruct((rows, heads), jnp.float32),
        ],
        compiler_params=pltpu.CompilerParams(dimension_semantics=("arbitrary", "arbitrary")),
    )(scalars, query_rows, keys_all, values_all)


def flash_backward(query_rows, grad_attended, keys_all, values_all, log_total, row_dot, first_row, head_dim, block_rows):
    rows, width = query_rows.shape
    heads = width // head_dim
    tokens = keys_all.shape[0]
    blocks = tokens // block_rows
    scaling = head_dim ** (-0.5)
    needed = (first_row + rows - 1) // block_rows + 1
    scalars = jnp.stack([needed, first_row]).astype(jnp.int32)

    def kernel(scalar_ref, q_ref, do_ref, k_ref, v_ref, lt_ref, rd_ref, dq_ref, dkv_ref, dq_acc):
        j = pl.program_id(0)

        @pl.when(j == 0)
        def _():
            dq_acc[...] = jnp.zeros_like(dq_acc)

        def block(masked):
            k = k_ref[...]
            v = v_ref[...]
            row_pos = scalar_ref[1] + lax.broadcasted_iota(jnp.int32, (rows, block_rows), 0)
            col_pos = j * block_rows + lax.broadcasted_iota(jnp.int32, (rows, block_rows), 1)
            keep = row_pos >= col_pos
            dk = jnp.zeros((block_rows, head_dim), jnp.float32)
            dv = jnp.zeros((block_rows, head_dim), jnp.float32)
            for h in range(heads):
                cols = slice(h * head_dim, (h + 1) * head_dim)
                q = q_ref[:, cols]
                do = do_ref[:, cols]
                s = lax.dot_general(q, k, (((1,), (1,)), ((), ())), preferred_element_type=jnp.float32) * scaling
                if masked:
                    s = jnp.where(keep, s, NEGATIVE)
                p = jnp.exp(s - lt_ref[:, h : h + 1])
                dp = lax.dot_general(do, v, (((1,), (1,)), ((), ())), preferred_element_type=jnp.float32)
                ds = (p * (dp - rd_ref[:, h : h + 1]) * scaling).astype(jnp.bfloat16)
                dq_acc[:, cols] += jnp.dot(ds, k, preferred_element_type=jnp.float32)
                dk += lax.dot_general(ds, q, (((0,), (0,)), ((), ())), preferred_element_type=jnp.float32)
                dv += lax.dot_general(p.astype(jnp.bfloat16), do, (((0,), (0,)), ((), ())), preferred_element_type=jnp.float32)
            dkv_ref[:, :head_dim] = dk.astype(dkv_ref.dtype)
            dkv_ref[:, head_dim:] = dv.astype(dkv_ref.dtype)

        below = j * block_rows + block_rows - 1 <= scalar_ref[1]

        @pl.when(jnp.logical_and(j < scalar_ref[0], below))
        def _():
            block(False)

        @pl.when(jnp.logical_and(j < scalar_ref[0], jnp.logical_not(below)))
        def _():
            block(True)

        @pl.when(j >= scalar_ref[0])
        def _():
            dkv_ref[...] = jnp.zeros_like(dkv_ref)

        @pl.when(j == blocks - 1)
        def _():
            dq_ref[...] = dq_acc[...].astype(dq_ref.dtype)

    def kv_map(j, s):
        return (jnp.minimum(j, s[0] - 1), 0)

    full = lambda j, s: (0, 0)
    grid_spec = pltpu.PrefetchScalarGridSpec(
        num_scalar_prefetch=1,
        grid=(blocks,),
        in_specs=[
            pl.BlockSpec((rows, width), full),
            pl.BlockSpec((rows, width), full),
            pl.BlockSpec((block_rows, head_dim), kv_map),
            pl.BlockSpec((block_rows, head_dim), kv_map),
            pl.BlockSpec((rows, heads), full),
            pl.BlockSpec((rows, heads), full),
        ],
        out_specs=[
            pl.BlockSpec((rows, width), full),
            pl.BlockSpec((block_rows, 2 * head_dim), lambda j, s: (j, 0)),
        ],
        scratch_shapes=[pltpu.VMEM((rows, width), jnp.float32)],
    )
    return pl.pallas_call(
        kernel,
        grid_spec=grid_spec,
        out_shape=[
            jax.ShapeDtypeStruct((rows, width), jnp.bfloat16),
            jax.ShapeDtypeStruct((tokens, 2 * head_dim), jnp.bfloat16),
        ],
        compiler_params=pltpu.CompilerParams(dimension_semantics=("arbitrary",)),
    )(scalars, query_rows, grad_attended, keys_all, values_all, log_total, row_dot)


def butterfly_gather(value, axis_name):
    size = lax.axis_size(axis_name)
    own = lax.axis_index(axis_name)
    held = value[None]
    stride = size // 2
    bits = 0
    while stride >= 1:
        pairs = [(i, i ^ stride) for i in range(size)]
        other = lax.ppermute(held, axis_name, pairs)
        low = (own & stride) == 0
        held = jnp.where(
            low, jnp.concatenate([held, other], 0), jnp.concatenate([other, held], 0)
        )
        stride //= 2
        bits += 1
    held = held.reshape((2,) * bits + value.shape)
    held = held.transpose(tuple(range(bits))[::-1] + tuple(range(bits, bits + value.ndim)))
    return held.reshape((size * value.shape[0],) + value.shape[1:])


def causal_gather(value, axis_name):
    size = lax.axis_size(axis_name)
    own = lax.axis_index(axis_name)
    received = [value]
    for shift in range(1, size):
        pairs = [(i, i + shift) for i in range(size - shift)]
        received.append(lax.ppermute(value, axis_name, pairs))
    by_shift = jnp.stack(received[::-1], 0)
    doubled = jnp.concatenate([by_shift, by_shift], 0)
    blocks = lax.dynamic_slice_in_dim(doubled, size - 1 - own, size, 0)
    return blocks.reshape((size * value.shape[0],) + value.shape[1:])


def causal_reduce(parts, axis_name):
    size = lax.axis_size(axis_name)
    own = lax.axis_index(axis_name)
    total = lax.dynamic_index_in_dim(parts, own, 0, keepdims=False).astype(jnp.float32)
    for shift in range(1, size):
        pairs = [(i, i - shift) for i in range(shift, size)]
        sent = lax.dynamic_index_in_dim(parts, jnp.maximum(own - shift, 0), 0, keepdims=False)
        total = total + lax.ppermute(sent, axis_name, pairs).astype(jnp.float32)
    return total


def butterfly_sum(value, axis_name):
    size = lax.axis_size(axis_name)
    stride = 1
    while stride < size:
        pairs = [(i, i ^ stride) for i in range(size)]
        value = value + lax.ppermute(value, axis_name, pairs)
        stride *= 2
    return value


def gram_pair_squares(left_gram, right_side, head_dim):
    rows = right_side.shape[0]
    right_heads = right_side.reshape(rows, right_side.shape[1] // head_dim, head_dim)
    right_gram = jnp.einsum(
        "ihd,jhd->hij", right_heads, right_heads, preferred_element_type=jnp.float32
    )
    return jnp.sum(right_gram * left_gram[None], axis=(1, 2))


def gram_squares(left_side, right_side, head_dim):
    left_gram = lax.dot_general(
        left_side, left_side, (((1,), (1,)), ((), ())), preferred_element_type=jnp.float32
    )
    return gram_pair_squares(left_gram, right_side, head_dim)


def body(hidden_in, query_rows, key_rows, value_rows, out_weight, grad_out, answer_mask):
    tok_dev = query_rows.shape[0]
    head_dim = HD
    group_size = HEADS // KVH
    local_groups = key_rows.shape[1] // head_dim
    scaling = head_dim ** (-0.5)
    own_index = lax.axis_index("ctx")
    first_row = own_index * tok_dev
    loss_weight = 0.25 + answer_mask.astype(jnp.float32)
    weighted = (grad_out.astype(jnp.float32) * loss_weight[:, None]).astype(jnp.bfloat16)
    hidden_gram = butterfly_sum(
        lax.dot_general(
            hidden_in, hidden_in, (((1,), (1,)), ((), ())), preferred_element_type=jnp.float32
        ),
        "head",
    )
    piece_part = (
        lax.all_gather(grad_out, "head", axis=1, tiled=True).astype(jnp.float32)
        * loss_weight[:, None]
    ).astype(jnp.bfloat16)
    pair_all = causal_gather(jnp.concatenate([key_rows, value_rows], axis=1), "ctx")
    hidden_gram, pair_all = lax.optimization_barrier((hidden_gram, pair_all))
    kv_width = key_rows.shape[1]
    keys_all, values_all = (pair_all[:, :kv_width], pair_all[:, kv_width:])
    tokens = keys_all.shape[0]
    block_rows = math.gcd(512, tokens)

    def fetch(table, block_number):
        return lax.dynamic_slice_in_dim(table, block_number * block_rows, block_rows, 0)

    def column_pos(block_number):
        return block_number * block_rows + jnp.arange(block_rows, dtype=jnp.int32)

    buffer = jnp.zeros((tokens, 2 * local_groups * head_dim), jnp.float32)
    rows = query_rows.shape[0]
    row_pos = first_row + jnp.arange(rows, dtype=jnp.int32)
    needed = (first_row + rows - 1) // block_rows + 1
    query_heads = query_rows.reshape(rows, local_groups, group_size, head_dim)
    log_totals = []
    shared_head = 0
    query_group = query_heads[:, shared_head]

    attended_part, log_total = flash_forward(
        query_group.reshape(rows, group_size * head_dim), keys_all, values_all, first_row,
        head_dim, block_rows,
    )
    log_totals.append(log_total)
    log_totals, attended = (log_totals, attended_part)
    grad_sum = lax.dot_general(
        piece_part, out_weight, (((1,), (1,)), ((), ())), preferred_element_type=jnp.float32
    )
    grad_sum, squares_out = (grad_sum, gram_squares(piece_part, attended, head_dim))
    grad_attended, squares_out = (grad_sum.astype(jnp.bfloat16), squares_out)
    backward_buffer = buffer
    rows = query_rows.shape[0]
    backward_row_pos = first_row + jnp.arange(rows, dtype=jnp.int32)
    needed = (first_row + rows - 1) // block_rows + 1
    query_heads = query_rows.reshape(rows, local_groups, group_size, head_dim)
    grad_heads = grad_attended.reshape(rows, local_groups, group_size, head_dim)
    attended_heads = attended.reshape(rows, local_groups, group_size, head_dim)
    shared_head = 0
    backward_query_group = query_heads[:, shared_head]
    grad_group = grad_heads[:, shared_head]
    backward_log_total = log_totals[shared_head]
    row_dot = jnp.sum(
        grad_group.astype(jnp.float32) * attended_heads[:, shared_head].astype(jnp.float32), axis=-1
    )
    grad_query_part, backward_buffer = flash_backward(
        backward_query_group.reshape(rows, group_size * head_dim),
        grad_group.reshape(rows, group_size * head_dim),
        keys_all,
        values_all,
        backward_log_total,
        row_dot,
        first_row,
        head_dim,
        block_rows,
    )
    ctx_size = lax.axis_size("ctx")
    key_sums = causal_reduce(
        backward_buffer.reshape((ctx_size, tokens // ctx_size) + backward_buffer.shape[1:]), "ctx"
    )
    grad_key = key_sums[:, : local_groups * head_dim].astype(jnp.bfloat16)
    grad_value = key_sums[:, local_groups * head_dim :].astype(jnp.bfloat16)
    squares_query = gram_pair_squares(hidden_gram, grad_query_part, head_dim)
    normal_size = D * head_dim * tok_dev
    fisher_q = jnp.log(squares_query / normal_size + EPSILON).reshape(1, -1)
    fisher_o = jnp.log(squares_out / normal_size + EPSILON).reshape(1, -1)
    return (grad_query_part, grad_key, grad_value, fisher_q, fisher_o)


def solution(mesh):
    return jax.shard_map(
        body,
        mesh=mesh,
        in_specs=(
            P("ctx", "head"),
            P("ctx", "head"),
            P("ctx", "head"),
            P("ctx", "head"),
            P("head", None),
            P("ctx", "head"),
            P("ctx"),
        ),
        out_specs=(
            P("ctx", "head"),
            P("ctx", "head"),
            P("ctx", "head"),
            P("ctx", "head"),
            P("ctx", "head"),
        ),
        check_vma=False,
    )
```

```python
import math

import jax
import jax.numpy as jnp
from jax import lax
from jax.experimental import pallas as pl
from jax.experimental.pallas import tpu as pltpu
from jax.sharding import PartitionSpec as P

D = 8192
HEADS = 64
KVH = 8
HD = 128


NEGATIVE = -1e30
EPSILON = 1e-06


def block_scores(query_group, key_block, scaling, row_pos, col_pos):
    scores = (
        jnp.einsum("tgd,kd->tgk", query_group, key_block, preferred_element_type=jnp.float32)
        * scaling
    )
    return jnp.where(row_pos[:, None, None] >= col_pos[None, None, :], scores, NEGATIVE)


def head_squares(left_side, right_side, head_dim):
    product = lax.dot_general(
        left_side, right_side, (((0,), (0,)), ((), ())), preferred_element_type=jnp.float32
    )
    shaped = (product * product).reshape(
        product.shape[0], right_side.shape[1] // head_dim, head_dim
    )
    return jnp.sum(shaped, axis=(0, 2))


def flash_backward(query_rows, grad_attended, keys_all, values_all, log_total, row_dot, first_row, head_dim, block_rows):
    rows, width = query_rows.shape
    heads = width // head_dim
    tokens = keys_all.shape[0]
    blocks = tokens // block_rows
    scaling = head_dim ** (-0.5)
    needed = (first_row + rows - 1) // block_rows + 1
    scalars = jnp.stack([needed, first_row]).astype(jnp.int32)

    def kernel(scalar_ref, q_ref, do_ref, k_ref, v_ref, lt_ref, rd_ref, dq_ref, dkv_ref, dq_acc):
        j = pl.program_id(0)

        @pl.when(j == 0)
        def _():
            dq_acc[...] = jnp.zeros_like(dq_acc)

        @pl.when(j < scalar_ref[0])
        def _():
            k = k_ref[...]
            v = v_ref[...]
            row_pos = scalar_ref[1] + lax.broadcasted_iota(jnp.int32, (rows, block_rows), 0)
            col_pos = j * block_rows + lax.broadcasted_iota(jnp.int32, (rows, block_rows), 1)
            keep = row_pos >= col_pos
            dk = jnp.zeros((block_rows, head_dim), jnp.float32)
            dv = jnp.zeros((block_rows, head_dim), jnp.float32)
            for h in range(heads):
                cols = slice(h * head_dim, (h + 1) * head_dim)
                q = q_ref[:, cols]
                do = do_ref[:, cols]
                s = lax.dot_general(q, k, (((1,), (1,)), ((), ())), preferred_element_type=jnp.float32) * scaling
                s = jnp.where(keep, s, NEGATIVE)
                p = jnp.exp(s - lt_ref[:, h : h + 1])
                dp = lax.dot_general(do, v, (((1,), (1,)), ((), ())), preferred_element_type=jnp.float32)
                ds = (p * (dp - rd_ref[:, h : h + 1]) * scaling).astype(jnp.bfloat16)
                dq_acc[:, cols] += jnp.dot(ds, k, preferred_element_type=jnp.float32)
                dk += lax.dot_general(ds, q, (((0,), (0,)), ((), ())), preferred_element_type=jnp.float32)
                dv += lax.dot_general(p.astype(jnp.bfloat16), do, (((0,), (0,)), ((), ())), preferred_element_type=jnp.float32)
            dkv_ref[:, :head_dim] = dk.astype(dkv_ref.dtype)
            dkv_ref[:, head_dim:] = dv.astype(dkv_ref.dtype)

        @pl.when(j >= scalar_ref[0])
        def _():
            dkv_ref[...] = jnp.zeros_like(dkv_ref)

        @pl.when(j == blocks - 1)
        def _():
            dq_ref[...] = dq_acc[...].astype(dq_ref.dtype)

    def kv_map(j, s):
        return (jnp.minimum(j, s[0] - 1), 0)

    full = lambda j, s: (0, 0)
    grid_spec = pltpu.PrefetchScalarGridSpec(
        num_scalar_prefetch=1,
        grid=(blocks,),
        in_specs=[
            pl.BlockSpec((rows, width), full),
            pl.BlockSpec((rows, width), full),
            pl.BlockSpec((block_rows, head_dim), kv_map),
            pl.BlockSpec((block_rows, head_dim), kv_map),
            pl.BlockSpec((rows, heads), full),
            pl.BlockSpec((rows, heads), full),
        ],
        out_specs=[
            pl.BlockSpec((rows, width), full),
            pl.BlockSpec((block_rows, 2 * head_dim), lambda j, s: (j, 0)),
        ],
        scratch_shapes=[pltpu.VMEM((rows, width), jnp.float32)],
    )
    return pl.pallas_call(
        kernel,
        grid_spec=grid_spec,
        out_shape=[
            jax.ShapeDtypeStruct((rows, width), jnp.bfloat16),
            jax.ShapeDtypeStruct((tokens, 2 * head_dim), jnp.bfloat16),
        ],
        compiler_params=pltpu.CompilerParams(dimension_semantics=("arbitrary",)),
    )(scalars, query_rows, grad_attended, keys_all, values_all, log_total, row_dot)


def butterfly_gather(value, axis_name):
    size = lax.axis_size(axis_name)
    own = lax.axis_index(axis_name)
    held = value[None]
    stride = size // 2
    bits = 0
    while stride >= 1:
        pairs = [(i, i ^ stride) for i in range(size)]
        other = lax.ppermute(held, axis_name, pairs)
        low = (own & stride) == 0
        held = jnp.where(
            low, jnp.concatenate([held, other], 0), jnp.concatenate([other, held], 0)
        )
        stride //= 2
        bits += 1
    held = held.reshape((2,) * bits + value.shape)
    held = held.transpose(tuple(range(bits))[::-1] + tuple(range(bits, bits + value.ndim)))
    return held.reshape((size * value.shape[0],) + value.shape[1:])


def causal_gather(value, axis_name):
    size = lax.axis_size(axis_name)
    own = lax.axis_index(axis_name)
    received = [value]
    for shift in range(1, size):
        pairs = [(i, i + shift) for i in range(size - shift)]
        received.append(lax.ppermute(value, axis_name, pairs))
    by_shift = jnp.stack(received[::-1], 0)
    doubled = jnp.concatenate([by_shift, by_shift], 0)
    blocks = lax.dynamic_slice_in_dim(doubled, size - 1 - own, size, 0)
    return blocks.reshape((size * value.shape[0],) + value.shape[1:])


def causal_reduce(parts, axis_name):
    size = lax.axis_size(axis_name)
    own = lax.axis_index(axis_name)
    total = lax.dynamic_index_in_dim(parts, own, 0, keepdims=False).astype(jnp.float32)
    for shift in range(1, size):
        pairs = [(i, i - shift) for i in range(shift, size)]
        sent = lax.dynamic_index_in_dim(parts, jnp.maximum(own - shift, 0), 0, keepdims=False)
        total = total + lax.ppermute(sent, axis_name, pairs).astype(jnp.float32)
    return total


def exchange_reduce(parts, axis_name):
    arrived = lax.all_to_all(parts, axis_name, 0, 0, tiled=True)
    return jnp.sum(arrived.astype(jnp.float32), axis=0)


def butterfly_sum(value, axis_name):
    size = lax.axis_size(axis_name)
    stride = 1
    while stride < size:
        pairs = [(i, i ^ stride) for i in range(size)]
        value = value + lax.ppermute(value, axis_name, pairs)
        stride *= 2
    return value


def gram_pair_squares(left_gram, right_side, head_dim):
    rows = right_side.shape[0]
    right_heads = right_side.reshape(rows, right_side.shape[1] // head_dim, head_dim)
    right_gram = jnp.einsum(
        "ihd,jhd->hij", right_heads, right_heads, preferred_element_type=jnp.float32
    )
    return jnp.sum(right_gram * left_gram[None], axis=(1, 2))


def gram_squares(left_side, right_side, head_dim):
    left_gram = lax.dot_general(
        left_side, left_side, (((1,), (1,)), ((), ())), preferred_element_type=jnp.float32
    )
    return gram_pair_squares(left_gram, right_side, head_dim)


def body(hidden_in, query_rows, key_rows, value_rows, out_weight, grad_out, answer_mask):
    tok_dev = query_rows.shape[0]
    head_dim = HD
    group_size = HEADS // KVH
    local_groups = key_rows.shape[1] // head_dim
    scaling = head_dim ** (-0.5)
    own_index = lax.axis_index("ctx")
    first_row = own_index * tok_dev
    loss_weight = 0.25 + answer_mask.astype(jnp.float32)
    weighted = (grad_out.astype(jnp.float32) * loss_weight[:, None]).astype(jnp.bfloat16)
    hidden_gram = butterfly_sum(
        lax.dot_general(
            hidden_in, hidden_in, (((1,), (1,)), ((), ())), preferred_element_type=jnp.float32
        ),
        "head",
    )
    piece_part = (
        lax.all_gather(grad_out, "head", axis=1, tiled=True).astype(jnp.float32)
        * loss_weight[:, None]
    ).astype(jnp.bfloat16)
    pair_all = causal_gather(jnp.concatenate([key_rows, value_rows], axis=1), "ctx")
    kv_width = key_rows.shape[1]
    keys_all, values_all = (pair_all[:, :kv_width], pair_all[:, kv_width:])
    tokens = keys_all.shape[0]
    block_rows = math.gcd(512, tokens)

    def fetch(table, block_number):
        return lax.dynamic_slice_in_dim(table, block_number * block_rows, block_rows, 0)

    def column_pos(block_number):
        return block_number * block_rows + jnp.arange(block_rows, dtype=jnp.int32)

    buffer = jnp.zeros((tokens, 2 * local_groups * head_dim), jnp.float32)
    rows = query_rows.shape[0]
    row_pos = first_row + jnp.arange(rows, dtype=jnp.int32)
    needed = (first_row + rows - 1) // block_rows + 1
    query_heads = query_rows.reshape(rows, local_groups, group_size, head_dim)
    log_totals = []
    shared_head = 0
    query_group = query_heads[:, shared_head]

    def stats_step(block_number, carried):
        running_max, running_sum = carried
        key_block = fetch(keys_all, block_number)
        scores = block_scores(query_group, key_block, scaling, row_pos, column_pos(block_number))
        new_max = jnp.maximum(running_max, jnp.max(scores, axis=-1))
        running_sum = running_sum * jnp.exp(running_max - new_max) + jnp.sum(
            jnp.exp(scores - new_max[..., None]), axis=-1
        )
        return (new_max, running_sum)

    start_max = jnp.full((rows, group_size), NEGATIVE, jnp.float32)
    start_sum = jnp.zeros((rows, group_size), jnp.float32)
    running_max, running_sum = lax.fori_loop(0, needed, stats_step, (start_max, start_sum))
    log_total = running_max + jnp.log(running_sum)

    def value_step(block_number, accumulated):
        key_block = fetch(keys_all, block_number)
        value_block = fetch(values_all, block_number)
        scores = block_scores(query_group, key_block, scaling, row_pos, column_pos(block_number))
        rounded = jnp.exp(scores - log_total[..., None]).astype(jnp.bfloat16)
        return accumulated + jnp.einsum(
            "tgk,kd->tgd", rounded, value_block, preferred_element_type=jnp.float32
        )

    accumulated = lax.fori_loop(
        0, needed, value_step, jnp.zeros((rows, group_size, head_dim), jnp.float32)
    )
    log_totals.append(log_total)
    attended_list = [accumulated.astype(jnp.bfloat16)]
    attended_part = jnp.stack(attended_list, axis=1).reshape(
        rows, local_groups * group_size * head_dim
    )
    log_totals, attended = (log_totals, attended_part)
    grad_sum = lax.dot_general(
        piece_part, out_weight, (((1,), (1,)), ((), ())), preferred_element_type=jnp.float32
    )
    grad_sum, squares_out = (grad_sum, gram_squares(piece_part, attended, head_dim))
    grad_attended, squares_out = (grad_sum.astype(jnp.bfloat16), squares_out)
    backward_buffer = buffer
    rows = query_rows.shape[0]
    backward_row_pos = first_row + jnp.arange(rows, dtype=jnp.int32)
    needed = (first_row + rows - 1) // block_rows + 1
    query_heads = query_rows.reshape(rows, local_groups, group_size, head_dim)
    grad_heads = grad_attended.reshape(rows, local_groups, group_size, head_dim)
    attended_heads = attended.reshape(rows, local_groups, group_size, head_dim)
    shared_head = 0
    backward_query_group = query_heads[:, shared_head]
    grad_group = grad_heads[:, shared_head]
    backward_log_total = log_totals[shared_head]
    row_dot = jnp.sum(
        grad_group.astype(jnp.float32) * attended_heads[:, shared_head].astype(jnp.float32), axis=-1
    )
    grad_query_part, backward_buffer = flash_backward(
        backward_query_group.reshape(rows, group_size * head_dim),
        grad_group.reshape(rows, group_size * head_dim),
        keys_all,
        values_all,
        backward_log_total,
        row_dot,
        first_row,
        head_dim,
        block_rows,
    )
    ctx_size = lax.axis_size("ctx")
    key_sums = exchange_reduce(
        backward_buffer.reshape((ctx_size, tokens // ctx_size) + backward_buffer.shape[1:]), "ctx"
    )
    grad_key = key_sums[:, : local_groups * head_dim].astype(jnp.bfloat16)
    grad_value = key_sums[:, local_groups * head_dim :].astype(jnp.bfloat16)
    squares_query = gram_pair_squares(hidden_gram, grad_query_part, head_dim)
    normal_size = D * head_dim * tok_dev
    fisher_q = jnp.log(squares_query / normal_size + EPSILON).reshape(1, -1)
    fisher_o = jnp.log(squares_out / normal_size + EPSILON).reshape(1, -1)
    return (grad_query_part, grad_key, grad_value, fisher_q, fisher_o)


def solution(mesh):
    return jax.shard_map(
        body,
        mesh=mesh,
        in_specs=(
            P("ctx", "head"),
            P("ctx", "head"),
            P("ctx", "head"),
            P("ctx", "head"),
            P("head", None),
            P("ctx", "head"),
            P("ctx"),
        ),
        out_specs=(
            P("ctx", "head"),
            P("ctx", "head"),
            P("ctx", "head"),
            P("ctx", "head"),
            P("ctx", "head"),
        ),
        check_vma=False,
    )
```

```python
import math

import jax
import jax.numpy as jnp
from jax import lax
from jax.experimental import pallas as pl
from jax.experimental.pallas import tpu as pltpu
from jax.sharding import PartitionSpec as P

D = 8192
HEADS = 64
KVH = 8
HD = 128


NEGATIVE = -1e30
EPSILON = 1e-06


def block_scores(query_group, key_block, scaling, row_pos, col_pos):
    scores = (
        jnp.einsum("tgd,kd->tgk", query_group, key_block, preferred_element_type=jnp.float32)
        * scaling
    )
    return jnp.where(row_pos[:, None, None] >= col_pos[None, None, :], scores, NEGATIVE)


def head_squares(left_side, right_side, head_dim):
    product = lax.dot_general(
        left_side, right_side, (((0,), (0,)), ((), ())), preferred_element_type=jnp.float32
    )
    shaped = (product * product).reshape(
        product.shape[0], right_side.shape[1] // head_dim, head_dim
    )
    return jnp.sum(shaped, axis=(0, 2))


def flash_backward(query_rows, grad_attended, keys_all, values_all, log_total, row_dot, first_row, head_dim, block_rows):
    rows, width = query_rows.shape
    heads = width // head_dim
    tokens = keys_all.shape[0]
    blocks = tokens // block_rows
    scaling = head_dim ** (-0.5)
    needed = (first_row + rows - 1) // block_rows + 1
    scalars = jnp.stack([needed, first_row]).astype(jnp.int32)

    def kernel(scalar_ref, q_ref, do_ref, k_ref, v_ref, lt_ref, rd_ref, dq_ref, dkv_ref, dq_acc):
        j = pl.program_id(0)

        @pl.when(j == 0)
        def _():
            dq_acc[...] = jnp.zeros_like(dq_acc)

        @pl.when(j < scalar_ref[0])
        def _():
            k = k_ref[...]
            v = v_ref[...]
            row_pos = scalar_ref[1] + lax.broadcasted_iota(jnp.int32, (rows, block_rows), 0)
            col_pos = j * block_rows + lax.broadcasted_iota(jnp.int32, (rows, block_rows), 1)
            keep = row_pos >= col_pos
            dk = jnp.zeros((block_rows, head_dim), jnp.float32)
            dv = jnp.zeros((block_rows, head_dim), jnp.float32)
            for h in range(heads):
                cols = slice(h * head_dim, (h + 1) * head_dim)
                q = q_ref[:, cols]
                do = do_ref[:, cols]
                s = lax.dot_general(q, k, (((1,), (1,)), ((), ())), preferred_element_type=jnp.float32) * scaling
                s = jnp.where(keep, s, NEGATIVE)
                p = jnp.exp(s - lt_ref[:, h : h + 1])
                dp = lax.dot_general(do, v, (((1,), (1,)), ((), ())), preferred_element_type=jnp.float32)
                ds = (p * (dp - rd_ref[:, h : h + 1]) * scaling).astype(jnp.bfloat16)
                dq_acc[:, cols] += jnp.dot(ds, k, preferred_element_type=jnp.float32)
                dk += lax.dot_general(ds, q, (((0,), (0,)), ((), ())), preferred_element_type=jnp.float32)
                dv += lax.dot_general(p.astype(jnp.bfloat16), do, (((0,), (0,)), ((), ())), preferred_element_type=jnp.float32)
            dkv_ref[:, :head_dim] = dk.astype(dkv_ref.dtype)
            dkv_ref[:, head_dim:] = dv.astype(dkv_ref.dtype)

        @pl.when(j >= scalar_ref[0])
        def _():
            dkv_ref[...] = jnp.zeros_like(dkv_ref)

        @pl.when(j == blocks - 1)
        def _():
            dq_ref[...] = dq_acc[...].astype(dq_ref.dtype)

    def kv_map(j, s):
        return (jnp.minimum(j, s[0] - 1), 0)

    full = lambda j, s: (0, 0)
    grid_spec = pltpu.PrefetchScalarGridSpec(
        num_scalar_prefetch=1,
        grid=(blocks,),
        in_specs=[
            pl.BlockSpec((rows, width), full),
            pl.BlockSpec((rows, width), full),
            pl.BlockSpec((block_rows, head_dim), kv_map),
            pl.BlockSpec((block_rows, head_dim), kv_map),
            pl.BlockSpec((rows, heads), full),
            pl.BlockSpec((rows, heads), full),
        ],
        out_specs=[
            pl.BlockSpec((rows, width), full),
            pl.BlockSpec((block_rows, 2 * head_dim), lambda j, s: (j, 0)),
        ],
        scratch_shapes=[pltpu.VMEM((rows, width), jnp.float32)],
    )
    return pl.pallas_call(
        kernel,
        grid_spec=grid_spec,
        out_shape=[
            jax.ShapeDtypeStruct((rows, width), jnp.bfloat16),
            jax.ShapeDtypeStruct((tokens, 2 * head_dim), jnp.bfloat16),
        ],
        compiler_params=pltpu.CompilerParams(dimension_semantics=("arbitrary",)),
    )(scalars, query_rows, grad_attended, keys_all, values_all, log_total, row_dot)


def butterfly_gather(value, axis_name):
    size = lax.axis_size(axis_name)
    own = lax.axis_index(axis_name)
    held = value[None]
    stride = size // 2
    bits = 0
    while stride >= 1:
        pairs = [(i, i ^ stride) for i in range(size)]
        other = lax.ppermute(held, axis_name, pairs)
        low = (own & stride) == 0
        held = jnp.where(
            low, jnp.concatenate([held, other], 0), jnp.concatenate([other, held], 0)
        )
        stride //= 2
        bits += 1
    held = held.reshape((2,) * bits + value.shape)
    held = held.transpose(tuple(range(bits))[::-1] + tuple(range(bits, bits + value.ndim)))
    return held.reshape((size * value.shape[0],) + value.shape[1:])


def causal_gather(value, axis_name):
    size = lax.axis_size(axis_name)
    own = lax.axis_index(axis_name)
    received = [value]
    for shift in range(1, size):
        pairs = [(i, i + shift) for i in range(size - shift)]
        received.append(lax.ppermute(value, axis_name, pairs))
    by_shift = jnp.stack(received[::-1], 0)
    doubled = jnp.concatenate([by_shift, by_shift], 0)
    blocks = lax.dynamic_slice_in_dim(doubled, size - 1 - own, size, 0)
    return blocks.reshape((size * value.shape[0],) + value.shape[1:])


def causal_reduce(parts, axis_name):
    size = lax.axis_size(axis_name)
    own = lax.axis_index(axis_name)
    total = lax.dynamic_index_in_dim(parts, own, 0, keepdims=False).astype(jnp.float32)
    for shift in range(1, size):
        pairs = [(i, i - shift) for i in range(shift, size)]
        sent = lax.dynamic_index_in_dim(parts, jnp.maximum(own - shift, 0), 0, keepdims=False)
        total = total + lax.ppermute(sent, axis_name, pairs).astype(jnp.float32)
    return total


def exchange_reduce(parts, axis_name):
    arrived = lax.all_to_all(parts, axis_name, 0, 0, tiled=True)
    return jnp.sum(arrived.astype(jnp.float32), axis=0)


def butterfly_sum(value, axis_name):
    size = lax.axis_size(axis_name)
    stride = 1
    while stride < size:
        pairs = [(i, i ^ stride) for i in range(size)]
        value = value + lax.ppermute(value, axis_name, pairs)
        stride *= 2
    return value


def gram_pair_squares(left_gram, right_side, head_dim):
    rows = right_side.shape[0]
    right_heads = right_side.reshape(rows, right_side.shape[1] // head_dim, head_dim)
    right_gram = jnp.einsum(
        "ihd,jhd->hij", right_heads, right_heads, preferred_element_type=jnp.float32
    )
    return jnp.sum(right_gram * left_gram[None], axis=(1, 2))


def gram_squares(left_side, right_side, head_dim):
    left_gram = lax.dot_general(
        left_side, left_side, (((1,), (1,)), ((), ())), preferred_element_type=jnp.float32
    )
    return gram_pair_squares(left_gram, right_side, head_dim)


def body(hidden_in, query_rows, key_rows, value_rows, out_weight, grad_out, answer_mask):
    tok_dev = query_rows.shape[0]
    head_dim = HD
    group_size = HEADS // KVH
    local_groups = key_rows.shape[1] // head_dim
    scaling = head_dim ** (-0.5)
    own_index = lax.axis_index("ctx")
    first_row = own_index * tok_dev
    loss_weight = 0.25 + answer_mask.astype(jnp.float32)
    weighted = (grad_out.astype(jnp.float32) * loss_weight[:, None]).astype(jnp.bfloat16)
    gram_part = lax.dot_general(
        hidden_in, hidden_in, (((1,), (1,)), ((), ())), preferred_element_type=jnp.float32
    )
    piece_part = (
        lax.all_gather(grad_out, "head", axis=1, tiled=True).astype(jnp.float32)
        * loss_weight[:, None]
    ).astype(jnp.bfloat16)
    gram_part, piece_part = lax.optimization_barrier((gram_part, piece_part))
    hidden_gram = jnp.sum(lax.all_gather(gram_part, "head", axis=0, tiled=False), axis=0)
    pair_all = causal_gather(jnp.concatenate([key_rows, value_rows], axis=1), "ctx")
    kv_width = key_rows.shape[1]
    keys_all, values_all = (pair_all[:, :kv_width], pair_all[:, kv_width:])
    tokens = keys_all.shape[0]
    block_rows = math.gcd(512, tokens)

    def fetch(table, block_number):
        return lax.dynamic_slice_in_dim(table, block_number * block_rows, block_rows, 0)

    def column_pos(block_number):
        return block_number * block_rows + jnp.arange(block_rows, dtype=jnp.int32)

    buffer = jnp.zeros((tokens, 2 * local_groups * head_dim), jnp.float32)
    rows = query_rows.shape[0]
    row_pos = first_row + jnp.arange(rows, dtype=jnp.int32)
    needed = (first_row + rows - 1) // block_rows + 1
    query_heads = query_rows.reshape(rows, local_groups, group_size, head_dim)
    log_totals = []
    shared_head = 0
    query_group = query_heads[:, shared_head]

    def stats_step(block_number, carried):
        running_max, running_sum = carried
        key_block = fetch(keys_all, block_number)
        scores = block_scores(query_group, key_block, scaling, row_pos, column_pos(block_number))
        new_max = jnp.maximum(running_max, jnp.max(scores, axis=-1))
        running_sum = running_sum * jnp.exp(running_max - new_max) + jnp.sum(
            jnp.exp(scores - new_max[..., None]), axis=-1
        )
        return (new_max, running_sum)

    start_max = jnp.full((rows, group_size), NEGATIVE, jnp.float32)
    start_sum = jnp.zeros((rows, group_size), jnp.float32)
    running_max, running_sum = lax.fori_loop(0, needed, stats_step, (start_max, start_sum))
    log_total = running_max + jnp.log(running_sum)

    def value_step(block_number, accumulated):
        key_block = fetch(keys_all, block_number)
        value_block = fetch(values_all, block_number)
        scores = block_scores(query_group, key_block, scaling, row_pos, column_pos(block_number))
        rounded = jnp.exp(scores - log_total[..., None]).astype(jnp.bfloat16)
        return accumulated + jnp.einsum(
            "tgk,kd->tgd", rounded, value_block, preferred_element_type=jnp.float32
        )

    accumulated = lax.fori_loop(
        0, needed, value_step, jnp.zeros((rows, group_size, head_dim), jnp.float32)
    )
    log_totals.append(log_total)
    attended_list = [accumulated.astype(jnp.bfloat16)]
    attended_part = jnp.stack(attended_list, axis=1).reshape(
        rows, local_groups * group_size * head_dim
    )
    log_totals, attended = (log_totals, attended_part)
    grad_sum = lax.dot_general(
        piece_part, out_weight, (((1,), (1,)), ((), ())), preferred_element_type=jnp.float32
    )
    grad_sum, squares_out = (grad_sum, gram_squares(piece_part, attended, head_dim))
    grad_attended, squares_out = (grad_sum.astype(jnp.bfloat16), squares_out)
    backward_buffer = buffer
    rows = query_rows.shape[0]
    backward_row_pos = first_row + jnp.arange(rows, dtype=jnp.int32)
    needed = (first_row + rows - 1) // block_rows + 1
    query_heads = query_rows.reshape(rows, local_groups, group_size, head_dim)
    grad_heads = grad_attended.reshape(rows, local_groups, group_size, head_dim)
    attended_heads = attended.reshape(rows, local_groups, group_size, head_dim)
    shared_head = 0
    backward_query_group = query_heads[:, shared_head]
    grad_group = grad_heads[:, shared_head]
    backward_log_total = log_totals[shared_head]
    row_dot = jnp.sum(
        grad_group.astype(jnp.float32) * attended_heads[:, shared_head].astype(jnp.float32), axis=-1
    )
    grad_query_part, backward_buffer = flash_backward(
        backward_query_group.reshape(rows, group_size * head_dim),
        grad_group.reshape(rows, group_size * head_dim),
        keys_all,
        values_all,
        backward_log_total,
        row_dot,
        first_row,
        head_dim,
        block_rows,
    )
    ctx_size = lax.axis_size("ctx")
    key_sums = exchange_reduce(
        backward_buffer.reshape((ctx_size, tokens // ctx_size) + backward_buffer.shape[1:]), "ctx"
    )
    grad_key = key_sums[:, : local_groups * head_dim].astype(jnp.bfloat16)
    grad_value = key_sums[:, local_groups * head_dim :].astype(jnp.bfloat16)
    squares_query = gram_pair_squares(hidden_gram, grad_query_part, head_dim)
    normal_size = D * head_dim * tok_dev
    fisher_q = jnp.log(squares_query / normal_size + EPSILON).reshape(1, -1)
    fisher_o = jnp.log(squares_out / normal_size + EPSILON).reshape(1, -1)
    return (grad_query_part, grad_key, grad_value, fisher_q, fisher_o)


def solution(mesh):
    return jax.shard_map(
        body,
        mesh=mesh,
        in_specs=(
            P("ctx", "head"),
            P("ctx", "head"),
            P("ctx", "head"),
            P("ctx", "head"),
            P("head", None),
            P("ctx", "head"),
            P("ctx"),
        ),
        out_specs=(
            P("ctx", "head"),
            P("ctx", "head"),
            P("ctx", "head"),
            P("ctx", "head"),
            P("ctx", "head"),
        ),
        check_vma=False,
    )
```

```python
import math

import jax
import jax.numpy as jnp
from jax import lax
from jax.experimental import pallas as pl
from jax.experimental.pallas import tpu as pltpu
from jax.sharding import PartitionSpec as P

D = 8192
HEADS = 64
KVH = 8
HD = 128


NEGATIVE = -1e30
EPSILON = 1e-06


def block_scores(query_group, key_block, scaling, row_pos, col_pos):
    scores = (
        jnp.einsum("tgd,kd->tgk", query_group, key_block, preferred_element_type=jnp.float32)
        * scaling
    )
    return jnp.where(row_pos[:, None, None] >= col_pos[None, None, :], scores, NEGATIVE)


def head_squares(left_side, right_side, head_dim):
    product = lax.dot_general(
        left_side, right_side, (((0,), (0,)), ((), ())), preferred_element_type=jnp.float32
    )
    shaped = (product * product).reshape(
        product.shape[0], right_side.shape[1] // head_dim, head_dim
    )
    return jnp.sum(shaped, axis=(0, 2))


def flash_backward(query_rows, grad_attended, keys_all, values_all, log_total, row_dot, first_row, head_dim, block_rows):
    rows, width = query_rows.shape
    heads = width // head_dim
    tokens = keys_all.shape[0]
    blocks = tokens // block_rows
    scaling = head_dim ** (-0.5)
    needed = (first_row + rows - 1) // block_rows + 1
    scalars = jnp.stack([needed, first_row]).astype(jnp.int32)

    def kernel(scalar_ref, q_ref, do_ref, k_ref, v_ref, lt_ref, rd_ref, dq_ref, dkv_ref, dq_acc):
        j = pl.program_id(0)

        @pl.when(j == 0)
        def _():
            dq_acc[...] = jnp.zeros_like(dq_acc)

        @pl.when(j < scalar_ref[0])
        def _():
            k = k_ref[...]
            v = v_ref[...]
            row_pos = scalar_ref[1] + lax.broadcasted_iota(jnp.int32, (rows, block_rows), 0)
            col_pos = j * block_rows + lax.broadcasted_iota(jnp.int32, (rows, block_rows), 1)
            keep = row_pos >= col_pos
            dk = jnp.zeros((block_rows, head_dim), jnp.float32)
            dv = jnp.zeros((block_rows, head_dim), jnp.float32)
            for h in range(heads):
                cols = slice(h * head_dim, (h + 1) * head_dim)
                q = q_ref[:, cols]
                do = do_ref[:, cols]
                s = lax.dot_general(q, k, (((1,), (1,)), ((), ())), preferred_element_type=jnp.float32) * scaling
                s = jnp.where(keep, s, NEGATIVE)
                p = jnp.exp(s - lt_ref[:, h : h + 1])
                dp = lax.dot_general(do, v, (((1,), (1,)), ((), ())), preferred_element_type=jnp.float32)
                ds = (p * (dp - rd_ref[:, h : h + 1]) * scaling).astype(jnp.bfloat16)
                dq_acc[:, cols] += jnp.dot(ds, k, preferred_element_type=jnp.float32)
                dk += lax.dot_general(ds, q, (((0,), (0,)), ((), ())), preferred_element_type=jnp.float32)
                dv += lax.dot_general(p.astype(jnp.bfloat16), do, (((0,), (0,)), ((), ())), preferred_element_type=jnp.float32)
            dkv_ref[:, :head_dim] = dk.astype(dkv_ref.dtype)
            dkv_ref[:, head_dim:] = dv.astype(dkv_ref.dtype)

        @pl.when(j >= scalar_ref[0])
        def _():
            dkv_ref[...] = jnp.zeros_like(dkv_ref)

        @pl.when(j == blocks - 1)
        def _():
            dq_ref[...] = dq_acc[...].astype(dq_ref.dtype)

    def kv_map(j, s):
        return (jnp.minimum(j, s[0] - 1), 0)

    full = lambda j, s: (0, 0)
    grid_spec = pltpu.PrefetchScalarGridSpec(
        num_scalar_prefetch=1,
        grid=(blocks,),
        in_specs=[
            pl.BlockSpec((rows, width), full),
            pl.BlockSpec((rows, width), full),
            pl.BlockSpec((block_rows, head_dim), kv_map),
            pl.BlockSpec((block_rows, head_dim), kv_map),
            pl.BlockSpec((rows, heads), full),
            pl.BlockSpec((rows, heads), full),
        ],
        out_specs=[
            pl.BlockSpec((rows, width), full),
            pl.BlockSpec((block_rows, 2 * head_dim), lambda j, s: (j, 0)),
        ],
        scratch_shapes=[pltpu.VMEM((rows, width), jnp.float32)],
    )
    return pl.pallas_call(
        kernel,
        grid_spec=grid_spec,
        out_shape=[
            jax.ShapeDtypeStruct((rows, width), jnp.bfloat16),
            jax.ShapeDtypeStruct((tokens, 2 * head_dim), jnp.bfloat16),
        ],
        compiler_params=pltpu.CompilerParams(dimension_semantics=("arbitrary",)),
    )(scalars, query_rows, grad_attended, keys_all, values_all, log_total, row_dot)


def butterfly_gather(value, axis_name):
    size = lax.axis_size(axis_name)
    own = lax.axis_index(axis_name)
    held = value[None]
    stride = size // 2
    bits = 0
    while stride >= 1:
        pairs = [(i, i ^ stride) for i in range(size)]
        other = lax.ppermute(held, axis_name, pairs)
        low = (own & stride) == 0
        held = jnp.where(
            low, jnp.concatenate([held, other], 0), jnp.concatenate([other, held], 0)
        )
        stride //= 2
        bits += 1
    held = held.reshape((2,) * bits + value.shape)
    held = held.transpose(tuple(range(bits))[::-1] + tuple(range(bits, bits + value.ndim)))
    return held.reshape((size * value.shape[0],) + value.shape[1:])


def causal_gather(value, axis_name):
    size = lax.axis_size(axis_name)
    own = lax.axis_index(axis_name)
    received = [value]
    for shift in range(1, size):
        pairs = [(i, i + shift) for i in range(size - shift)]
        received.append(lax.ppermute(value, axis_name, pairs))
    by_shift = jnp.stack(received[::-1], 0)
    doubled = jnp.concatenate([by_shift, by_shift], 0)
    blocks = lax.dynamic_slice_in_dim(doubled, size - 1 - own, size, 0)
    return blocks.reshape((size * value.shape[0],) + value.shape[1:])


def causal_reduce(parts, axis_name):
    size = lax.axis_size(axis_name)
    own = lax.axis_index(axis_name)
    total = lax.dynamic_index_in_dim(parts, own, 0, keepdims=False).astype(jnp.float32)
    for shift in range(1, size):
        pairs = [(i, i - shift) for i in range(shift, size)]
        sent = lax.dynamic_index_in_dim(parts, jnp.maximum(own - shift, 0), 0, keepdims=False)
        total = total + lax.ppermute(sent, axis_name, pairs).astype(jnp.float32)
    return total


def exchange_reduce(parts, axis_name):
    arrived = lax.all_to_all(parts, axis_name, 0, 0, tiled=True)
    return jnp.sum(arrived.astype(jnp.float32), axis=0)


def butterfly_sum(value, axis_name):
    size = lax.axis_size(axis_name)
    stride = 1
    while stride < size:
        pairs = [(i, i ^ stride) for i in range(size)]
        value = value + lax.ppermute(value, axis_name, pairs)
        stride *= 2
    return value


def gram_pair_squares(left_gram, right_side, head_dim):
    rows = right_side.shape[0]
    right_heads = right_side.reshape(rows, right_side.shape[1] // head_dim, head_dim)
    right_gram = jnp.einsum(
        "ihd,jhd->hij", right_heads, right_heads, preferred_element_type=jnp.float32
    )
    return jnp.sum(right_gram * left_gram[None], axis=(1, 2))


def gram_squares(left_side, right_side, head_dim):
    left_gram = lax.dot_general(
        left_side, left_side, (((1,), (1,)), ((), ())), preferred_element_type=jnp.float32
    )
    return gram_pair_squares(left_gram, right_side, head_dim)


def body(hidden_in, query_rows, key_rows, value_rows, out_weight, grad_out, answer_mask):
    tok_dev = query_rows.shape[0]
    head_dim = HD
    group_size = HEADS // KVH
    local_groups = key_rows.shape[1] // head_dim
    scaling = head_dim ** (-0.5)
    own_index = lax.axis_index("ctx")
    first_row = own_index * tok_dev
    loss_weight = 0.25 + answer_mask.astype(jnp.float32)
    weighted = (grad_out.astype(jnp.float32) * loss_weight[:, None]).astype(jnp.bfloat16)
    hidden_gram = butterfly_sum(
        lax.dot_general(
            hidden_in, hidden_in, (((1,), (1,)), ((), ())), preferred_element_type=jnp.float32
        ),
        "head",
    )
    piece_part = (
        lax.all_gather(grad_out, "head", axis=1, tiled=True).astype(jnp.float32)
        * loss_weight[:, None]
    ).astype(jnp.bfloat16)
    pair_all = causal_gather(jnp.concatenate([key_rows, value_rows], axis=1), "ctx")
    kv_width = key_rows.shape[1]
    keys_all, values_all = (pair_all[:, :kv_width], pair_all[:, kv_width:])
    tokens = keys_all.shape[0]
    block_rows = math.gcd(512, tokens)

    def fetch(table, block_number):
        return lax.dynamic_slice_in_dim(table, block_number * block_rows, block_rows, 0)

    def column_pos(block_number):
        return block_number * block_rows + jnp.arange(block_rows, dtype=jnp.int32)

    buffer = jnp.zeros((tokens, 2 * local_groups * head_dim), jnp.float32)
    rows = query_rows.shape[0]
    row_pos = first_row + jnp.arange(rows, dtype=jnp.int32)
    needed = (first_row + rows - 1) // block_rows + 1
    query_heads = query_rows.reshape(rows, local_groups, group_size, head_dim)
    log_totals = []
    shared_head = 0
    query_group = query_heads[:, shared_head]

    def stats_step(block_number, carried):
        running_max, running_sum = carried
        key_block = fetch(keys_all, block_number)
        scores = block_scores(query_group, key_block, scaling, row_pos, column_pos(block_number))
        new_max = jnp.maximum(running_max, jnp.max(scores, axis=-1))
        running_sum = running_sum * jnp.exp(running_max - new_max) + jnp.sum(
            jnp.exp(scores - new_max[..., None]), axis=-1
        )
        return (new_max, running_sum)

    start_max = jnp.full((rows, group_size), NEGATIVE, jnp.float32)
    start_sum = jnp.zeros((rows, group_size), jnp.float32)
    running_max, running_sum = lax.fori_loop(0, needed, stats_step, (start_max, start_sum))
    log_total = running_max + jnp.log(running_sum)

    def value_step(block_number, accumulated):
        key_block = fetch(keys_all, block_number)
        value_block = fetch(values_all, block_number)
        scores = block_scores(query_group, key_block, scaling, row_pos, column_pos(block_number))
        rounded = jnp.exp(scores - log_total[..., None]).astype(jnp.bfloat16)
        return accumulated + jnp.einsum(
            "tgk,kd->tgd", rounded, value_block, preferred_element_type=jnp.float32
        )

    accumulated = lax.fori_loop(
        0, needed, value_step, jnp.zeros((rows, group_size, head_dim), jnp.float32)
    )
    log_totals.append(log_total)
    attended_list = [accumulated.astype(jnp.bfloat16)]
    attended_part = jnp.stack(attended_list, axis=1).reshape(
        rows, local_groups * group_size * head_dim
    )
    log_totals, attended = (log_totals, attended_part)
    grad_sum = lax.dot_general(
        piece_part, out_weight, (((1,), (1,)), ((), ())), preferred_element_type=jnp.float32
    )
    grad_sum, squares_out = (grad_sum, gram_squares(piece_part, attended, head_dim))
    grad_attended, squares_out = (grad_sum.astype(jnp.bfloat16), squares_out)
    hidden_gram, grad_attended = lax.optimization_barrier((hidden_gram, grad_attended))
    backward_buffer = buffer
    rows = query_rows.shape[0]
    backward_row_pos = first_row + jnp.arange(rows, dtype=jnp.int32)
    needed = (first_row + rows - 1) // block_rows + 1
    query_heads = query_rows.reshape(rows, local_groups, group_size, head_dim)
    grad_heads = grad_attended.reshape(rows, local_groups, group_size, head_dim)
    attended_heads = attended.reshape(rows, local_groups, group_size, head_dim)
    shared_head = 0
    backward_query_group = query_heads[:, shared_head]
    grad_group = grad_heads[:, shared_head]
    backward_log_total = log_totals[shared_head]
    row_dot = jnp.sum(
        grad_group.astype(jnp.float32) * attended_heads[:, shared_head].astype(jnp.float32), axis=-1
    )
    grad_query_part, backward_buffer = flash_backward(
        backward_query_group.reshape(rows, group_size * head_dim),
        grad_group.reshape(rows, group_size * head_dim),
        keys_all,
        values_all,
        backward_log_total,
        row_dot,
        first_row,
        head_dim,
        block_rows,
    )
    ctx_size = lax.axis_size("ctx")
    key_sums = exchange_reduce(
        backward_buffer.reshape((ctx_size, tokens // ctx_size) + backward_buffer.shape[1:]), "ctx"
    )
    grad_key = key_sums[:, : local_groups * head_dim].astype(jnp.bfloat16)
    grad_value = key_sums[:, local_groups * head_dim :].astype(jnp.bfloat16)
    squares_query = gram_pair_squares(hidden_gram, grad_query_part, head_dim)
    normal_size = D * head_dim * tok_dev
    fisher_q = jnp.log(squares_query / normal_size + EPSILON).reshape(1, -1)
    fisher_o = jnp.log(squares_out / normal_size + EPSILON).reshape(1, -1)
    return (grad_query_part, grad_key, grad_value, fisher_q, fisher_o)


def solution(mesh):
    return jax.shard_map(
        body,
        mesh=mesh,
        in_specs=(
            P("ctx", "head"),
            P("ctx", "head"),
            P("ctx", "head"),
            P("ctx", "head"),
            P("head", None),
            P("ctx", "head"),
            P("ctx"),
        ),
        out_specs=(
            P("ctx", "head"),
            P("ctx", "head"),
            P("ctx", "head"),
            P("ctx", "head"),
            P("ctx", "head"),
        ),
        check_vma=False,
    )
```

```python
import math

import jax
import jax.numpy as jnp
from jax import lax
from jax.experimental import pallas as pl
from jax.experimental.pallas import tpu as pltpu
from jax.sharding import PartitionSpec as P

D = 8192
HEADS = 64
KVH = 8
HD = 128


NEGATIVE = -1e30
EPSILON = 1e-06


def block_scores(query_group, key_block, scaling, row_pos, col_pos):
    scores = (
        jnp.einsum("tgd,kd->tgk", query_group, key_block, preferred_element_type=jnp.float32)
        * scaling
    )
    return jnp.where(row_pos[:, None, None] >= col_pos[None, None, :], scores, NEGATIVE)


def head_squares(left_side, right_side, head_dim):
    product = lax.dot_general(
        left_side, right_side, (((0,), (0,)), ((), ())), preferred_element_type=jnp.float32
    )
    shaped = (product * product).reshape(
        product.shape[0], right_side.shape[1] // head_dim, head_dim
    )
    return jnp.sum(shaped, axis=(0, 2))


def flash_backward(query_rows, grad_attended, keys_all, values_all, log_total, row_dot, first_row, head_dim, block_rows):
    rows, width = query_rows.shape
    heads = width // head_dim
    tokens = keys_all.shape[0]
    blocks = tokens // block_rows
    scaling = head_dim ** (-0.5)
    needed = (first_row + rows - 1) // block_rows + 1
    scalars = jnp.stack([needed, first_row]).astype(jnp.int32)

    def kernel(scalar_ref, q_ref, do_ref, k_ref, v_ref, lt_ref, rd_ref, dq_ref, dkv_ref, dq_acc):
        j = pl.program_id(0)

        @pl.when(j == 0)
        def _():
            dq_acc[...] = jnp.zeros_like(dq_acc)

        @pl.when(j < scalar_ref[0])
        def _():
            k = k_ref[...]
            v = v_ref[...]
            row_pos = scalar_ref[1] + lax.broadcasted_iota(jnp.int32, (rows, block_rows), 0)
            col_pos = j * block_rows + lax.broadcasted_iota(jnp.int32, (rows, block_rows), 1)
            keep = row_pos >= col_pos
            dk = jnp.zeros((block_rows, head_dim), jnp.float32)
            dv = jnp.zeros((block_rows, head_dim), jnp.float32)
            for h in range(heads):
                cols = slice(h * head_dim, (h + 1) * head_dim)
                q = q_ref[:, cols]
                do = do_ref[:, cols]
                s = lax.dot_general(q, k, (((1,), (1,)), ((), ())), preferred_element_type=jnp.float32) * scaling
                s = jnp.where(keep, s, NEGATIVE)
                p = jnp.exp(s - lt_ref[:, h : h + 1])
                dp = lax.dot_general(do, v, (((1,), (1,)), ((), ())), preferred_element_type=jnp.float32)
                ds = (p * (dp - rd_ref[:, h : h + 1]) * scaling).astype(jnp.bfloat16)
                dq_acc[:, cols] += jnp.dot(ds, k, preferred_element_type=jnp.float32)
                dk += lax.dot_general(ds, q, (((0,), (0,)), ((), ())), preferred_element_type=jnp.float32)
                dv += lax.dot_general(p.astype(jnp.bfloat16), do, (((0,), (0,)), ((), ())), preferred_element_type=jnp.float32)
            dkv_ref[:, :head_dim] = dk.astype(dkv_ref.dtype)
            dkv_ref[:, head_dim:] = dv.astype(dkv_ref.dtype)

        @pl.when(j >= scalar_ref[0])
        def _():
            dkv_ref[...] = jnp.zeros_like(dkv_ref)

        @pl.when(j == blocks - 1)
        def _():
            dq_ref[...] = dq_acc[...].astype(dq_ref.dtype)

    def kv_map(j, s):
        return (jnp.minimum(j, s[0] - 1), 0)

    full = lambda j, s: (0, 0)
    grid_spec = pltpu.PrefetchScalarGridSpec(
        num_scalar_prefetch=1,
        grid=(blocks,),
        in_specs=[
            pl.BlockSpec((rows, width), full),
            pl.BlockSpec((rows, width), full),
            pl.BlockSpec((block_rows, head_dim), kv_map),
            pl.BlockSpec((block_rows, head_dim), kv_map),
            pl.BlockSpec((rows, heads), full),
            pl.BlockSpec((rows, heads), full),
        ],
        out_specs=[
            pl.BlockSpec((rows, width), full),
            pl.BlockSpec((block_rows, 2 * head_dim), lambda j, s: (j, 0)),
        ],
        scratch_shapes=[pltpu.VMEM((rows, width), jnp.float32)],
    )
    return pl.pallas_call(
        kernel,
        grid_spec=grid_spec,
        out_shape=[
            jax.ShapeDtypeStruct((rows, width), jnp.bfloat16),
            jax.ShapeDtypeStruct((tokens, 2 * head_dim), jnp.bfloat16),
        ],
        compiler_params=pltpu.CompilerParams(dimension_semantics=("arbitrary",)),
    )(scalars, query_rows, grad_attended, keys_all, values_all, log_total, row_dot)


def butterfly_gather(value, axis_name):
    size = lax.axis_size(axis_name)
    own = lax.axis_index(axis_name)
    held = value[None]
    stride = size // 2
    bits = 0
    while stride >= 1:
        pairs = [(i, i ^ stride) for i in range(size)]
        other = lax.ppermute(held, axis_name, pairs)
        low = (own & stride) == 0
        held = jnp.where(
            low, jnp.concatenate([held, other], 0), jnp.concatenate([other, held], 0)
        )
        stride //= 2
        bits += 1
    held = held.reshape((2,) * bits + value.shape)
    held = held.transpose(tuple(range(bits))[::-1] + tuple(range(bits, bits + value.ndim)))
    return held.reshape((size * value.shape[0],) + value.shape[1:])


def causal_gather(value, axis_name):
    size = lax.axis_size(axis_name)
    own = lax.axis_index(axis_name)
    received = [value]
    for shift in range(1, size):
        pairs = [(i, i + shift) for i in range(size - shift)]
        received.append(lax.ppermute(value, axis_name, pairs))
    by_shift = jnp.stack(received[::-1], 0)
    doubled = jnp.concatenate([by_shift, by_shift], 0)
    blocks = lax.dynamic_slice_in_dim(doubled, size - 1 - own, size, 0)
    return blocks.reshape((size * value.shape[0],) + value.shape[1:])


def causal_reduce(parts, axis_name):
    size = lax.axis_size(axis_name)
    own = lax.axis_index(axis_name)
    total = lax.dynamic_index_in_dim(parts, own, 0, keepdims=False).astype(jnp.float32)
    for shift in range(1, size):
        pairs = [(i, i - shift) for i in range(shift, size)]
        sent = lax.dynamic_index_in_dim(parts, jnp.maximum(own - shift, 0), 0, keepdims=False)
        total = total + lax.ppermute(sent, axis_name, pairs).astype(jnp.float32)
    return total


def exchange_reduce(parts, axis_name):
    arrived = lax.all_to_all(parts, axis_name, 0, 0, tiled=True)
    return jnp.sum(arrived.astype(jnp.float32), axis=0)


def staged_gather(value, axis_name):
    size = lax.axis_size(axis_name)
    pairs = [[2 * i, 2 * i + 1] for i in range(size // 2)]
    across = [list(range(0, size, 2)), list(range(1, size, 2))]
    value = lax.all_gather(value, axis_name, axis=1, tiled=True, axis_index_groups=pairs)
    return lax.all_gather(value, axis_name, axis=1, tiled=True, axis_index_groups=across)


def butterfly_sum(value, axis_name):
    size = lax.axis_size(axis_name)
    stride = 1
    while stride < size:
        pairs = [(i, i ^ stride) for i in range(size)]
        value = value + lax.ppermute(value, axis_name, pairs)
        stride *= 2
    return value


def gram_pair_squares(left_gram, right_side, head_dim):
    rows = right_side.shape[0]
    right_heads = right_side.reshape(rows, right_side.shape[1] // head_dim, head_dim)
    right_gram = jnp.einsum(
        "ihd,jhd->hij", right_heads, right_heads, preferred_element_type=jnp.float32
    )
    return jnp.sum(right_gram * left_gram[None], axis=(1, 2))


def gram_squares(left_side, right_side, head_dim):
    left_gram = lax.dot_general(
        left_side, left_side, (((1,), (1,)), ((), ())), preferred_element_type=jnp.float32
    )
    return gram_pair_squares(left_gram, right_side, head_dim)


def body(hidden_in, query_rows, key_rows, value_rows, out_weight, grad_out, answer_mask):
    tok_dev = query_rows.shape[0]
    head_dim = HD
    group_size = HEADS // KVH
    local_groups = key_rows.shape[1] // head_dim
    scaling = head_dim ** (-0.5)
    own_index = lax.axis_index("ctx")
    first_row = own_index * tok_dev
    loss_weight = 0.25 + answer_mask.astype(jnp.float32)
    weighted = (grad_out.astype(jnp.float32) * loss_weight[:, None]).astype(jnp.bfloat16)
    hidden_gram = butterfly_sum(
        lax.dot_general(
            hidden_in, hidden_in, (((1,), (1,)), ((), ())), preferred_element_type=jnp.float32
        ),
        "head",
    )
    piece_part = (
        staged_gather(grad_out, "head").astype(jnp.float32)
        * loss_weight[:, None]
    ).astype(jnp.bfloat16)
    pair_all = causal_gather(jnp.concatenate([key_rows, value_rows], axis=1), "ctx")
    kv_width = key_rows.shape[1]
    keys_all, values_all = (pair_all[:, :kv_width], pair_all[:, kv_width:])
    tokens = keys_all.shape[0]
    block_rows = math.gcd(512, tokens)

    def fetch(table, block_number):
        return lax.dynamic_slice_in_dim(table, block_number * block_rows, block_rows, 0)

    def column_pos(block_number):
        return block_number * block_rows + jnp.arange(block_rows, dtype=jnp.int32)

    buffer = jnp.zeros((tokens, 2 * local_groups * head_dim), jnp.float32)
    rows = query_rows.shape[0]
    row_pos = first_row + jnp.arange(rows, dtype=jnp.int32)
    needed = (first_row + rows - 1) // block_rows + 1
    query_heads = query_rows.reshape(rows, local_groups, group_size, head_dim)
    log_totals = []
    shared_head = 0
    query_group = query_heads[:, shared_head]

    def stats_step(block_number, carried):
        running_max, running_sum = carried
        key_block = fetch(keys_all, block_number)
        scores = block_scores(query_group, key_block, scaling, row_pos, column_pos(block_number))
        new_max = jnp.maximum(running_max, jnp.max(scores, axis=-1))
        running_sum = running_sum * jnp.exp(running_max - new_max) + jnp.sum(
            jnp.exp(scores - new_max[..., None]), axis=-1
        )
        return (new_max, running_sum)

    start_max = jnp.full((rows, group_size), NEGATIVE, jnp.float32)
    start_sum = jnp.zeros((rows, group_size), jnp.float32)
    running_max, running_sum = lax.fori_loop(0, needed, stats_step, (start_max, start_sum))
    log_total = running_max + jnp.log(running_sum)

    def value_step(block_number, accumulated):
        key_block = fetch(keys_all, block_number)
        value_block = fetch(values_all, block_number)
        scores = block_scores(query_group, key_block, scaling, row_pos, column_pos(block_number))
        rounded = jnp.exp(scores - log_total[..., None]).astype(jnp.bfloat16)
        return accumulated + jnp.einsum(
            "tgk,kd->tgd", rounded, value_block, preferred_element_type=jnp.float32
        )

    accumulated = lax.fori_loop(
        0, needed, value_step, jnp.zeros((rows, group_size, head_dim), jnp.float32)
    )
    log_totals.append(log_total)
    attended_list = [accumulated.astype(jnp.bfloat16)]
    attended_part = jnp.stack(attended_list, axis=1).reshape(
        rows, local_groups * group_size * head_dim
    )
    log_totals, attended = (log_totals, attended_part)
    grad_sum = lax.dot_general(
        piece_part, out_weight, (((1,), (1,)), ((), ())), preferred_element_type=jnp.float32
    )
    grad_sum, squares_out = (grad_sum, gram_squares(piece_part, attended, head_dim))
    grad_attended, squares_out = (grad_sum.astype(jnp.bfloat16), squares_out)
    backward_buffer = buffer
    rows = query_rows.shape[0]
    backward_row_pos = first_row + jnp.arange(rows, dtype=jnp.int32)
    needed = (first_row + rows - 1) // block_rows + 1
    query_heads = query_rows.reshape(rows, local_groups, group_size, head_dim)
    grad_heads = grad_attended.reshape(rows, local_groups, group_size, head_dim)
    attended_heads = attended.reshape(rows, local_groups, group_size, head_dim)
    shared_head = 0
    backward_query_group = query_heads[:, shared_head]
    grad_group = grad_heads[:, shared_head]
    backward_log_total = log_totals[shared_head]
    row_dot = jnp.sum(
        grad_group.astype(jnp.float32) * attended_heads[:, shared_head].astype(jnp.float32), axis=-1
    )
    grad_query_part, backward_buffer = flash_backward(
        backward_query_group.reshape(rows, group_size * head_dim),
        grad_group.reshape(rows, group_size * head_dim),
        keys_all,
        values_all,
        backward_log_total,
        row_dot,
        first_row,
        head_dim,
        block_rows,
    )
    ctx_size = lax.axis_size("ctx")
    key_sums = exchange_reduce(
        backward_buffer.reshape((ctx_size, tokens // ctx_size) + backward_buffer.shape[1:]), "ctx"
    )
    grad_key = key_sums[:, : local_groups * head_dim].astype(jnp.bfloat16)
    grad_value = key_sums[:, local_groups * head_dim :].astype(jnp.bfloat16)
    squares_query = gram_pair_squares(hidden_gram, grad_query_part, head_dim)
    normal_size = D * head_dim * tok_dev
    fisher_q = jnp.log(squares_query / normal_size + EPSILON).reshape(1, -1)
    fisher_o = jnp.log(squares_out / normal_size + EPSILON).reshape(1, -1)
    return (grad_query_part, grad_key, grad_value, fisher_q, fisher_o)


def solution(mesh):
    return jax.shard_map(
        body,
        mesh=mesh,
        in_specs=(
            P("ctx", "head"),
            P("ctx", "head"),
            P("ctx", "head"),
            P("ctx", "head"),
            P("head", None),
            P("ctx", "head"),
            P("ctx"),
        ),
        out_specs=(
            P("ctx", "head"),
            P("ctx", "head"),
            P("ctx", "head"),
            P("ctx", "head"),
            P("ctx", "head"),
        ),
        check_vma=False,
    )
```

```python
import math

import jax
import jax.numpy as jnp
from jax import lax
from jax.experimental import pallas as pl
from jax.experimental.pallas import tpu as pltpu
from jax.sharding import PartitionSpec as P

D = 8192
HEADS = 64
KVH = 8
HD = 128


NEGATIVE = -1e30
EPSILON = 1e-06


def block_scores(query_group, key_block, scaling, row_pos, col_pos):
    scores = (
        jnp.einsum("tgd,kd->tgk", query_group, key_block, preferred_element_type=jnp.float32)
        * scaling
    )
    return jnp.where(row_pos[:, None, None] >= col_pos[None, None, :], scores, NEGATIVE)


def head_squares(left_side, right_side, head_dim):
    product = lax.dot_general(
        left_side, right_side, (((0,), (0,)), ((), ())), preferred_element_type=jnp.float32
    )
    shaped = (product * product).reshape(
        product.shape[0], right_side.shape[1] // head_dim, head_dim
    )
    return jnp.sum(shaped, axis=(0, 2))


def flash_backward(query_rows, grad_attended, keys_all, values_all, log_total, row_dot, first_row, head_dim, block_rows):
    rows, width = query_rows.shape
    heads = width // head_dim
    tokens = keys_all.shape[0]
    blocks = tokens // block_rows
    scaling = head_dim ** (-0.5)
    needed = (first_row + rows - 1) // block_rows + 1
    scalars = jnp.stack([needed, first_row]).astype(jnp.int32)

    def kernel(scalar_ref, q_ref, do_ref, k_ref, v_ref, lt_ref, rd_ref, dq_ref, dkv_ref, dq_acc):
        j = pl.program_id(0)

        @pl.when(j == 0)
        def _():
            dq_acc[...] = jnp.zeros_like(dq_acc)

        @pl.when(j < scalar_ref[0])
        def _():
            k = k_ref[...]
            v = v_ref[...]
            row_pos = scalar_ref[1] + lax.broadcasted_iota(jnp.int32, (rows, block_rows), 0)
            col_pos = j * block_rows + lax.broadcasted_iota(jnp.int32, (rows, block_rows), 1)
            keep = row_pos >= col_pos
            dk = jnp.zeros((block_rows, head_dim), jnp.float32)
            dv = jnp.zeros((block_rows, head_dim), jnp.float32)
            for h in range(heads):
                cols = slice(h * head_dim, (h + 1) * head_dim)
                q = q_ref[:, cols]
                do = do_ref[:, cols]
                s = lax.dot_general(q, k, (((1,), (1,)), ((), ())), preferred_element_type=jnp.float32) * scaling
                s = jnp.where(keep, s, NEGATIVE)
                p = jnp.exp(s - lt_ref[:, h : h + 1])
                dp = lax.dot_general(do, v, (((1,), (1,)), ((), ())), preferred_element_type=jnp.float32)
                ds = (p * (dp - rd_ref[:, h : h + 1])).astype(jnp.bfloat16)
                dq_acc[:, cols] += jnp.dot(ds, k, preferred_element_type=jnp.float32)
                dk += lax.dot_general(ds, q, (((0,), (0,)), ((), ())), preferred_element_type=jnp.float32)
                dv += lax.dot_general(p.astype(jnp.bfloat16), do, (((0,), (0,)), ((), ())), preferred_element_type=jnp.float32)
            dkv_ref[:, :head_dim] = (dk * scaling).astype(dkv_ref.dtype)
            dkv_ref[:, head_dim:] = dv.astype(dkv_ref.dtype)

        @pl.when(j >= scalar_ref[0])
        def _():
            dkv_ref[...] = jnp.zeros_like(dkv_ref)

        @pl.when(j == blocks - 1)
        def _():
            dq_ref[...] = (dq_acc[...] * scaling).astype(dq_ref.dtype)

    def kv_map(j, s):
        return (jnp.minimum(j, s[0] - 1), 0)

    full = lambda j, s: (0, 0)
    grid_spec = pltpu.PrefetchScalarGridSpec(
        num_scalar_prefetch=1,
        grid=(blocks,),
        in_specs=[
            pl.BlockSpec((rows, width), full),
            pl.BlockSpec((rows, width), full),
            pl.BlockSpec((block_rows, head_dim), kv_map),
            pl.BlockSpec((block_rows, head_dim), kv_map),
            pl.BlockSpec((rows, heads), full),
            pl.BlockSpec((rows, heads), full),
        ],
        out_specs=[
            pl.BlockSpec((rows, width), full),
            pl.BlockSpec((block_rows, 2 * head_dim), lambda j, s: (j, 0)),
        ],
        scratch_shapes=[pltpu.VMEM((rows, width), jnp.float32)],
    )
    return pl.pallas_call(
        kernel,
        grid_spec=grid_spec,
        out_shape=[
            jax.ShapeDtypeStruct((rows, width), jnp.bfloat16),
            jax.ShapeDtypeStruct((tokens, 2 * head_dim), jnp.bfloat16),
        ],
        compiler_params=pltpu.CompilerParams(dimension_semantics=("arbitrary",)),
    )(scalars, query_rows, grad_attended, keys_all, values_all, log_total, row_dot)


def butterfly_gather(value, axis_name):
    size = lax.axis_size(axis_name)
    own = lax.axis_index(axis_name)
    held = value[None]
    stride = size // 2
    bits = 0
    while stride >= 1:
        pairs = [(i, i ^ stride) for i in range(size)]
        other = lax.ppermute(held, axis_name, pairs)
        low = (own & stride) == 0
        held = jnp.where(
            low, jnp.concatenate([held, other], 0), jnp.concatenate([other, held], 0)
        )
        stride //= 2
        bits += 1
    held = held.reshape((2,) * bits + value.shape)
    held = held.transpose(tuple(range(bits))[::-1] + tuple(range(bits, bits + value.ndim)))
    return held.reshape((size * value.shape[0],) + value.shape[1:])


def causal_gather(value, axis_name):
    size = lax.axis_size(axis_name)
    own = lax.axis_index(axis_name)
    received = [value]
    for shift in range(1, size):
        pairs = [(i, i + shift) for i in range(size - shift)]
        received.append(lax.ppermute(value, axis_name, pairs))
    by_shift = jnp.stack(received[::-1], 0)
    doubled = jnp.concatenate([by_shift, by_shift], 0)
    blocks = lax.dynamic_slice_in_dim(doubled, size - 1 - own, size, 0)
    return blocks.reshape((size * value.shape[0],) + value.shape[1:])


def causal_reduce(parts, axis_name):
    size = lax.axis_size(axis_name)
    own = lax.axis_index(axis_name)
    total = lax.dynamic_index_in_dim(parts, own, 0, keepdims=False).astype(jnp.float32)
    for shift in range(1, size):
        pairs = [(i, i - shift) for i in range(shift, size)]
        sent = lax.dynamic_index_in_dim(parts, jnp.maximum(own - shift, 0), 0, keepdims=False)
        total = total + lax.ppermute(sent, axis_name, pairs).astype(jnp.float32)
    return total


def exchange_reduce(parts, axis_name):
    arrived = lax.all_to_all(parts, axis_name, 0, 0, tiled=True)
    return jnp.sum(arrived.astype(jnp.float32), axis=0)


def butterfly_sum(value, axis_name):
    size = lax.axis_size(axis_name)
    stride = 1
    while stride < size:
        pairs = [(i, i ^ stride) for i in range(size)]
        value = value + lax.ppermute(value, axis_name, pairs)
        stride *= 2
    return value


def gram_pair_squares(left_gram, right_side, head_dim):
    rows = right_side.shape[0]
    right_heads = right_side.reshape(rows, right_side.shape[1] // head_dim, head_dim)
    right_gram = jnp.einsum(
        "ihd,jhd->hij", right_heads, right_heads, preferred_element_type=jnp.float32
    )
    return jnp.sum(right_gram * left_gram[None], axis=(1, 2))


def gram_squares(left_side, right_side, head_dim):
    left_gram = lax.dot_general(
        left_side, left_side, (((1,), (1,)), ((), ())), preferred_element_type=jnp.float32
    )
    return gram_pair_squares(left_gram, right_side, head_dim)


def body(hidden_in, query_rows, key_rows, value_rows, out_weight, grad_out, answer_mask):
    tok_dev = query_rows.shape[0]
    head_dim = HD
    group_size = HEADS // KVH
    local_groups = key_rows.shape[1] // head_dim
    scaling = head_dim ** (-0.5)
    own_index = lax.axis_index("ctx")
    first_row = own_index * tok_dev
    loss_weight = 0.25 + answer_mask.astype(jnp.float32)
    weighted = (grad_out.astype(jnp.float32) * loss_weight[:, None]).astype(jnp.bfloat16)
    hidden_gram = butterfly_sum(
        lax.dot_general(
            hidden_in, hidden_in, (((1,), (1,)), ((), ())), preferred_element_type=jnp.float32
        ),
        "head",
    )
    piece_part = (
        lax.all_gather(grad_out, "head", axis=1, tiled=True).astype(jnp.float32)
        * loss_weight[:, None]
    ).astype(jnp.bfloat16)
    pair_all = causal_gather(jnp.concatenate([key_rows, value_rows], axis=1), "ctx")
    kv_width = key_rows.shape[1]
    keys_all, values_all = (pair_all[:, :kv_width], pair_all[:, kv_width:])
    tokens = keys_all.shape[0]
    block_rows = math.gcd(512, tokens)

    def fetch(table, block_number):
        return lax.dynamic_slice_in_dim(table, block_number * block_rows, block_rows, 0)

    def column_pos(block_number):
        return block_number * block_rows + jnp.arange(block_rows, dtype=jnp.int32)

    buffer = jnp.zeros((tokens, 2 * local_groups * head_dim), jnp.float32)
    rows = query_rows.shape[0]
    row_pos = first_row + jnp.arange(rows, dtype=jnp.int32)
    needed = (first_row + rows - 1) // block_rows + 1
    query_heads = query_rows.reshape(rows, local_groups, group_size, head_dim)
    log_totals = []
    shared_head = 0
    query_group = query_heads[:, shared_head]

    def stats_step(block_number, carried):
        running_max, running_sum = carried
        key_block = fetch(keys_all, block_number)
        scores = block_scores(query_group, key_block, scaling, row_pos, column_pos(block_number))
        new_max = jnp.maximum(running_max, jnp.max(scores, axis=-1))
        running_sum = running_sum * jnp.exp(running_max - new_max) + jnp.sum(
            jnp.exp(scores - new_max[..., None]), axis=-1
        )
        return (new_max, running_sum)

    start_max = jnp.full((rows, group_size), NEGATIVE, jnp.float32)
    start_sum = jnp.zeros((rows, group_size), jnp.float32)
    running_max, running_sum = lax.fori_loop(0, needed, stats_step, (start_max, start_sum))
    log_total = running_max + jnp.log(running_sum)

    def value_step(block_number, accumulated):
        key_block = fetch(keys_all, block_number)
        value_block = fetch(values_all, block_number)
        scores = block_scores(query_group, key_block, scaling, row_pos, column_pos(block_number))
        rounded = jnp.exp(scores - log_total[..., None]).astype(jnp.bfloat16)
        return accumulated + jnp.einsum(
            "tgk,kd->tgd", rounded, value_block, preferred_element_type=jnp.float32
        )

    accumulated = lax.fori_loop(
        0, needed, value_step, jnp.zeros((rows, group_size, head_dim), jnp.float32)
    )
    log_totals.append(log_total)
    attended_list = [accumulated.astype(jnp.bfloat16)]
    attended_part = jnp.stack(attended_list, axis=1).reshape(
        rows, local_groups * group_size * head_dim
    )
    log_totals, attended = (log_totals, attended_part)
    grad_sum = lax.dot_general(
        piece_part, out_weight, (((1,), (1,)), ((), ())), preferred_element_type=jnp.float32
    )
    grad_sum, squares_out = (grad_sum, gram_squares(piece_part, attended, head_dim))
    grad_attended, squares_out = (grad_sum.astype(jnp.bfloat16), squares_out)
    backward_buffer = buffer
    rows = query_rows.shape[0]
    backward_row_pos = first_row + jnp.arange(rows, dtype=jnp.int32)
    needed = (first_row + rows - 1) // block_rows + 1
    query_heads = query_rows.reshape(rows, local_groups, group_size, head_dim)
    grad_heads = grad_attended.reshape(rows, local_groups, group_size, head_dim)
    attended_heads = attended.reshape(rows, local_groups, group_size, head_dim)
    shared_head = 0
    backward_query_group = query_heads[:, shared_head]
    grad_group = grad_heads[:, shared_head]
    backward_log_total = log_totals[shared_head]
    row_dot = jnp.sum(
        grad_group.astype(jnp.float32) * attended_heads[:, shared_head].astype(jnp.float32), axis=-1
    )
    grad_query_part, backward_buffer = flash_backward(
        backward_query_group.reshape(rows, group_size * head_dim),
        grad_group.reshape(rows, group_size * head_dim),
        keys_all,
        values_all,
        backward_log_total,
        row_dot,
        first_row,
        head_dim,
        block_rows,
    )
    ctx_size = lax.axis_size("ctx")
    key_sums = exchange_reduce(
        backward_buffer.reshape((ctx_size, tokens // ctx_size) + backward_buffer.shape[1:]), "ctx"
    )
    grad_key = key_sums[:, : local_groups * head_dim].astype(jnp.bfloat16)
    grad_value = key_sums[:, local_groups * head_dim :].astype(jnp.bfloat16)
    squares_query = gram_pair_squares(hidden_gram, grad_query_part, head_dim)
    normal_size = D * head_dim * tok_dev
    fisher_q = jnp.log(squares_query / normal_size + EPSILON).reshape(1, -1)
    fisher_o = jnp.log(squares_out / normal_size + EPSILON).reshape(1, -1)
    return (grad_query_part, grad_key, grad_value, fisher_q, fisher_o)


def solution(mesh):
    return jax.shard_map(
        body,
        mesh=mesh,
        in_specs=(
            P("ctx", "head"),
            P("ctx", "head"),
            P("ctx", "head"),
            P("ctx", "head"),
            P("head", None),
            P("ctx", "head"),
            P("ctx"),
        ),
        out_specs=(
            P("ctx", "head"),
            P("ctx", "head"),
            P("ctx", "head"),
            P("ctx", "head"),
            P("ctx", "head"),
        ),
        check_vma=False,
    )
```

```python
import math

import jax
import jax.numpy as jnp
from jax import lax
from jax.experimental import pallas as pl
from jax.experimental.pallas import tpu as pltpu
from jax.sharding import PartitionSpec as P

D = 8192
HEADS = 64
KVH = 8
HD = 128


NEGATIVE = -1e30
EPSILON = 1e-06


def block_scores(query_group, key_block, scaling, row_pos, col_pos):
    scores = (
        jnp.einsum("tgd,kd->tgk", query_group, key_block, preferred_element_type=jnp.float32)
        * scaling
    )
    return jnp.where(row_pos[:, None, None] >= col_pos[None, None, :], scores, NEGATIVE)


def head_squares(left_side, right_side, head_dim):
    product = lax.dot_general(
        left_side, right_side, (((0,), (0,)), ((), ())), preferred_element_type=jnp.float32
    )
    shaped = (product * product).reshape(
        product.shape[0], right_side.shape[1] // head_dim, head_dim
    )
    return jnp.sum(shaped, axis=(0, 2))


def flash_backward(query_rows, grad_attended, keys_all, values_all, log_total, row_dot, first_row, head_dim, block_rows):
    rows, width = query_rows.shape
    heads = width // head_dim
    tokens = keys_all.shape[0]
    blocks = tokens // block_rows
    scaling = head_dim ** (-0.5)
    needed = (first_row + rows - 1) // block_rows + 1
    scalars = jnp.stack([needed, first_row]).astype(jnp.int32)

    def kernel(scalar_ref, q_ref, do_ref, k_ref, v_ref, lt_ref, rd_ref, dq_ref, dkv_ref, dq_acc):
        j = pl.program_id(0)

        @pl.when(j == 0)
        def _():
            dq_acc[...] = jnp.zeros_like(dq_acc)

        @pl.when(j < scalar_ref[0])
        def _():
            k = k_ref[...]
            v = v_ref[...]
            row_pos = scalar_ref[1] + lax.broadcasted_iota(jnp.int32, (rows, block_rows), 0)
            col_pos = j * block_rows + lax.broadcasted_iota(jnp.int32, (rows, block_rows), 1)
            keep = row_pos >= col_pos
            dk = jnp.zeros((block_rows, head_dim), jnp.float32)
            dv = jnp.zeros((block_rows, head_dim), jnp.float32)
            for h in range(heads):
                cols = slice(h * head_dim, (h + 1) * head_dim)
                q = q_ref[:, cols]
                do = do_ref[:, cols]
                s = lax.dot_general(q, k, (((1,), (1,)), ((), ())), preferred_element_type=jnp.float32) * scaling
                s = jnp.where(keep, s, NEGATIVE)
                p = jnp.exp(s - lt_ref[:, h : h + 1])
                dp = lax.dot_general(do, v, (((1,), (1,)), ((), ())), preferred_element_type=jnp.float32)
                ds = (p * (dp - rd_ref[:, h : h + 1])).astype(jnp.bfloat16)
                dq_acc[:, cols] += jnp.dot(ds, k, preferred_element_type=jnp.float32)
                dk += lax.dot_general(ds, q, (((0,), (0,)), ((), ())), preferred_element_type=jnp.float32)
                dv += lax.dot_general(p.astype(jnp.bfloat16), do, (((0,), (0,)), ((), ())), preferred_element_type=jnp.float32)
            dkv_ref[:, :head_dim] = (dk * scaling).astype(dkv_ref.dtype)
            dkv_ref[:, head_dim:] = dv.astype(dkv_ref.dtype)

        @pl.when(j >= scalar_ref[0])
        def _():
            dkv_ref[...] = jnp.zeros_like(dkv_ref)

        @pl.when(j == blocks - 1)
        def _():
            dq_ref[...] = (dq_acc[...] * scaling).astype(dq_ref.dtype)

    def kv_map(j, s):
        return (jnp.minimum(j, s[0] - 1), 0)

    full = lambda j, s: (0, 0)
    grid_spec = pltpu.PrefetchScalarGridSpec(
        num_scalar_prefetch=1,
        grid=(blocks,),
        in_specs=[
            pl.BlockSpec((rows, width), full),
            pl.BlockSpec((rows, width), full),
            pl.BlockSpec((block_rows, head_dim), kv_map),
            pl.BlockSpec((block_rows, head_dim), kv_map),
            pl.BlockSpec((rows, heads), full),
            pl.BlockSpec((rows, heads), full),
        ],
        out_specs=[
            pl.BlockSpec((rows, width), full),
            pl.BlockSpec((block_rows, 2 * head_dim), lambda j, s: (j, 0)),
        ],
        scratch_shapes=[pltpu.VMEM((rows, width), jnp.float32)],
    )
    return pl.pallas_call(
        kernel,
        grid_spec=grid_spec,
        out_shape=[
            jax.ShapeDtypeStruct((rows, width), jnp.bfloat16),
            jax.ShapeDtypeStruct((tokens, 2 * head_dim), jnp.bfloat16),
        ],
        compiler_params=pltpu.CompilerParams(dimension_semantics=("arbitrary",)),
    )(scalars, query_rows, grad_attended, keys_all, values_all, log_total, row_dot)


def butterfly_gather(value, axis_name):
    size = lax.axis_size(axis_name)
    own = lax.axis_index(axis_name)
    held = value[None]
    stride = size // 2
    bits = 0
    while stride >= 1:
        pairs = [(i, i ^ stride) for i in range(size)]
        other = lax.ppermute(held, axis_name, pairs)
        low = (own & stride) == 0
        held = jnp.where(
            low, jnp.concatenate([held, other], 0), jnp.concatenate([other, held], 0)
        )
        stride //= 2
        bits += 1
    held = held.reshape((2,) * bits + value.shape)
    held = held.transpose(tuple(range(bits))[::-1] + tuple(range(bits, bits + value.ndim)))
    return held.reshape((size * value.shape[0],) + value.shape[1:])


def causal_gather(value, axis_name):
    size = lax.axis_size(axis_name)
    own = lax.axis_index(axis_name)
    received = [value]
    for shift in range(1, size):
        pairs = [(i, i + shift) for i in range(size - shift)]
        received.append(lax.ppermute(value, axis_name, pairs))
    by_shift = jnp.stack(received[::-1], 0)
    doubled = jnp.concatenate([by_shift, by_shift], 0)
    blocks = lax.dynamic_slice_in_dim(doubled, size - 1 - own, size, 0)
    return blocks.reshape((size * value.shape[0],) + value.shape[1:])


def causal_reduce(parts, axis_name):
    size = lax.axis_size(axis_name)
    own = lax.axis_index(axis_name)
    total = lax.dynamic_index_in_dim(parts, own, 0, keepdims=False).astype(jnp.float32)
    for shift in range(1, size):
        pairs = [(i, i - shift) for i in range(shift, size)]
        sent = lax.dynamic_index_in_dim(parts, jnp.maximum(own - shift, 0), 0, keepdims=False)
        total = total + lax.ppermute(sent, axis_name, pairs).astype(jnp.float32)
    return total


def exchange_gather(value, axis_name):
    size = lax.axis_size(axis_name)
    copies = jnp.broadcast_to(value[None], (size,) + value.shape)
    arrived = lax.all_to_all(copies, axis_name, 0, 0, tiled=True)
    return arrived.reshape((size * value.shape[0],) + value.shape[1:])


def exchange_reduce(parts, axis_name):
    arrived = lax.all_to_all(parts, axis_name, 0, 0, tiled=True)
    return jnp.sum(arrived.astype(jnp.float32), axis=0)


def butterfly_sum(value, axis_name):
    size = lax.axis_size(axis_name)
    stride = 1
    while stride < size:
        pairs = [(i, i ^ stride) for i in range(size)]
        value = value + lax.ppermute(value, axis_name, pairs)
        stride *= 2
    return value


def gram_pair_squares(left_gram, right_side, head_dim):
    rows = right_side.shape[0]
    right_heads = right_side.reshape(rows, right_side.shape[1] // head_dim, head_dim)
    right_gram = jnp.einsum(
        "ihd,jhd->hij", right_heads, right_heads, preferred_element_type=jnp.float32
    )
    return jnp.sum(right_gram * left_gram[None], axis=(1, 2))


def gram_squares(left_side, right_side, head_dim):
    left_gram = lax.dot_general(
        left_side, left_side, (((1,), (1,)), ((), ())), preferred_element_type=jnp.float32
    )
    return gram_pair_squares(left_gram, right_side, head_dim)


def body(hidden_in, query_rows, key_rows, value_rows, out_weight, grad_out, answer_mask):
    tok_dev = query_rows.shape[0]
    head_dim = HD
    group_size = HEADS // KVH
    local_groups = key_rows.shape[1] // head_dim
    scaling = head_dim ** (-0.5)
    own_index = lax.axis_index("ctx")
    first_row = own_index * tok_dev
    loss_weight = 0.25 + answer_mask.astype(jnp.float32)
    weighted = (grad_out.astype(jnp.float32) * loss_weight[:, None]).astype(jnp.bfloat16)
    hidden_gram = butterfly_sum(
        lax.dot_general(
            hidden_in, hidden_in, (((1,), (1,)), ((), ())), preferred_element_type=jnp.float32
        ),
        "head",
    )
    piece_part = (
        lax.all_gather(grad_out, "head", axis=1, tiled=True).astype(jnp.float32)
        * loss_weight[:, None]
    ).astype(jnp.bfloat16)
    pair_all = exchange_gather(jnp.concatenate([key_rows, value_rows], axis=1), "ctx")
    kv_width = key_rows.shape[1]
    keys_all, values_all = (pair_all[:, :kv_width], pair_all[:, kv_width:])
    tokens = keys_all.shape[0]
    block_rows = math.gcd(512, tokens)

    def fetch(table, block_number):
        return lax.dynamic_slice_in_dim(table, block_number * block_rows, block_rows, 0)

    def column_pos(block_number):
        return block_number * block_rows + jnp.arange(block_rows, dtype=jnp.int32)

    buffer = jnp.zeros((tokens, 2 * local_groups * head_dim), jnp.float32)
    rows = query_rows.shape[0]
    row_pos = first_row + jnp.arange(rows, dtype=jnp.int32)
    needed = (first_row + rows - 1) // block_rows + 1
    query_heads = query_rows.reshape(rows, local_groups, group_size, head_dim)
    log_totals = []
    shared_head = 0
    query_group = query_heads[:, shared_head]

    def stats_step(block_number, carried):
        running_max, running_sum = carried
        key_block = fetch(keys_all, block_number)
        scores = block_scores(query_group, key_block, scaling, row_pos, column_pos(block_number))
        new_max = jnp.maximum(running_max, jnp.max(scores, axis=-1))
        running_sum = running_sum * jnp.exp(running_max - new_max) + jnp.sum(
            jnp.exp(scores - new_max[..., None]), axis=-1
        )
        return (new_max, running_sum)

    start_max = jnp.full((rows, group_size), NEGATIVE, jnp.float32)
    start_sum = jnp.zeros((rows, group_size), jnp.float32)
    running_max, running_sum = lax.fori_loop(0, needed, stats_step, (start_max, start_sum))
    log_total = running_max + jnp.log(running_sum)

    def value_step(block_number, accumulated):
        key_block = fetch(keys_all, block_number)
        value_block = fetch(values_all, block_number)
        scores = block_scores(query_group, key_block, scaling, row_pos, column_pos(block_number))
        rounded = jnp.exp(scores - log_total[..., None]).astype(jnp.bfloat16)
        return accumulated + jnp.einsum(
            "tgk,kd->tgd", rounded, value_block, preferred_element_type=jnp.float32
        )

    accumulated = lax.fori_loop(
        0, needed, value_step, jnp.zeros((rows, group_size, head_dim), jnp.float32)
    )
    log_totals.append(log_total)
    attended_list = [accumulated.astype(jnp.bfloat16)]
    attended_part = jnp.stack(attended_list, axis=1).reshape(
        rows, local_groups * group_size * head_dim
    )
    log_totals, attended = (log_totals, attended_part)
    grad_sum = lax.dot_general(
        piece_part, out_weight, (((1,), (1,)), ((), ())), preferred_element_type=jnp.float32
    )
    grad_sum, squares_out = (grad_sum, gram_squares(piece_part, attended, head_dim))
    grad_attended, squares_out = (grad_sum.astype(jnp.bfloat16), squares_out)
    backward_buffer = buffer
    rows = query_rows.shape[0]
    backward_row_pos = first_row + jnp.arange(rows, dtype=jnp.int32)
    needed = (first_row + rows - 1) // block_rows + 1
    query_heads = query_rows.reshape(rows, local_groups, group_size, head_dim)
    grad_heads = grad_attended.reshape(rows, local_groups, group_size, head_dim)
    attended_heads = attended.reshape(rows, local_groups, group_size, head_dim)
    shared_head = 0
    backward_query_group = query_heads[:, shared_head]
    grad_group = grad_heads[:, shared_head]
    backward_log_total = log_totals[shared_head]
    row_dot = jnp.sum(
        grad_group.astype(jnp.float32) * attended_heads[:, shared_head].astype(jnp.float32), axis=-1
    )
    grad_query_part, backward_buffer = flash_backward(
        backward_query_group.reshape(rows, group_size * head_dim),
        grad_group.reshape(rows, group_size * head_dim),
        keys_all,
        values_all,
        backward_log_total,
        row_dot,
        first_row,
        head_dim,
        block_rows,
    )
    ctx_size = lax.axis_size("ctx")
    key_sums = exchange_reduce(
        backward_buffer.reshape((ctx_size, tokens // ctx_size) + backward_buffer.shape[1:]), "ctx"
    )
    grad_key = key_sums[:, : local_groups * head_dim].astype(jnp.bfloat16)
    grad_value = key_sums[:, local_groups * head_dim :].astype(jnp.bfloat16)
    squares_query = gram_pair_squares(hidden_gram, grad_query_part, head_dim)
    normal_size = D * head_dim * tok_dev
    fisher_q = jnp.log(squares_query / normal_size + EPSILON).reshape(1, -1)
    fisher_o = jnp.log(squares_out / normal_size + EPSILON).reshape(1, -1)
    return (grad_query_part, grad_key, grad_value, fisher_q, fisher_o)


def solution(mesh):
    return jax.shard_map(
        body,
        mesh=mesh,
        in_specs=(
            P("ctx", "head"),
            P("ctx", "head"),
            P("ctx", "head"),
            P("ctx", "head"),
            P("head", None),
            P("ctx", "head"),
            P("ctx"),
        ),
        out_specs=(
            P("ctx", "head"),
            P("ctx", "head"),
            P("ctx", "head"),
            P("ctx", "head"),
            P("ctx", "head"),
        ),
        check_vma=False,
    )
```

```python
import math

import jax
import jax.numpy as jnp
from jax import lax
from jax.experimental import pallas as pl
from jax.experimental.pallas import tpu as pltpu
from jax.sharding import PartitionSpec as P

D = 8192
HEADS = 64
KVH = 8
HD = 128


NEGATIVE = -1e30
EPSILON = 1e-06


def block_scores(query_group, key_block, scaling, row_pos, col_pos):
    scores = (
        jnp.einsum("tgd,kd->tgk", query_group, key_block, preferred_element_type=jnp.float32)
        * scaling
    )
    return jnp.where(row_pos[:, None, None] >= col_pos[None, None, :], scores, NEGATIVE)


def head_squares(left_side, right_side, head_dim):
    product = lax.dot_general(
        left_side, right_side, (((0,), (0,)), ((), ())), preferred_element_type=jnp.float32
    )
    shaped = (product * product).reshape(
        product.shape[0], right_side.shape[1] // head_dim, head_dim
    )
    return jnp.sum(shaped, axis=(0, 2))


def flash_backward(query_rows, grad_attended, keys_all, values_all, log_total, row_dot, first_row, head_dim, block_rows):
    rows, width = query_rows.shape
    heads = width // head_dim
    tokens = keys_all.shape[0]
    blocks = tokens // block_rows
    scaling = head_dim ** (-0.5)
    needed = (first_row + rows - 1) // block_rows + 1
    scalars = jnp.stack([needed, first_row]).astype(jnp.int32)

    def kernel(scalar_ref, q_ref, do_ref, k_ref, v_ref, lt_ref, rd_ref, dq_ref, dkv_ref, dq_acc):
        j = pl.program_id(0)

        @pl.when(j == 0)
        def _():
            dq_acc[...] = jnp.zeros_like(dq_acc)

        @pl.when(j < scalar_ref[0])
        def _():
            k = k_ref[...]
            v = v_ref[...]
            row_pos = scalar_ref[1] + lax.broadcasted_iota(jnp.int32, (rows, block_rows), 0)
            col_pos = j * block_rows + lax.broadcasted_iota(jnp.int32, (rows, block_rows), 1)
            keep = row_pos >= col_pos
            dk = jnp.zeros((block_rows, head_dim), jnp.float32)
            dv = jnp.zeros((block_rows, head_dim), jnp.float32)
            for h in range(heads):
                cols = slice(h * head_dim, (h + 1) * head_dim)
                q = q_ref[:, cols]
                do = do_ref[:, cols]
                s = lax.dot_general(q, k, (((1,), (1,)), ((), ())), preferred_element_type=jnp.float32) * scaling
                s = jnp.where(keep, s, NEGATIVE)
                p = jnp.exp(s - lt_ref[:, h : h + 1])
                dp = lax.dot_general(do, v, (((1,), (1,)), ((), ())), preferred_element_type=jnp.float32)
                ds = (p * (dp - rd_ref[:, h : h + 1])).astype(jnp.bfloat16)
                dq_acc[:, cols] += jnp.dot(ds, k, preferred_element_type=jnp.float32)
                dk += lax.dot_general(ds, q, (((0,), (0,)), ((), ())), preferred_element_type=jnp.float32)
                dv += lax.dot_general(p.astype(jnp.bfloat16), do, (((0,), (0,)), ((), ())), preferred_element_type=jnp.float32)
            dkv_ref[:, :head_dim] = (dk * scaling).astype(dkv_ref.dtype)
            dkv_ref[:, head_dim:] = dv.astype(dkv_ref.dtype)

        @pl.when(j >= scalar_ref[0])
        def _():
            dkv_ref[...] = jnp.zeros_like(dkv_ref)

        @pl.when(j == blocks - 1)
        def _():
            dq_ref[...] = (dq_acc[...] * scaling).astype(dq_ref.dtype)

    def kv_map(j, s):
        return (jnp.minimum(j, s[0] - 1), 0)

    full = lambda j, s: (0, 0)
    grid_spec = pltpu.PrefetchScalarGridSpec(
        num_scalar_prefetch=1,
        grid=(blocks,),
        in_specs=[
            pl.BlockSpec((rows, width), full),
            pl.BlockSpec((rows, width), full),
            pl.BlockSpec((block_rows, head_dim), kv_map),
            pl.BlockSpec((block_rows, head_dim), kv_map),
            pl.BlockSpec((rows, heads), full),
            pl.BlockSpec((rows, heads), full),
        ],
        out_specs=[
            pl.BlockSpec((rows, width), full),
            pl.BlockSpec((block_rows, 2 * head_dim), lambda j, s: (j, 0)),
        ],
        scratch_shapes=[pltpu.VMEM((rows, width), jnp.float32)],
    )
    return pl.pallas_call(
        kernel,
        grid_spec=grid_spec,
        out_shape=[
            jax.ShapeDtypeStruct((rows, width), jnp.bfloat16),
            jax.ShapeDtypeStruct((tokens, 2 * head_dim), jnp.bfloat16),
        ],
        compiler_params=pltpu.CompilerParams(dimension_semantics=("arbitrary",)),
    )(scalars, query_rows, grad_attended, keys_all, values_all, log_total, row_dot)


def butterfly_gather(value, axis_name):
    size = lax.axis_size(axis_name)
    own = lax.axis_index(axis_name)
    held = value[None]
    stride = size // 2
    bits = 0
    while stride >= 1:
        pairs = [(i, i ^ stride) for i in range(size)]
        other = lax.ppermute(held, axis_name, pairs)
        low = (own & stride) == 0
        held = jnp.where(
            low, jnp.concatenate([held, other], 0), jnp.concatenate([other, held], 0)
        )
        stride //= 2
        bits += 1
    held = held.reshape((2,) * bits + value.shape)
    held = held.transpose(tuple(range(bits))[::-1] + tuple(range(bits, bits + value.ndim)))
    return held.reshape((size * value.shape[0],) + value.shape[1:])


def causal_gather(value, axis_name):
    size = lax.axis_size(axis_name)
    own = lax.axis_index(axis_name)
    received = [value]
    for shift in range(1, size):
        pairs = [(i, i + shift) for i in range(size - shift)]
        received.append(lax.ppermute(value, axis_name, pairs))
    by_shift = jnp.stack(received[::-1], 0)
    doubled = jnp.concatenate([by_shift, by_shift], 0)
    blocks = lax.dynamic_slice_in_dim(doubled, size - 1 - own, size, 0)
    return blocks.reshape((size * value.shape[0],) + value.shape[1:])


def causal_reduce(parts, axis_name):
    size = lax.axis_size(axis_name)
    own = lax.axis_index(axis_name)
    total = lax.dynamic_index_in_dim(parts, own, 0, keepdims=False).astype(jnp.float32)
    for shift in range(1, size):
        pairs = [(i, i - shift) for i in range(shift, size)]
        sent = lax.dynamic_index_in_dim(parts, jnp.maximum(own - shift, 0), 0, keepdims=False)
        total = total + lax.ppermute(sent, axis_name, pairs).astype(jnp.float32)
    return total


def exchange_gather(value, axis_name):
    size = lax.axis_size(axis_name)
    copies = jnp.broadcast_to(value[None], (size,) + value.shape)
    arrived = lax.all_to_all(copies, axis_name, 0, 0, tiled=True)
    return arrived.reshape((size * value.shape[0],) + value.shape[1:])


def exchange_reduce(parts, axis_name):
    arrived = lax.all_to_all(parts, axis_name, 0, 0, tiled=True)
    return jnp.sum(arrived.astype(jnp.float32), axis=0)


def butterfly_sum(value, axis_name):
    size = lax.axis_size(axis_name)
    stride = 1
    while stride < size:
        pairs = [(i, i ^ stride) for i in range(size)]
        value = value + lax.ppermute(value, axis_name, pairs)
        stride *= 2
    return value


def gram_pair_squares(left_gram, right_side, head_dim):
    rows = right_side.shape[0]
    right_heads = right_side.reshape(rows, right_side.shape[1] // head_dim, head_dim)
    right_gram = jnp.einsum(
        "ihd,jhd->hij", right_heads, right_heads, preferred_element_type=jnp.float32
    )
    return jnp.sum(right_gram * left_gram[None], axis=(1, 2))


def gram_squares(left_side, right_side, head_dim):
    left_gram = lax.dot_general(
        left_side, left_side, (((1,), (1,)), ((), ())), preferred_element_type=jnp.float32
    )
    return gram_pair_squares(left_gram, right_side, head_dim)


def body(hidden_in, query_rows, key_rows, value_rows, out_weight, grad_out, answer_mask):
    tok_dev = query_rows.shape[0]
    head_dim = HD
    group_size = HEADS // KVH
    local_groups = key_rows.shape[1] // head_dim
    scaling = head_dim ** (-0.5)
    own_index = lax.axis_index("ctx")
    first_row = own_index * tok_dev
    loss_weight = 0.25 + answer_mask.astype(jnp.float32)
    weighted = (grad_out.astype(jnp.float32) * loss_weight[:, None]).astype(jnp.bfloat16)
    gram_part = lax.dot_general(
        hidden_in, hidden_in, (((1,), (1,)), ((), ())), preferred_element_type=jnp.float32
    )
    piece_part = (
        lax.all_gather(grad_out, "head", axis=1, tiled=True).astype(jnp.float32)
        * loss_weight[:, None]
    ).astype(jnp.bfloat16)
    pair_all = exchange_gather(jnp.concatenate([key_rows, value_rows], axis=1), "ctx")
    gram_part, pair_all = lax.optimization_barrier((gram_part, pair_all))
    hidden_gram = butterfly_sum(gram_part, "head")
    kv_width = key_rows.shape[1]
    keys_all, values_all = (pair_all[:, :kv_width], pair_all[:, kv_width:])
    tokens = keys_all.shape[0]
    block_rows = math.gcd(512, tokens)

    def fetch(table, block_number):
        return lax.dynamic_slice_in_dim(table, block_number * block_rows, block_rows, 0)

    def column_pos(block_number):
        return block_number * block_rows + jnp.arange(block_rows, dtype=jnp.int32)

    buffer = jnp.zeros((tokens, 2 * local_groups * head_dim), jnp.float32)
    rows = query_rows.shape[0]
    row_pos = first_row + jnp.arange(rows, dtype=jnp.int32)
    needed = (first_row + rows - 1) // block_rows + 1
    query_heads = query_rows.reshape(rows, local_groups, group_size, head_dim)
    log_totals = []
    shared_head = 0
    query_group = query_heads[:, shared_head]

    def stats_step(block_number, carried):
        running_max, running_sum = carried
        key_block = fetch(keys_all, block_number)
        scores = block_scores(query_group, key_block, scaling, row_pos, column_pos(block_number))
        new_max = jnp.maximum(running_max, jnp.max(scores, axis=-1))
        running_sum = running_sum * jnp.exp(running_max - new_max) + jnp.sum(
            jnp.exp(scores - new_max[..., None]), axis=-1
        )
        return (new_max, running_sum)

    start_max = jnp.full((rows, group_size), NEGATIVE, jnp.float32)
    start_sum = jnp.zeros((rows, group_size), jnp.float32)
    running_max, running_sum = lax.fori_loop(0, needed, stats_step, (start_max, start_sum))
    log_total = running_max + jnp.log(running_sum)

    def value_step(block_number, accumulated):
        key_block = fetch(keys_all, block_number)
        value_block = fetch(values_all, block_number)
        scores = block_scores(query_group, key_block, scaling, row_pos, column_pos(block_number))
        rounded = jnp.exp(scores - log_total[..., None]).astype(jnp.bfloat16)
        return accumulated + jnp.einsum(
            "tgk,kd->tgd", rounded, value_block, preferred_element_type=jnp.float32
        )

    accumulated = lax.fori_loop(
        0, needed, value_step, jnp.zeros((rows, group_size, head_dim), jnp.float32)
    )
    log_totals.append(log_total)
    attended_list = [accumulated.astype(jnp.bfloat16)]
    attended_part = jnp.stack(attended_list, axis=1).reshape(
        rows, local_groups * group_size * head_dim
    )
    log_totals, attended = (log_totals, attended_part)
    grad_sum = lax.dot_general(
        piece_part, out_weight, (((1,), (1,)), ((), ())), preferred_element_type=jnp.float32
    )
    grad_sum, squares_out = (grad_sum, gram_squares(piece_part, attended, head_dim))
    grad_attended, squares_out = (grad_sum.astype(jnp.bfloat16), squares_out)
    hidden_gram, squares_out, grad_attended = lax.optimization_barrier(
        (hidden_gram, squares_out, grad_attended)
    )
    backward_buffer = buffer
    rows = query_rows.shape[0]
    backward_row_pos = first_row + jnp.arange(rows, dtype=jnp.int32)
    needed = (first_row + rows - 1) // block_rows + 1
    query_heads = query_rows.reshape(rows, local_groups, group_size, head_dim)
    grad_heads = grad_attended.reshape(rows, local_groups, group_size, head_dim)
    attended_heads = attended.reshape(rows, local_groups, group_size, head_dim)
    shared_head = 0
    backward_query_group = query_heads[:, shared_head]
    grad_group = grad_heads[:, shared_head]
    backward_log_total = log_totals[shared_head]
    row_dot = jnp.sum(
        grad_group.astype(jnp.float32) * attended_heads[:, shared_head].astype(jnp.float32), axis=-1
    )
    grad_query_part, backward_buffer = flash_backward(
        backward_query_group.reshape(rows, group_size * head_dim),
        grad_group.reshape(rows, group_size * head_dim),
        keys_all,
        values_all,
        backward_log_total,
        row_dot,
        first_row,
        head_dim,
        block_rows,
    )
    ctx_size = lax.axis_size("ctx")
    key_sums = exchange_reduce(
        backward_buffer.reshape((ctx_size, tokens // ctx_size) + backward_buffer.shape[1:]), "ctx"
    )
    grad_key = key_sums[:, : local_groups * head_dim].astype(jnp.bfloat16)
    grad_value = key_sums[:, local_groups * head_dim :].astype(jnp.bfloat16)
    squares_query = gram_pair_squares(hidden_gram, grad_query_part, head_dim)
    normal_size = D * head_dim * tok_dev
    fisher_q = jnp.log(squares_query / normal_size + EPSILON).reshape(1, -1)
    fisher_o = jnp.log(squares_out / normal_size + EPSILON).reshape(1, -1)
    return (grad_query_part, grad_key, grad_value, fisher_q, fisher_o)


def solution(mesh):
    return jax.shard_map(
        body,
        mesh=mesh,
        in_specs=(
            P("ctx", "head"),
            P("ctx", "head"),
            P("ctx", "head"),
            P("ctx", "head"),
            P("head", None),
            P("ctx", "head"),
            P("ctx"),
        ),
        out_specs=(
            P("ctx", "head"),
            P("ctx", "head"),
            P("ctx", "head"),
            P("ctx", "head"),
            P("ctx", "head"),
        ),
        check_vma=False,
    )
```

```python
import math

import jax
import jax.numpy as jnp
from jax import lax
from jax.experimental import pallas as pl
from jax.experimental.pallas import tpu as pltpu
from jax.sharding import PartitionSpec as P

D = 8192
HEADS = 64
KVH = 8
HD = 128


NEGATIVE = -1e30
EPSILON = 1e-06


def block_scores(query_group, key_block, scaling, row_pos, col_pos):
    scores = (
        jnp.einsum("tgd,kd->tgk", query_group, key_block, preferred_element_type=jnp.float32)
        * scaling
    )
    return jnp.where(row_pos[:, None, None] >= col_pos[None, None, :], scores, NEGATIVE)


def head_squares(left_side, right_side, head_dim):
    product = lax.dot_general(
        left_side, right_side, (((0,), (0,)), ((), ())), preferred_element_type=jnp.float32
    )
    shaped = (product * product).reshape(
        product.shape[0], right_side.shape[1] // head_dim, head_dim
    )
    return jnp.sum(shaped, axis=(0, 2))


def flash_backward(query_rows, grad_attended, keys_all, values_all, log_total, row_dot, first_row, head_dim, block_rows):
    rows, width = query_rows.shape
    heads = width // head_dim
    tokens = keys_all.shape[0]
    blocks = tokens // block_rows
    scaling = head_dim ** (-0.5)
    needed = (first_row + rows - 1) // block_rows + 1
    scalars = jnp.stack([needed, first_row]).astype(jnp.int32)

    def kernel(scalar_ref, q_ref, do_ref, k_ref, v_ref, lt_ref, rd_ref, dq_ref, dkv_ref, dq_acc):
        j = pl.program_id(0)

        @pl.when(j == 0)
        def _():
            dq_acc[...] = jnp.zeros_like(dq_acc)

        def block(masked):
            k = k_ref[...]
            v = v_ref[...]
            k_turned = k.T
            col_pos = j * block_rows + lax.broadcasted_iota(jnp.int32, (block_rows, rows), 0)
            row_pos = scalar_ref[1] + lax.broadcasted_iota(jnp.int32, (block_rows, rows), 1)
            keep = row_pos >= col_pos
            dk = jnp.zeros((block_rows, head_dim), jnp.float32)
            dv = jnp.zeros((block_rows, head_dim), jnp.float32)
            for h in range(heads):
                cols = slice(h * head_dim, (h + 1) * head_dim)
                q = q_ref[:, cols]
                do = do_ref[:, cols]
                s = lax.dot_general(k, q, (((1,), (1,)), ((), ())), preferred_element_type=jnp.float32) * scaling
                if masked:
                    s = jnp.where(keep, s, NEGATIVE)
                p = jnp.exp(s - lt_ref[h : h + 1, :])
                dp = lax.dot_general(v, do, (((1,), (1,)), ((), ())), preferred_element_type=jnp.float32)
                ds = (p * (dp - rd_ref[h : h + 1, :])).astype(jnp.bfloat16)
                dq_acc[cols, :] += jnp.dot(k_turned, ds, preferred_element_type=jnp.float32)
                dk += jnp.dot(ds, q, preferred_element_type=jnp.float32)
                dv += jnp.dot(p.astype(jnp.bfloat16), do, preferred_element_type=jnp.float32)
            dkv_ref[:, :head_dim] = (dk * scaling).astype(dkv_ref.dtype)
            dkv_ref[:, head_dim:] = dv.astype(dkv_ref.dtype)

        below = j * block_rows + block_rows - 1 <= scalar_ref[1]

        @pl.when(jnp.logical_and(j < scalar_ref[0], below))
        def _():
            block(False)

        @pl.when(jnp.logical_and(j < scalar_ref[0], jnp.logical_not(below)))
        def _():
            block(True)

        @pl.when(j >= scalar_ref[0])
        def _():
            dkv_ref[...] = jnp.zeros_like(dkv_ref)

        @pl.when(j == blocks - 1)
        def _():
            dq_ref[...] = (dq_acc[...].T * scaling).astype(dq_ref.dtype)

    def kv_map(j, s):
        return (jnp.minimum(j, s[0] - 1), 0)

    full = lambda j, s: (0, 0)
    grid_spec = pltpu.PrefetchScalarGridSpec(
        num_scalar_prefetch=1,
        grid=(blocks,),
        in_specs=[
            pl.BlockSpec((rows, width), full),
            pl.BlockSpec((rows, width), full),
            pl.BlockSpec((block_rows, head_dim), kv_map),
            pl.BlockSpec((block_rows, head_dim), kv_map),
            pl.BlockSpec((heads, rows), full),
            pl.BlockSpec((heads, rows), full),
        ],
        out_specs=[
            pl.BlockSpec((rows, width), full),
            pl.BlockSpec((block_rows, 2 * head_dim), lambda j, s: (j, 0)),
        ],
        scratch_shapes=[pltpu.VMEM((width, rows), jnp.float32)],
    )
    return pl.pallas_call(
        kernel,
        grid_spec=grid_spec,
        out_shape=[
            jax.ShapeDtypeStruct((rows, width), jnp.bfloat16),
            jax.ShapeDtypeStruct((tokens, 2 * head_dim), jnp.bfloat16),
        ],
        compiler_params=pltpu.CompilerParams(dimension_semantics=("arbitrary",)),
    )(scalars, query_rows, grad_attended, keys_all, values_all, log_total.T, row_dot.T)


def butterfly_gather(value, axis_name):
    size = lax.axis_size(axis_name)
    own = lax.axis_index(axis_name)
    held = value[None]
    stride = size // 2
    bits = 0
    while stride >= 1:
        pairs = [(i, i ^ stride) for i in range(size)]
        other = lax.ppermute(held, axis_name, pairs)
        low = (own & stride) == 0
        held = jnp.where(
            low, jnp.concatenate([held, other], 0), jnp.concatenate([other, held], 0)
        )
        stride //= 2
        bits += 1
    held = held.reshape((2,) * bits + value.shape)
    held = held.transpose(tuple(range(bits))[::-1] + tuple(range(bits, bits + value.ndim)))
    return held.reshape((size * value.shape[0],) + value.shape[1:])


def causal_gather(value, axis_name):
    size = lax.axis_size(axis_name)
    own = lax.axis_index(axis_name)
    received = [value]
    for shift in range(1, size):
        pairs = [(i, i + shift) for i in range(size - shift)]
        received.append(lax.ppermute(value, axis_name, pairs))
    by_shift = jnp.stack(received[::-1], 0)
    doubled = jnp.concatenate([by_shift, by_shift], 0)
    blocks = lax.dynamic_slice_in_dim(doubled, size - 1 - own, size, 0)
    return blocks.reshape((size * value.shape[0],) + value.shape[1:])


def causal_reduce(parts, axis_name):
    size = lax.axis_size(axis_name)
    own = lax.axis_index(axis_name)
    total = lax.dynamic_index_in_dim(parts, own, 0, keepdims=False).astype(jnp.float32)
    for shift in range(1, size):
        pairs = [(i, i - shift) for i in range(shift, size)]
        sent = lax.dynamic_index_in_dim(parts, jnp.maximum(own - shift, 0), 0, keepdims=False)
        total = total + lax.ppermute(sent, axis_name, pairs).astype(jnp.float32)
    return total


def exchange_reduce(parts, axis_name):
    arrived = lax.all_to_all(parts, axis_name, 0, 0, tiled=True)
    return jnp.sum(arrived.astype(jnp.float32), axis=0)


def butterfly_sum(value, axis_name):
    size = lax.axis_size(axis_name)
    stride = 1
    while stride < size:
        pairs = [(i, i ^ stride) for i in range(size)]
        value = value + lax.ppermute(value, axis_name, pairs)
        stride *= 2
    return value


def gram_pair_squares(left_gram, right_side, head_dim):
    rows = right_side.shape[0]
    right_heads = right_side.reshape(rows, right_side.shape[1] // head_dim, head_dim)
    right_gram = jnp.einsum(
        "ihd,jhd->hij", right_heads, right_heads, preferred_element_type=jnp.float32
    )
    return jnp.sum(right_gram * left_gram[None], axis=(1, 2))


def gram_squares(left_side, right_side, head_dim):
    left_gram = lax.dot_general(
        left_side, left_side, (((1,), (1,)), ((), ())), preferred_element_type=jnp.float32
    )
    return gram_pair_squares(left_gram, right_side, head_dim)


def body(hidden_in, query_rows, key_rows, value_rows, out_weight, grad_out, answer_mask):
    tok_dev = query_rows.shape[0]
    head_dim = HD
    group_size = HEADS // KVH
    local_groups = key_rows.shape[1] // head_dim
    scaling = head_dim ** (-0.5)
    own_index = lax.axis_index("ctx")
    first_row = own_index * tok_dev
    loss_weight = 0.25 + answer_mask.astype(jnp.float32)
    weighted = (grad_out.astype(jnp.float32) * loss_weight[:, None]).astype(jnp.bfloat16)
    hidden_gram = butterfly_sum(
        lax.dot_general(
            hidden_in, hidden_in, (((1,), (1,)), ((), ())), preferred_element_type=jnp.float32
        ),
        "head",
    )
    piece_part = (
        lax.all_gather(grad_out, "head", axis=1, tiled=True).astype(jnp.float32)
        * loss_weight[:, None]
    ).astype(jnp.bfloat16)
    pair_all = causal_gather(jnp.concatenate([key_rows, value_rows], axis=1), "ctx")
    kv_width = key_rows.shape[1]
    keys_all, values_all = (pair_all[:, :kv_width], pair_all[:, kv_width:])
    tokens = keys_all.shape[0]
    block_rows = math.gcd(512, tokens)

    def fetch(table, block_number):
        return lax.dynamic_slice_in_dim(table, block_number * block_rows, block_rows, 0)

    def column_pos(block_number):
        return block_number * block_rows + jnp.arange(block_rows, dtype=jnp.int32)

    buffer = jnp.zeros((tokens, 2 * local_groups * head_dim), jnp.float32)
    rows = query_rows.shape[0]
    row_pos = first_row + jnp.arange(rows, dtype=jnp.int32)
    needed = (first_row + rows - 1) // block_rows + 1
    query_heads = query_rows.reshape(rows, local_groups, group_size, head_dim)
    log_totals = []
    shared_head = 0
    query_group = query_heads[:, shared_head]

    def stats_step(block_number, carried):
        running_max, running_sum = carried
        key_block = fetch(keys_all, block_number)
        scores = block_scores(query_group, key_block, scaling, row_pos, column_pos(block_number))
        new_max = jnp.maximum(running_max, jnp.max(scores, axis=-1))
        running_sum = running_sum * jnp.exp(running_max - new_max) + jnp.sum(
            jnp.exp(scores - new_max[..., None]), axis=-1
        )
        return (new_max, running_sum)

    start_max = jnp.full((rows, group_size), NEGATIVE, jnp.float32)
    start_sum = jnp.zeros((rows, group_size), jnp.float32)
    running_max, running_sum = lax.fori_loop(0, needed, stats_step, (start_max, start_sum))
    log_total = running_max + jnp.log(running_sum)

    def value_step(block_number, accumulated):
        key_block = fetch(keys_all, block_number)
        value_block = fetch(values_all, block_number)
        scores = block_scores(query_group, key_block, scaling, row_pos, column_pos(block_number))
        rounded = jnp.exp(scores - log_total[..., None]).astype(jnp.bfloat16)
        return accumulated + jnp.einsum(
            "tgk,kd->tgd", rounded, value_block, preferred_element_type=jnp.float32
        )

    accumulated = lax.fori_loop(
        0, needed, value_step, jnp.zeros((rows, group_size, head_dim), jnp.float32)
    )
    log_totals.append(log_total)
    attended_list = [accumulated.astype(jnp.bfloat16)]
    attended_part = jnp.stack(attended_list, axis=1).reshape(
        rows, local_groups * group_size * head_dim
    )
    log_totals, attended = (log_totals, attended_part)
    grad_sum = lax.dot_general(
        piece_part, out_weight, (((1,), (1,)), ((), ())), preferred_element_type=jnp.float32
    )
    grad_sum, squares_out = (grad_sum, gram_squares(piece_part, attended, head_dim))
    grad_attended, squares_out = (grad_sum.astype(jnp.bfloat16), squares_out)
    backward_buffer = buffer
    rows = query_rows.shape[0]
    backward_row_pos = first_row + jnp.arange(rows, dtype=jnp.int32)
    needed = (first_row + rows - 1) // block_rows + 1
    query_heads = query_rows.reshape(rows, local_groups, group_size, head_dim)
    grad_heads = grad_attended.reshape(rows, local_groups, group_size, head_dim)
    attended_heads = attended.reshape(rows, local_groups, group_size, head_dim)
    shared_head = 0
    backward_query_group = query_heads[:, shared_head]
    grad_group = grad_heads[:, shared_head]
    backward_log_total = log_totals[shared_head]
    row_dot = jnp.sum(
        grad_group.astype(jnp.float32) * attended_heads[:, shared_head].astype(jnp.float32), axis=-1
    )
    grad_query_part, backward_buffer = flash_backward(
        backward_query_group.reshape(rows, group_size * head_dim),
        grad_group.reshape(rows, group_size * head_dim),
        keys_all,
        values_all,
        backward_log_total,
        row_dot,
        first_row,
        head_dim,
        block_rows,
    )
    ctx_size = lax.axis_size("ctx")
    key_sums = exchange_reduce(
        backward_buffer.reshape((ctx_size, tokens // ctx_size) + backward_buffer.shape[1:]), "ctx"
    )
    grad_key = key_sums[:, : local_groups * head_dim].astype(jnp.bfloat16)
    grad_value = key_sums[:, local_groups * head_dim :].astype(jnp.bfloat16)
    squares_query = gram_pair_squares(hidden_gram, grad_query_part, head_dim)
    normal_size = D * head_dim * tok_dev
    fisher_q = jnp.log(squares_query / normal_size + EPSILON).reshape(1, -1)
    fisher_o = jnp.log(squares_out / normal_size + EPSILON).reshape(1, -1)
    return (grad_query_part, grad_key, grad_value, fisher_q, fisher_o)


def solution(mesh):
    return jax.shard_map(
        body,
        mesh=mesh,
        in_specs=(
            P("ctx", "head"),
            P("ctx", "head"),
            P("ctx", "head"),
            P("ctx", "head"),
            P("head", None),
            P("ctx", "head"),
            P("ctx"),
        ),
        out_specs=(
            P("ctx", "head"),
            P("ctx", "head"),
            P("ctx", "head"),
            P("ctx", "head"),
            P("ctx", "head"),
        ),
        check_vma=False,
    )
```

```python
import math

import jax
import jax.numpy as jnp
from jax import lax
from jax.experimental import pallas as pl
from jax.experimental.pallas import tpu as pltpu
from jax.sharding import PartitionSpec as P

D = 8192
HEADS = 64
KVH = 8
HD = 128


NEGATIVE = -1e30
EPSILON = 1e-06


def block_scores(query_group, key_block, scaling, row_pos, col_pos):
    scores = (
        jnp.einsum("tgd,kd->tgk", query_group, key_block, preferred_element_type=jnp.float32)
        * scaling
    )
    return jnp.where(row_pos[:, None, None] >= col_pos[None, None, :], scores, NEGATIVE)


def head_squares(left_side, right_side, head_dim):
    product = lax.dot_general(
        left_side, right_side, (((0,), (0,)), ((), ())), preferred_element_type=jnp.float32
    )
    shaped = (product * product).reshape(
        product.shape[0], right_side.shape[1] // head_dim, head_dim
    )
    return jnp.sum(shaped, axis=(0, 2))


def flash_backward(query_rows, grad_attended, keys_all, values_all, log_total, row_dot, first_row, head_dim, block_rows):
    rows, width = query_rows.shape
    heads = width // head_dim
    tokens = keys_all.shape[0]
    blocks = tokens // block_rows
    scaling = head_dim ** (-0.5)
    needed = (first_row + rows - 1) // block_rows + 1
    scalars = jnp.stack([needed, first_row]).astype(jnp.int32)

    def kernel(scalar_ref, q_ref, do_ref, k_ref, v_ref, lt_ref, rd_ref, dq_ref, dkv_ref, dq_acc):
        j = pl.program_id(0)

        @pl.when(j == 0)
        def _():
            dq_acc[...] = jnp.zeros_like(dq_acc)

        def block(masked):
            k = k_ref[...]
            v = v_ref[...]
            k_turned = k.T
            col_pos = j * block_rows + lax.broadcasted_iota(jnp.int32, (block_rows, rows), 0)
            row_pos = scalar_ref[1] + lax.broadcasted_iota(jnp.int32, (block_rows, rows), 1)
            keep = row_pos >= col_pos
            dk = jnp.zeros((block_rows, head_dim), jnp.float32)
            dv = jnp.zeros((block_rows, head_dim), jnp.float32)
            for h in range(heads):
                cols = slice(h * head_dim, (h + 1) * head_dim)
                q = q_ref[:, cols]
                do = do_ref[:, cols]
                s = lax.dot_general(k, q, (((1,), (1,)), ((), ())), preferred_element_type=jnp.float32) * scaling
                if masked:
                    s = jnp.where(keep, s, NEGATIVE)
                p = jnp.exp(s - lt_ref[h : h + 1, :])
                dp = lax.dot_general(v, do, (((1,), (1,)), ((), ())), preferred_element_type=jnp.float32)
                ds = (p * (dp - rd_ref[h : h + 1, :])).astype(jnp.bfloat16)
                dq_acc[cols, :] += jnp.dot(k_turned, ds, preferred_element_type=jnp.float32)
                dk += jnp.dot(ds, q, preferred_element_type=jnp.float32)
                dv += jnp.dot(p.astype(jnp.bfloat16), do, preferred_element_type=jnp.float32)
            dkv_ref[:, :head_dim] = (dk * scaling).astype(dkv_ref.dtype)
            dkv_ref[:, head_dim:] = dv.astype(dkv_ref.dtype)

        below = j * block_rows + block_rows - 1 <= scalar_ref[1]

        @pl.when(jnp.logical_and(j < scalar_ref[0], below))
        def _():
            block(False)

        @pl.when(jnp.logical_and(j < scalar_ref[0], jnp.logical_not(below)))
        def _():
            block(True)

        @pl.when(j >= scalar_ref[0])
        def _():
            dkv_ref[...] = jnp.zeros_like(dkv_ref)

        @pl.when(j == blocks - 1)
        def _():
            dq_ref[...] = (dq_acc[...].T * scaling).astype(dq_ref.dtype)

    def kv_map(j, s):
        return (jnp.minimum(j, s[0] - 1), 0)

    full = lambda j, s: (0, 0)
    grid_spec = pltpu.PrefetchScalarGridSpec(
        num_scalar_prefetch=1,
        grid=(blocks,),
        in_specs=[
            pl.BlockSpec((rows, width), full),
            pl.BlockSpec((rows, width), full),
            pl.BlockSpec((block_rows, head_dim), kv_map),
            pl.BlockSpec((block_rows, head_dim), kv_map),
            pl.BlockSpec((heads, rows), full),
            pl.BlockSpec((heads, rows), full),
        ],
        out_specs=[
            pl.BlockSpec((rows, width), full),
            pl.BlockSpec((block_rows, 2 * head_dim), lambda j, s: (j, 0)),
        ],
        scratch_shapes=[pltpu.VMEM((width, rows), jnp.float32)],
    )
    return pl.pallas_call(
        kernel,
        grid_spec=grid_spec,
        out_shape=[
            jax.ShapeDtypeStruct((rows, width), jnp.bfloat16),
            jax.ShapeDtypeStruct((tokens, 2 * head_dim), jnp.bfloat16),
        ],
        compiler_params=pltpu.CompilerParams(dimension_semantics=("arbitrary",)),
    )(scalars, query_rows, grad_attended, keys_all, values_all, log_total.T, row_dot.T)


def weighted_matmul(gathered, loss_weight, out_weight, tile=256, chunk=1024):
    rows, depth = gathered.shape
    width = out_weight.shape[0]

    def kernel(x_ref, lw_ref, w_ref, o_ref, xw):
        @pl.when(pl.program_id(0) == 0)
        def _():
            for c in range(depth // chunk):
                part = slice(c * chunk, (c + 1) * chunk)
                xw[:, part] = (x_ref[:, part].astype(jnp.float32) * lw_ref[...]).astype(xw.dtype)

        o_ref[...] = lax.dot_general(
            xw[...], w_ref[...], (((1,), (1,)), ((), ())), preferred_element_type=jnp.float32
        ).astype(o_ref.dtype)

    return pl.pallas_call(
        kernel,
        grid=(width // tile,),
        in_specs=[
            pl.BlockSpec((rows, depth), lambda n: (0, 0)),
            pl.BlockSpec((rows, 1), lambda n: (0, 0)),
            pl.BlockSpec((tile, depth), lambda n: (n, 0)),
        ],
        out_specs=pl.BlockSpec((rows, tile), lambda n: (0, n)),
        out_shape=jax.ShapeDtypeStruct((rows, width), jnp.bfloat16),
        scratch_shapes=[pltpu.VMEM((rows, depth), jnp.bfloat16)],
        compiler_params=pltpu.CompilerParams(dimension_semantics=("arbitrary",)),
    )(gathered, loss_weight[:, None], out_weight)


def butterfly_gather(value, axis_name):
    size = lax.axis_size(axis_name)
    own = lax.axis_index(axis_name)
    held = value[None]
    stride = size // 2
    bits = 0
    while stride >= 1:
        pairs = [(i, i ^ stride) for i in range(size)]
        other = lax.ppermute(held, axis_name, pairs)
        low = (own & stride) == 0
        held = jnp.where(
            low, jnp.concatenate([held, other], 0), jnp.concatenate([other, held], 0)
        )
        stride //= 2
        bits += 1
    held = held.reshape((2,) * bits + value.shape)
    held = held.transpose(tuple(range(bits))[::-1] + tuple(range(bits, bits + value.ndim)))
    return held.reshape((size * value.shape[0],) + value.shape[1:])


def causal_gather(value, axis_name):
    size = lax.axis_size(axis_name)
    own = lax.axis_index(axis_name)
    received = [value]
    for shift in range(1, size):
        pairs = [(i, i + shift) for i in range(size - shift)]
        received.append(lax.ppermute(value, axis_name, pairs))
    by_shift = jnp.stack(received[::-1], 0)
    doubled = jnp.concatenate([by_shift, by_shift], 0)
    blocks = lax.dynamic_slice_in_dim(doubled, size - 1 - own, size, 0)
    return blocks.reshape((size * value.shape[0],) + value.shape[1:])


def causal_reduce(parts, axis_name):
    size = lax.axis_size(axis_name)
    own = lax.axis_index(axis_name)
    total = lax.dynamic_index_in_dim(parts, own, 0, keepdims=False).astype(jnp.float32)
    for shift in range(1, size):
        pairs = [(i, i - shift) for i in range(shift, size)]
        sent = lax.dynamic_index_in_dim(parts, jnp.maximum(own - shift, 0), 0, keepdims=False)
        total = total + lax.ppermute(sent, axis_name, pairs).astype(jnp.float32)
    return total


def exchange_reduce(parts, axis_name):
    arrived = lax.all_to_all(parts, axis_name, 0, 0, tiled=True)
    return jnp.sum(arrived.astype(jnp.float32), axis=0)


def butterfly_sum(value, axis_name):
    size = lax.axis_size(axis_name)
    stride = 1
    while stride < size:
        pairs = [(i, i ^ stride) for i in range(size)]
        value = value + lax.ppermute(value, axis_name, pairs)
        stride *= 2
    return value


def gram_pair_squares(left_gram, right_side, head_dim):
    rows = right_side.shape[0]
    right_heads = right_side.reshape(rows, right_side.shape[1] // head_dim, head_dim)
    right_gram = jnp.einsum(
        "ihd,jhd->hij", right_heads, right_heads, preferred_element_type=jnp.float32
    )
    return jnp.sum(right_gram * left_gram[None], axis=(1, 2))


def gram_squares(left_side, right_side, head_dim):
    left_gram = lax.dot_general(
        left_side, left_side, (((1,), (1,)), ((), ())), preferred_element_type=jnp.float32
    )
    return gram_pair_squares(left_gram, right_side, head_dim)


def body(hidden_in, query_rows, key_rows, value_rows, out_weight, grad_out, answer_mask):
    tok_dev = query_rows.shape[0]
    head_dim = HD
    group_size = HEADS // KVH
    local_groups = key_rows.shape[1] // head_dim
    scaling = head_dim ** (-0.5)
    own_index = lax.axis_index("ctx")
    first_row = own_index * tok_dev
    loss_weight = 0.25 + answer_mask.astype(jnp.float32)
    weighted = (grad_out.astype(jnp.float32) * loss_weight[:, None]).astype(jnp.bfloat16)
    hidden_gram = butterfly_sum(
        lax.dot_general(
            hidden_in, hidden_in, (((1,), (1,)), ((), ())), preferred_element_type=jnp.float32
        ),
        "head",
    )
    gathered_out = lax.all_gather(grad_out, "head", axis=1, tiled=True)
    piece_part = (gathered_out.astype(jnp.float32) * loss_weight[:, None]).astype(jnp.bfloat16)
    pair_all = causal_gather(jnp.concatenate([key_rows, value_rows], axis=1), "ctx")
    kv_width = key_rows.shape[1]
    keys_all, values_all = (pair_all[:, :kv_width], pair_all[:, kv_width:])
    tokens = keys_all.shape[0]
    block_rows = math.gcd(512, tokens)

    def fetch(table, block_number):
        return lax.dynamic_slice_in_dim(table, block_number * block_rows, block_rows, 0)

    def column_pos(block_number):
        return block_number * block_rows + jnp.arange(block_rows, dtype=jnp.int32)

    buffer = jnp.zeros((tokens, 2 * local_groups * head_dim), jnp.float32)
    rows = query_rows.shape[0]
    row_pos = first_row + jnp.arange(rows, dtype=jnp.int32)
    needed = (first_row + rows - 1) // block_rows + 1
    query_heads = query_rows.reshape(rows, local_groups, group_size, head_dim)
    log_totals = []
    shared_head = 0
    query_group = query_heads[:, shared_head]

    def stats_step(block_number, carried):
        running_max, running_sum = carried
        key_block = fetch(keys_all, block_number)
        scores = block_scores(query_group, key_block, scaling, row_pos, column_pos(block_number))
        new_max = jnp.maximum(running_max, jnp.max(scores, axis=-1))
        running_sum = running_sum * jnp.exp(running_max - new_max) + jnp.sum(
            jnp.exp(scores - new_max[..., None]), axis=-1
        )
        return (new_max, running_sum)

    start_max = jnp.full((rows, group_size), NEGATIVE, jnp.float32)
    start_sum = jnp.zeros((rows, group_size), jnp.float32)
    running_max, running_sum = lax.fori_loop(0, needed, stats_step, (start_max, start_sum))
    log_total = running_max + jnp.log(running_sum)

    def value_step(block_number, accumulated):
        key_block = fetch(keys_all, block_number)
        value_block = fetch(values_all, block_number)
        scores = block_scores(query_group, key_block, scaling, row_pos, column_pos(block_number))
        rounded = jnp.exp(scores - log_total[..., None]).astype(jnp.bfloat16)
        return accumulated + jnp.einsum(
            "tgk,kd->tgd", rounded, value_block, preferred_element_type=jnp.float32
        )

    accumulated = lax.fori_loop(
        0, needed, value_step, jnp.zeros((rows, group_size, head_dim), jnp.float32)
    )
    log_totals.append(log_total)
    attended_list = [accumulated.astype(jnp.bfloat16)]
    attended_part = jnp.stack(attended_list, axis=1).reshape(
        rows, local_groups * group_size * head_dim
    )
    log_totals, attended = (log_totals, attended_part)
    grad_attended = weighted_matmul(gathered_out, loss_weight, out_weight)
    squares_out = gram_squares(piece_part, attended, head_dim)
    backward_buffer = buffer
    rows = query_rows.shape[0]
    backward_row_pos = first_row + jnp.arange(rows, dtype=jnp.int32)
    needed = (first_row + rows - 1) // block_rows + 1
    query_heads = query_rows.reshape(rows, local_groups, group_size, head_dim)
    grad_heads = grad_attended.reshape(rows, local_groups, group_size, head_dim)
    attended_heads = attended.reshape(rows, local_groups, group_size, head_dim)
    shared_head = 0
    backward_query_group = query_heads[:, shared_head]
    grad_group = grad_heads[:, shared_head]
    backward_log_total = log_totals[shared_head]
    row_dot = jnp.sum(
        grad_group.astype(jnp.float32) * attended_heads[:, shared_head].astype(jnp.float32), axis=-1
    )
    grad_query_part, backward_buffer = flash_backward(
        backward_query_group.reshape(rows, group_size * head_dim),
        grad_group.reshape(rows, group_size * head_dim),
        keys_all,
        values_all,
        backward_log_total,
        row_dot,
        first_row,
        head_dim,
        block_rows,
    )
    ctx_size = lax.axis_size("ctx")
    key_sums = exchange_reduce(
        backward_buffer.reshape((ctx_size, tokens // ctx_size) + backward_buffer.shape[1:]), "ctx"
    )
    grad_key = key_sums[:, : local_groups * head_dim].astype(jnp.bfloat16)
    grad_value = key_sums[:, local_groups * head_dim :].astype(jnp.bfloat16)
    squares_query = gram_pair_squares(hidden_gram, grad_query_part, head_dim)
    normal_size = D * head_dim * tok_dev
    fisher_q = jnp.log(squares_query / normal_size + EPSILON).reshape(1, -1)
    fisher_o = jnp.log(squares_out / normal_size + EPSILON).reshape(1, -1)
    return (grad_query_part, grad_key, grad_value, fisher_q, fisher_o)


def solution(mesh):
    return jax.shard_map(
        body,
        mesh=mesh,
        in_specs=(
            P("ctx", "head"),
            P("ctx", "head"),
            P("ctx", "head"),
            P("ctx", "head"),
            P("head", None),
            P("ctx", "head"),
            P("ctx"),
        ),
        out_specs=(
            P("ctx", "head"),
            P("ctx", "head"),
            P("ctx", "head"),
            P("ctx", "head"),
            P("ctx", "head"),
        ),
        check_vma=False,
    )
```

```python
import math

import jax
import jax.numpy as jnp
from jax import lax
from jax.experimental import pallas as pl
from jax.experimental.pallas import tpu as pltpu
from jax.sharding import PartitionSpec as P

D = 8192
HEADS = 64
KVH = 8
HD = 128


NEGATIVE = -1e30
EPSILON = 1e-06


def block_scores(query_group, key_block, scaling, row_pos, col_pos):
    scores = (
        jnp.einsum("tgd,kd->tgk", query_group, key_block, preferred_element_type=jnp.float32)
        * scaling
    )
    return jnp.where(row_pos[:, None, None] >= col_pos[None, None, :], scores, NEGATIVE)


def head_squares(left_side, right_side, head_dim):
    product = lax.dot_general(
        left_side, right_side, (((0,), (0,)), ((), ())), preferred_element_type=jnp.float32
    )
    shaped = (product * product).reshape(
        product.shape[0], right_side.shape[1] // head_dim, head_dim
    )
    return jnp.sum(shaped, axis=(0, 2))


def flash_backward(query_rows, grad_attended, keys_all, values_all, log_total, row_dot, first_row, head_dim, block_rows):
    rows, width = query_rows.shape
    heads = width // head_dim
    tokens = keys_all.shape[0]
    blocks = tokens // block_rows
    scaling = head_dim ** (-0.5)
    needed = (first_row + rows - 1) // block_rows + 1
    scalars = jnp.stack([needed, first_row]).astype(jnp.int32)

    def kernel(scalar_ref, q_ref, do_ref, k_ref, v_ref, lt_ref, rd_ref, dq_ref, dkv_ref, dq_acc):
        j = pl.program_id(0)

        @pl.when(j == 0)
        def _():
            dq_acc[...] = jnp.zeros_like(dq_acc)

        def block(masked):
            k = k_ref[...]
            v = v_ref[...]
            k_turned = k.T
            col_pos = j * block_rows + lax.broadcasted_iota(jnp.int32, (block_rows, rows), 0)
            row_pos = scalar_ref[1] + lax.broadcasted_iota(jnp.int32, (block_rows, rows), 1)
            keep = row_pos >= col_pos
            dk = jnp.zeros((block_rows, head_dim), jnp.float32)
            dv = jnp.zeros((block_rows, head_dim), jnp.float32)
            for h in range(heads):
                cols = slice(h * head_dim, (h + 1) * head_dim)
                q = q_ref[:, cols]
                do = do_ref[:, cols]
                s = lax.dot_general(k, q, (((1,), (1,)), ((), ())), preferred_element_type=jnp.float32) * scaling
                if masked:
                    s = jnp.where(keep, s, NEGATIVE)
                p = jnp.exp(s - lt_ref[h : h + 1, :])
                dp = lax.dot_general(v, do, (((1,), (1,)), ((), ())), preferred_element_type=jnp.float32)
                ds = (p * (dp - rd_ref[h : h + 1, :])).astype(jnp.bfloat16)
                dq_acc[cols, :] += jnp.dot(k_turned, ds, preferred_element_type=jnp.float32)
                dk += jnp.dot(ds, q, preferred_element_type=jnp.float32)
                dv += jnp.dot(p.astype(jnp.bfloat16), do, preferred_element_type=jnp.float32)
            dkv_ref[:, :head_dim] = (dk * scaling).astype(dkv_ref.dtype)
            dkv_ref[:, head_dim:] = dv.astype(dkv_ref.dtype)

        below = j * block_rows + block_rows - 1 <= scalar_ref[1]

        @pl.when(jnp.logical_and(j < scalar_ref[0], below))
        def _():
            block(False)

        @pl.when(jnp.logical_and(j < scalar_ref[0], jnp.logical_not(below)))
        def _():
            block(True)

        @pl.when(j >= scalar_ref[0])
        def _():
            dkv_ref[...] = jnp.zeros_like(dkv_ref)

        @pl.when(j == blocks - 1)
        def _():
            dq_ref[...] = (dq_acc[...].T * scaling).astype(dq_ref.dtype)

    def kv_map(j, s):
        return (jnp.minimum(j, s[0] - 1), 0)

    full = lambda j, s: (0, 0)
    grid_spec = pltpu.PrefetchScalarGridSpec(
        num_scalar_prefetch=1,
        grid=(blocks,),
        in_specs=[
            pl.BlockSpec((rows, width), full),
            pl.BlockSpec((rows, width), full),
            pl.BlockSpec((block_rows, head_dim), kv_map),
            pl.BlockSpec((block_rows, head_dim), kv_map),
            pl.BlockSpec((heads, rows), full),
            pl.BlockSpec((heads, rows), full),
        ],
        out_specs=[
            pl.BlockSpec((rows, width), full),
            pl.BlockSpec((block_rows, 2 * head_dim), lambda j, s: (j, 0)),
        ],
        scratch_shapes=[pltpu.VMEM((width, rows), jnp.float32)],
    )
    return pl.pallas_call(
        kernel,
        grid_spec=grid_spec,
        out_shape=[
            jax.ShapeDtypeStruct((rows, width), jnp.bfloat16),
            jax.ShapeDtypeStruct((tokens, 2 * head_dim), jnp.bfloat16),
        ],
        compiler_params=pltpu.CompilerParams(dimension_semantics=("arbitrary",)),
    )(scalars, query_rows, grad_attended, keys_all, values_all, log_total.T, row_dot.T)


def butterfly_gather(value, axis_name):
    size = lax.axis_size(axis_name)
    own = lax.axis_index(axis_name)
    held = value[None]
    stride = size // 2
    bits = 0
    while stride >= 1:
        pairs = [(i, i ^ stride) for i in range(size)]
        other = lax.ppermute(held, axis_name, pairs)
        low = (own & stride) == 0
        held = jnp.where(
            low, jnp.concatenate([held, other], 0), jnp.concatenate([other, held], 0)
        )
        stride //= 2
        bits += 1
    held = held.reshape((2,) * bits + value.shape)
    held = held.transpose(tuple(range(bits))[::-1] + tuple(range(bits, bits + value.ndim)))
    return held.reshape((size * value.shape[0],) + value.shape[1:])


def causal_gather(value, axis_name):
    size = lax.axis_size(axis_name)
    own = lax.axis_index(axis_name)
    received = [value]
    for shift in range(1, size):
        pairs = [(i, i + shift) for i in range(size - shift)]
        received.append(lax.ppermute(value, axis_name, pairs))
    by_shift = jnp.stack(received[::-1], 0)
    doubled = jnp.concatenate([by_shift, by_shift], 0)
    blocks = lax.dynamic_slice_in_dim(doubled, size - 1 - own, size, 0)
    return blocks.reshape((size * value.shape[0],) + value.shape[1:])


def causal_reduce(parts, axis_name):
    size = lax.axis_size(axis_name)
    own = lax.axis_index(axis_name)
    total = lax.dynamic_index_in_dim(parts, own, 0, keepdims=False).astype(jnp.float32)
    for shift in range(1, size):
        pairs = [(i, i - shift) for i in range(shift, size)]
        sent = lax.dynamic_index_in_dim(parts, jnp.maximum(own - shift, 0), 0, keepdims=False)
        total = total + lax.ppermute(sent, axis_name, pairs).astype(jnp.float32)
    return total


def exchange_reduce(parts, axis_name):
    arrived = lax.all_to_all(parts, axis_name, 0, 0, tiled=True)
    return jnp.sum(arrived.astype(jnp.float32), axis=0)


def butterfly_sum(value, axis_name):
    size = lax.axis_size(axis_name)
    stride = 1
    while stride < size:
        pairs = [(i, i ^ stride) for i in range(size)]
        value = value + lax.ppermute(value, axis_name, pairs)
        stride *= 2
    return value


def gram_pair_squares(left_gram, right_side, head_dim):
    rows = right_side.shape[0]
    right_heads = right_side.reshape(rows, right_side.shape[1] // head_dim, head_dim)
    right_gram = jnp.einsum(
        "ihd,jhd->hij", right_heads, right_heads, preferred_element_type=jnp.float32
    )
    return jnp.sum(right_gram * left_gram[None], axis=(1, 2))


def gram_squares(left_side, right_side, head_dim):
    left_gram = lax.dot_general(
        left_side, left_side, (((1,), (1,)), ((), ())), preferred_element_type=jnp.float32
    )
    return gram_pair_squares(left_gram, right_side, head_dim)


def body(hidden_in, query_rows, key_rows, value_rows, out_weight, grad_out, answer_mask):
    tok_dev = query_rows.shape[0]
    head_dim = HD
    group_size = HEADS // KVH
    local_groups = key_rows.shape[1] // head_dim
    scaling = head_dim ** (-0.5)
    own_index = lax.axis_index("ctx")
    first_row = own_index * tok_dev
    loss_weight = 0.25 + answer_mask.astype(jnp.float32)
    weighted = (grad_out.astype(jnp.float32) * loss_weight[:, None]).astype(jnp.bfloat16)
    hidden_gram = butterfly_sum(
        lax.dot_general(
            hidden_in, hidden_in, (((1,), (1,)), ((), ())), preferred_element_type=jnp.float32
        ),
        "head",
    )
    piece_part = (
        lax.all_gather(grad_out, "head", axis=1, tiled=True).astype(jnp.float32)
        * loss_weight[:, None]
    ).astype(jnp.bfloat16)
    pair_all = causal_gather(jnp.concatenate([key_rows, value_rows], axis=1), "ctx")
    kv_width = key_rows.shape[1]
    keys_all, values_all = (pair_all[:, :kv_width], pair_all[:, kv_width:])
    tokens = keys_all.shape[0]
    block_rows = math.gcd(512, tokens)

    def fetch(table, block_number):
        return lax.dynamic_slice_in_dim(table, block_number * block_rows, block_rows, 0)

    def column_pos(block_number):
        return block_number * block_rows + jnp.arange(block_rows, dtype=jnp.int32)

    buffer = jnp.zeros((tokens, 2 * local_groups * head_dim), jnp.float32)
    rows = query_rows.shape[0]
    row_pos = first_row + jnp.arange(rows, dtype=jnp.int32)
    needed = (first_row + rows - 1) // block_rows + 1
    query_heads = query_rows.reshape(rows, local_groups, group_size, head_dim)
    log_totals = []
    shared_head = 0
    query_group = query_heads[:, shared_head]

    def stats_step(block_number, carried):
        running_max, running_sum = carried
        key_block = fetch(keys_all, block_number)
        scores = block_scores(query_group, key_block, scaling, row_pos, column_pos(block_number))
        new_max = jnp.maximum(running_max, jnp.max(scores, axis=-1))
        running_sum = running_sum * jnp.exp(running_max - new_max) + jnp.sum(
            jnp.exp(scores - new_max[..., None]), axis=-1
        )
        return (new_max, running_sum)

    start_max = jnp.full((rows, group_size), NEGATIVE, jnp.float32)
    start_sum = jnp.zeros((rows, group_size), jnp.float32)
    running_max, running_sum = lax.fori_loop(0, needed, stats_step, (start_max, start_sum))
    log_total = running_max + jnp.log(running_sum)

    def value_step(block_number, accumulated):
        key_block = fetch(keys_all, block_number)
        value_block = fetch(values_all, block_number)
        scores = block_scores(query_group, key_block, scaling, row_pos, column_pos(block_number))
        rounded = jnp.exp(scores - log_total[..., None]).astype(jnp.bfloat16)
        return accumulated + jnp.einsum(
            "tgk,kd->tgd", rounded, value_block, preferred_element_type=jnp.float32
        )

    accumulated = lax.fori_loop(
        0, needed, value_step, jnp.zeros((rows, group_size, head_dim), jnp.float32)
    )
    log_totals.append(log_total)
    attended_list = [accumulated.astype(jnp.bfloat16)]
    attended_part = jnp.stack(attended_list, axis=1).reshape(
        rows, local_groups * group_size * head_dim
    )
    log_totals, attended = (log_totals, attended_part)
    grad_sum = lax.dot_general(
        piece_part, out_weight, (((1,), (1,)), ((), ())), preferred_element_type=jnp.float32
    )
    grad_sum, squares_out = (grad_sum, gram_squares(piece_part, attended, head_dim))
    grad_attended, squares_out = (grad_sum.astype(jnp.bfloat16), squares_out)
    backward_buffer = buffer
    rows = query_rows.shape[0]
    backward_row_pos = first_row + jnp.arange(rows, dtype=jnp.int32)
    needed = (first_row + rows - 1) // block_rows + 1
    query_heads = query_rows.reshape(rows, local_groups, group_size, head_dim)
    grad_heads = grad_attended.reshape(rows, local_groups, group_size, head_dim)
    attended_heads = attended.reshape(rows, local_groups, group_size, head_dim)
    shared_head = 0
    backward_query_group = query_heads[:, shared_head]
    grad_group = grad_heads[:, shared_head]
    backward_log_total = log_totals[shared_head]
    row_dot = jnp.sum(
        grad_group.astype(jnp.float32) * attended_heads[:, shared_head].astype(jnp.float32), axis=-1
    )
    grad_query_part, backward_buffer = flash_backward(
        backward_query_group.reshape(rows, group_size * head_dim),
        grad_group.reshape(rows, group_size * head_dim),
        keys_all,
        values_all,
        backward_log_total,
        row_dot,
        first_row,
        head_dim,
        2 * block_rows,
    )
    ctx_size = lax.axis_size("ctx")
    key_sums = exchange_reduce(
        backward_buffer.reshape((ctx_size, tokens // ctx_size) + backward_buffer.shape[1:]), "ctx"
    )
    grad_key = key_sums[:, : local_groups * head_dim].astype(jnp.bfloat16)
    grad_value = key_sums[:, local_groups * head_dim :].astype(jnp.bfloat16)
    squares_query = gram_pair_squares(hidden_gram, grad_query_part, head_dim)
    normal_size = D * head_dim * tok_dev
    fisher_q = jnp.log(squares_query / normal_size + EPSILON).reshape(1, -1)
    fisher_o = jnp.log(squares_out / normal_size + EPSILON).reshape(1, -1)
    return (grad_query_part, grad_key, grad_value, fisher_q, fisher_o)


def solution(mesh):
    return jax.shard_map(
        body,
        mesh=mesh,
        in_specs=(
            P("ctx", "head"),
            P("ctx", "head"),
            P("ctx", "head"),
            P("ctx", "head"),
            P("head", None),
            P("ctx", "head"),
            P("ctx"),
        ),
        out_specs=(
            P("ctx", "head"),
            P("ctx", "head"),
            P("ctx", "head"),
            P("ctx", "head"),
            P("ctx", "head"),
        ),
        check_vma=False,
    )
```

```python
import math

import jax
import jax.numpy as jnp
from jax import lax
from jax.experimental import pallas as pl
from jax.experimental.pallas import tpu as pltpu
from jax.sharding import PartitionSpec as P

D = 8192
HEADS = 64
KVH = 8
HD = 128


NEGATIVE = -1e30
EPSILON = 1e-06


def block_scores(query_group, key_block, scaling, row_pos, col_pos):
    scores = (
        jnp.einsum("tgd,kd->tgk", query_group, key_block, preferred_element_type=jnp.float32)
        * scaling
    )
    return jnp.where(row_pos[:, None, None] >= col_pos[None, None, :], scores, NEGATIVE)


def head_squares(left_side, right_side, head_dim):
    product = lax.dot_general(
        left_side, right_side, (((0,), (0,)), ((), ())), preferred_element_type=jnp.float32
    )
    shaped = (product * product).reshape(
        product.shape[0], right_side.shape[1] // head_dim, head_dim
    )
    return jnp.sum(shaped, axis=(0, 2))


def flash_backward(query_rows, grad_attended, keys_all, values_all, log_total, row_dot, first_row, head_dim, block_rows):
    rows, width = query_rows.shape
    heads = width // head_dim
    tokens = keys_all.shape[0]
    blocks = tokens // block_rows
    scaling = head_dim ** (-0.5)
    needed = (first_row + rows - 1) // block_rows + 1
    scalars = jnp.stack([needed, first_row]).astype(jnp.int32)

    def kernel(scalar_ref, q_ref, do_ref, k_ref, v_ref, lt_ref, rd_ref, dq_ref, dkv_ref, dq_acc):
        j = pl.program_id(0)

        @pl.when(j == 0)
        def _():
            dq_acc[...] = jnp.zeros_like(dq_acc)

        def block(masked):
            k = k_ref[...]
            v = v_ref[...]
            k_turned = k.T
            col_pos = j * block_rows + lax.broadcasted_iota(jnp.int32, (block_rows, rows), 0)
            row_pos = scalar_ref[1] + lax.broadcasted_iota(jnp.int32, (block_rows, rows), 1)
            keep = row_pos >= col_pos
            dk = jnp.zeros((block_rows, head_dim), jnp.float32)
            dv = jnp.zeros((block_rows, head_dim), jnp.float32)
            for h in range(heads):
                cols = slice(h * head_dim, (h + 1) * head_dim)
                q = q_ref[:, cols]
                do = do_ref[:, cols]
                s = lax.dot_general(k, q, (((1,), (1,)), ((), ())), preferred_element_type=jnp.float32) * scaling
                if masked:
                    s = jnp.where(keep, s, NEGATIVE)
                p = jnp.exp(s - lt_ref[h : h + 1, :])
                dp = lax.dot_general(v, do, (((1,), (1,)), ((), ())), preferred_element_type=jnp.float32)
                ds = (p * (dp - rd_ref[h : h + 1, :])).astype(jnp.bfloat16)
                dq_acc[cols, :] += jnp.dot(k_turned, ds, preferred_element_type=jnp.float32)
                dk += jnp.dot(ds, q, preferred_element_type=jnp.float32)
                dv += jnp.dot(p.astype(jnp.bfloat16), do, preferred_element_type=jnp.float32)
            dkv_ref[:, :head_dim] = (dk * scaling).astype(dkv_ref.dtype)
            dkv_ref[:, head_dim:] = dv.astype(dkv_ref.dtype)

        below = j * block_rows + block_rows - 1 <= scalar_ref[1]

        @pl.when(jnp.logical_and(j < scalar_ref[0], below))
        def _():
            block(False)

        @pl.when(jnp.logical_and(j < scalar_ref[0], jnp.logical_not(below)))
        def _():
            block(True)

        @pl.when(j >= scalar_ref[0])
        def _():
            dkv_ref[...] = jnp.zeros_like(dkv_ref)

        @pl.when(j == blocks - 1)
        def _():
            dq_ref[...] = (dq_acc[...].T * scaling).astype(dq_ref.dtype)

    def kv_map(j, s):
        return (jnp.minimum(j, s[0] - 1), 0)

    full = lambda j, s: (0, 0)
    grid_spec = pltpu.PrefetchScalarGridSpec(
        num_scalar_prefetch=1,
        grid=(blocks,),
        in_specs=[
            pl.BlockSpec((rows, width), full),
            pl.BlockSpec((rows, width), full),
            pl.BlockSpec((block_rows, head_dim), kv_map),
            pl.BlockSpec((block_rows, head_dim), kv_map),
            pl.BlockSpec((heads, rows), full),
            pl.BlockSpec((heads, rows), full),
        ],
        out_specs=[
            pl.BlockSpec((rows, width), full),
            pl.BlockSpec((block_rows, 2 * head_dim), lambda j, s: (j, 0)),
        ],
        scratch_shapes=[pltpu.VMEM((width, rows), jnp.float32)],
    )
    return pl.pallas_call(
        kernel,
        grid_spec=grid_spec,
        out_shape=[
            jax.ShapeDtypeStruct((rows, width), jnp.bfloat16),
            jax.ShapeDtypeStruct((tokens, 2 * head_dim), jnp.bfloat16),
        ],
        compiler_params=pltpu.CompilerParams(dimension_semantics=("arbitrary",)),
    )(scalars, query_rows, grad_attended, keys_all, values_all, log_total.T, row_dot.T)


def butterfly_gather(value, axis_name):
    size = lax.axis_size(axis_name)
    own = lax.axis_index(axis_name)
    held = value[None]
    stride = size // 2
    bits = 0
    while stride >= 1:
        pairs = [(i, i ^ stride) for i in range(size)]
        other = lax.ppermute(held, axis_name, pairs)
        low = (own & stride) == 0
        held = jnp.where(
            low, jnp.concatenate([held, other], 0), jnp.concatenate([other, held], 0)
        )
        stride //= 2
        bits += 1
    held = held.reshape((2,) * bits + value.shape)
    held = held.transpose(tuple(range(bits))[::-1] + tuple(range(bits, bits + value.ndim)))
    return held.reshape((size * value.shape[0],) + value.shape[1:])


def causal_gather(value, axis_name):
    size = lax.axis_size(axis_name)
    own = lax.axis_index(axis_name)
    received = [value]
    for shift in range(1, size):
        pairs = [(i, i + shift) for i in range(size - shift)]
        received.append(lax.ppermute(value, axis_name, pairs))
    by_shift = jnp.stack(received[::-1], 0)
    doubled = jnp.concatenate([by_shift, by_shift], 0)
    blocks = lax.dynamic_slice_in_dim(doubled, size - 1 - own, size, 0)
    return blocks.reshape((size * value.shape[0],) + value.shape[1:])


def causal_reduce(parts, axis_name):
    size = lax.axis_size(axis_name)
    own = lax.axis_index(axis_name)
    total = lax.dynamic_index_in_dim(parts, own, 0, keepdims=False).astype(jnp.float32)
    for shift in range(1, size):
        pairs = [(i, i - shift) for i in range(shift, size)]
        sent = lax.dynamic_index_in_dim(parts, jnp.maximum(own - shift, 0), 0, keepdims=False)
        total = total + lax.ppermute(sent, axis_name, pairs).astype(jnp.float32)
    return total


def exchange_gather(value, axis_name):
    size = lax.axis_size(axis_name)
    copies = jnp.broadcast_to(value[None], (size,) + value.shape)
    arrived = lax.all_to_all(copies, axis_name, 0, 0, tiled=True)
    return arrived.reshape((size * value.shape[0],) + value.shape[1:])


def exchange_reduce(parts, axis_name):
    arrived = lax.all_to_all(parts, axis_name, 0, 0, tiled=True)
    return jnp.sum(arrived.astype(jnp.float32), axis=0)


def butterfly_sum(value, axis_name):
    size = lax.axis_size(axis_name)
    stride = 1
    while stride < size:
        pairs = [(i, i ^ stride) for i in range(size)]
        value = value + lax.ppermute(value, axis_name, pairs)
        stride *= 2
    return value


def gram_pair_squares(left_gram, right_side, head_dim):
    rows = right_side.shape[0]
    right_heads = right_side.reshape(rows, right_side.shape[1] // head_dim, head_dim)
    right_gram = jnp.einsum(
        "ihd,jhd->hij", right_heads, right_heads, preferred_element_type=jnp.float32
    )
    return jnp.sum(right_gram * left_gram[None], axis=(1, 2))


def gram_squares(left_side, right_side, head_dim):
    left_gram = lax.dot_general(
        left_side, left_side, (((1,), (1,)), ((), ())), preferred_element_type=jnp.float32
    )
    return gram_pair_squares(left_gram, right_side, head_dim)


def body(hidden_in, query_rows, key_rows, value_rows, out_weight, grad_out, answer_mask):
    tok_dev = query_rows.shape[0]
    head_dim = HD
    group_size = HEADS // KVH
    local_groups = key_rows.shape[1] // head_dim
    scaling = head_dim ** (-0.5)
    own_index = lax.axis_index("ctx")
    first_row = own_index * tok_dev
    loss_weight = 0.25 + answer_mask.astype(jnp.float32)
    weighted = (grad_out.astype(jnp.float32) * loss_weight[:, None]).astype(jnp.bfloat16)
    hidden_gram = butterfly_sum(
        lax.dot_general(
            hidden_in, hidden_in, (((1,), (1,)), ((), ())), preferred_element_type=jnp.float32
        ),
        "head",
    )
    piece_part = (
        lax.all_gather(grad_out, "head", axis=1, tiled=True).astype(jnp.float32)
        * loss_weight[:, None]
    ).astype(jnp.bfloat16)
    pair_all = exchange_gather(jnp.concatenate([key_rows, value_rows], axis=1), "ctx")
    kv_width = key_rows.shape[1]
    keys_all, values_all = (pair_all[:, :kv_width], pair_all[:, kv_width:])
    tokens = keys_all.shape[0]
    block_rows = math.gcd(1024, tokens)

    def fetch(table, block_number):
        return lax.dynamic_slice_in_dim(table, block_number * block_rows, block_rows, 0)

    def column_pos(block_number):
        return block_number * block_rows + jnp.arange(block_rows, dtype=jnp.int32)

    buffer = jnp.zeros((tokens, 2 * local_groups * head_dim), jnp.float32)
    rows = query_rows.shape[0]
    row_pos = first_row + jnp.arange(rows, dtype=jnp.int32)
    needed = (first_row + rows - 1) // block_rows + 1
    query_heads = query_rows.reshape(rows, local_groups, group_size, head_dim)
    log_totals = []
    shared_head = 0
    query_group = query_heads[:, shared_head]

    def stats_step(block_number, carried):
        running_max, running_sum = carried
        key_block = fetch(keys_all, block_number)
        scores = block_scores(query_group, key_block, scaling, row_pos, column_pos(block_number))
        new_max = jnp.maximum(running_max, jnp.max(scores, axis=-1))
        running_sum = running_sum * jnp.exp(running_max - new_max) + jnp.sum(
            jnp.exp(scores - new_max[..., None]), axis=-1
        )
        return (new_max, running_sum)

    start_max = jnp.full((rows, group_size), NEGATIVE, jnp.float32)
    start_sum = jnp.zeros((rows, group_size), jnp.float32)
    running_max, running_sum = lax.fori_loop(0, needed, stats_step, (start_max, start_sum))
    log_total = running_max + jnp.log(running_sum)

    def value_step(block_number, accumulated):
        key_block = fetch(keys_all, block_number)
        value_block = fetch(values_all, block_number)
        scores = block_scores(query_group, key_block, scaling, row_pos, column_pos(block_number))
        rounded = jnp.exp(scores - log_total[..., None]).astype(jnp.bfloat16)
        return accumulated + jnp.einsum(
            "tgk,kd->tgd", rounded, value_block, preferred_element_type=jnp.float32
        )

    accumulated = lax.fori_loop(
        0, needed, value_step, jnp.zeros((rows, group_size, head_dim), jnp.float32)
    )
    log_totals.append(log_total)
    attended_list = [accumulated.astype(jnp.bfloat16)]
    attended_part = jnp.stack(attended_list, axis=1).reshape(
        rows, local_groups * group_size * head_dim
    )
    log_totals, attended = (log_totals, attended_part)
    grad_sum = lax.dot_general(
        piece_part, out_weight, (((1,), (1,)), ((), ())), preferred_element_type=jnp.float32
    )
    grad_sum, squares_out = (grad_sum, gram_squares(piece_part, attended, head_dim))
    grad_attended, squares_out = (grad_sum.astype(jnp.bfloat16), squares_out)
    backward_buffer = buffer
    rows = query_rows.shape[0]
    backward_row_pos = first_row + jnp.arange(rows, dtype=jnp.int32)
    needed = (first_row + rows - 1) // block_rows + 1
    query_heads = query_rows.reshape(rows, local_groups, group_size, head_dim)
    grad_heads = grad_attended.reshape(rows, local_groups, group_size, head_dim)
    attended_heads = attended.reshape(rows, local_groups, group_size, head_dim)
    shared_head = 0
    backward_query_group = query_heads[:, shared_head]
    grad_group = grad_heads[:, shared_head]
    backward_log_total = log_totals[shared_head]
    row_dot = jnp.sum(
        grad_group.astype(jnp.float32) * attended_heads[:, shared_head].astype(jnp.float32), axis=-1
    )
    grad_query_part, backward_buffer = flash_backward(
        backward_query_group.reshape(rows, group_size * head_dim),
        grad_group.reshape(rows, group_size * head_dim),
        keys_all,
        values_all,
        backward_log_total,
        row_dot,
        first_row,
        head_dim,
        block_rows,
    )
    ctx_size = lax.axis_size("ctx")
    key_sums = exchange_reduce(
        backward_buffer.reshape((ctx_size, tokens // ctx_size) + backward_buffer.shape[1:]), "ctx"
    )
    grad_key = key_sums[:, : local_groups * head_dim].astype(jnp.bfloat16)
    grad_value = key_sums[:, local_groups * head_dim :].astype(jnp.bfloat16)
    squares_query = gram_pair_squares(hidden_gram, grad_query_part, head_dim)
    normal_size = D * head_dim * tok_dev
    fisher_q = jnp.log(squares_query / normal_size + EPSILON).reshape(1, -1)
    fisher_o = jnp.log(squares_out / normal_size + EPSILON).reshape(1, -1)
    return (grad_query_part, grad_key, grad_value, fisher_q, fisher_o)


def solution(mesh):
    return jax.shard_map(
        body,
        mesh=mesh,
        in_specs=(
            P("ctx", "head"),
            P("ctx", "head"),
            P("ctx", "head"),
            P("ctx", "head"),
            P("head", None),
            P("ctx", "head"),
            P("ctx"),
        ),
        out_specs=(
            P("ctx", "head"),
            P("ctx", "head"),
            P("ctx", "head"),
            P("ctx", "head"),
            P("ctx", "head"),
        ),
        check_vma=False,
    )
```

```python
import math

import jax
import jax.numpy as jnp
from jax import lax
from jax.experimental import pallas as pl
from jax.experimental.pallas import tpu as pltpu
from jax.sharding import PartitionSpec as P

D = 8192
HEADS = 64
KVH = 8
HD = 128


NEGATIVE = -1e30
EPSILON = 1e-06


def block_scores(query_group, key_block, scaling, row_pos, col_pos):
    scores = (
        jnp.einsum("tgd,kd->tgk", query_group, key_block, preferred_element_type=jnp.float32)
        * scaling
    )
    return jnp.where(row_pos[:, None, None] >= col_pos[None, None, :], scores, NEGATIVE)


def head_squares(left_side, right_side, head_dim):
    product = lax.dot_general(
        left_side, right_side, (((0,), (0,)), ((), ())), preferred_element_type=jnp.float32
    )
    shaped = (product * product).reshape(
        product.shape[0], right_side.shape[1] // head_dim, head_dim
    )
    return jnp.sum(shaped, axis=(0, 2))


def flash_backward(query_rows, grad_attended, keys_all, values_all, log_total, row_dot, first_row, head_dim, block_rows):
    rows, width = query_rows.shape
    heads = width // head_dim
    tokens = keys_all.shape[0]
    blocks = tokens // block_rows
    scaling = head_dim ** (-0.5)
    needed = (first_row + rows - 1) // block_rows + 1
    scalars = jnp.stack([needed, first_row]).astype(jnp.int32)

    def kernel(scalar_ref, q_ref, do_ref, k_ref, v_ref, lt_ref, rd_ref, dq_ref, dkv_ref, dq_acc):
        j = pl.program_id(0)

        @pl.when(j == 0)
        def _():
            dq_acc[...] = jnp.zeros_like(dq_acc)

        def block(masked):
            k = k_ref[...]
            v = v_ref[...]
            k_turned = k.T
            col_pos = j * block_rows + lax.broadcasted_iota(jnp.int32, (block_rows, rows), 0)
            row_pos = scalar_ref[1] + lax.broadcasted_iota(jnp.int32, (block_rows, rows), 1)
            keep = row_pos >= col_pos
            dk = jnp.zeros((block_rows, head_dim), jnp.float32)
            dv = jnp.zeros((block_rows, head_dim), jnp.float32)
            for h in range(heads):
                cols = slice(h * head_dim, (h + 1) * head_dim)
                q = q_ref[:, cols]
                do = do_ref[:, cols]
                s = lax.dot_general(k, q, (((1,), (1,)), ((), ())), preferred_element_type=jnp.float32) * scaling
                if masked:
                    s = jnp.where(keep, s, NEGATIVE)
                p = jnp.exp(s - lt_ref[h : h + 1, :])
                dp = lax.dot_general(v, do, (((1,), (1,)), ((), ())), preferred_element_type=jnp.float32)
                ds = (p * (dp - rd_ref[h : h + 1, :])).astype(jnp.bfloat16)
                dq_acc[cols, :] += jnp.dot(k_turned, ds, preferred_element_type=jnp.float32)
                dk += jnp.dot(ds, q, preferred_element_type=jnp.float32)
                dv += jnp.dot(p.astype(jnp.bfloat16), do, preferred_element_type=jnp.float32)
            dkv_ref[:, :head_dim] = (dk * scaling).astype(dkv_ref.dtype)
            dkv_ref[:, head_dim:] = dv.astype(dkv_ref.dtype)

        below = j * block_rows + block_rows - 1 <= scalar_ref[1]

        @pl.when(jnp.logical_and(j < scalar_ref[0], below))
        def _():
            block(False)

        @pl.when(jnp.logical_and(j < scalar_ref[0], jnp.logical_not(below)))
        def _():
            block(True)

        @pl.when(j >= scalar_ref[0])
        def _():
            dkv_ref[...] = jnp.zeros_like(dkv_ref)

        @pl.when(j == blocks - 1)
        def _():
            dq_ref[...] = (dq_acc[...].T * scaling).astype(dq_ref.dtype)

    def kv_map(j, s):
        return (jnp.minimum(j, s[0] - 1), 0)

    full = lambda j, s: (0, 0)
    grid_spec = pltpu.PrefetchScalarGridSpec(
        num_scalar_prefetch=1,
        grid=(blocks,),
        in_specs=[
            pl.BlockSpec((rows, width), full),
            pl.BlockSpec((rows, width), full),
            pl.BlockSpec((block_rows, head_dim), kv_map),
            pl.BlockSpec((block_rows, head_dim), kv_map),
            pl.BlockSpec((heads, rows), full),
            pl.BlockSpec((heads, rows), full),
        ],
        out_specs=[
            pl.BlockSpec((rows, width), full),
            pl.BlockSpec((block_rows, 2 * head_dim), lambda j, s: (j, 0)),
        ],
        scratch_shapes=[pltpu.VMEM((width, rows), jnp.float32)],
    )
    return pl.pallas_call(
        kernel,
        grid_spec=grid_spec,
        out_shape=[
            jax.ShapeDtypeStruct((rows, width), jnp.bfloat16),
            jax.ShapeDtypeStruct((tokens, 2 * head_dim), jnp.bfloat16),
        ],
        compiler_params=pltpu.CompilerParams(dimension_semantics=("arbitrary",)),
    )(scalars, query_rows, grad_attended, keys_all, values_all, log_total.T, row_dot.T)


def butterfly_gather(value, axis_name):
    size = lax.axis_size(axis_name)
    own = lax.axis_index(axis_name)
    held = value[None]
    stride = size // 2
    bits = 0
    while stride >= 1:
        pairs = [(i, i ^ stride) for i in range(size)]
        other = lax.ppermute(held, axis_name, pairs)
        low = (own & stride) == 0
        held = jnp.where(
            low, jnp.concatenate([held, other], 0), jnp.concatenate([other, held], 0)
        )
        stride //= 2
        bits += 1
    held = held.reshape((2,) * bits + value.shape)
    held = held.transpose(tuple(range(bits))[::-1] + tuple(range(bits, bits + value.ndim)))
    return held.reshape((size * value.shape[0],) + value.shape[1:])


def causal_gather(value, axis_name):
    size = lax.axis_size(axis_name)
    own = lax.axis_index(axis_name)
    received = [value]
    for shift in range(1, size):
        pairs = [(i, i + shift) for i in range(size - shift)]
        received.append(lax.ppermute(value, axis_name, pairs))
    by_shift = jnp.stack(received[::-1], 0)
    doubled = jnp.concatenate([by_shift, by_shift], 0)
    blocks = lax.dynamic_slice_in_dim(doubled, size - 1 - own, size, 0)
    return blocks.reshape((size * value.shape[0],) + value.shape[1:])


def causal_reduce(parts, axis_name):
    size = lax.axis_size(axis_name)
    own = lax.axis_index(axis_name)
    total = lax.dynamic_index_in_dim(parts, own, 0, keepdims=False).astype(jnp.float32)
    for shift in range(1, size):
        pairs = [(i, i - shift) for i in range(shift, size)]
        sent = lax.dynamic_index_in_dim(parts, jnp.maximum(own - shift, 0), 0, keepdims=False)
        total = total + lax.ppermute(sent, axis_name, pairs).astype(jnp.float32)
    return total


def exchange_gather(value, axis_name):
    size = lax.axis_size(axis_name)
    copies = jnp.broadcast_to(value[None], (size,) + value.shape)
    arrived = lax.all_to_all(copies, axis_name, 0, 0, tiled=True)
    return arrived.reshape((size * value.shape[0],) + value.shape[1:])


def exchange_reduce(parts, axis_name):
    arrived = lax.all_to_all(parts, axis_name, 0, 0, tiled=True)
    return jnp.sum(arrived.astype(jnp.float32), axis=0)


def butterfly_sum(value, axis_name):
    size = lax.axis_size(axis_name)
    stride = 1
    while stride < size:
        pairs = [(i, i ^ stride) for i in range(size)]
        value = value + lax.ppermute(value, axis_name, pairs)
        stride *= 2
    return value


def gram_pair_squares(left_gram, right_side, head_dim):
    rows = right_side.shape[0]
    right_heads = right_side.reshape(rows, right_side.shape[1] // head_dim, head_dim)
    right_gram = jnp.einsum(
        "ihd,jhd->hij", right_heads, right_heads, preferred_element_type=jnp.float32
    )
    return jnp.sum(right_gram * left_gram[None], axis=(1, 2))


def gram_squares(left_side, right_side, head_dim):
    left_gram = lax.dot_general(
        left_side, left_side, (((1,), (1,)), ((), ())), preferred_element_type=jnp.float32
    )
    return gram_pair_squares(left_gram, right_side, head_dim)


def body(hidden_in, query_rows, key_rows, value_rows, out_weight, grad_out, answer_mask):
    tok_dev = query_rows.shape[0]
    head_dim = HD
    group_size = HEADS // KVH
    local_groups = key_rows.shape[1] // head_dim
    scaling = head_dim ** (-0.5)
    own_index = lax.axis_index("ctx")
    first_row = own_index * tok_dev
    loss_weight = 0.25 + answer_mask.astype(jnp.float32)
    weighted = (grad_out.astype(jnp.float32) * loss_weight[:, None]).astype(jnp.bfloat16)
    gram_part = lax.dot_general(
        hidden_in, hidden_in, (((1,), (1,)), ((), ())), preferred_element_type=jnp.float32
    )
    piece_part = (
        lax.all_gather(grad_out, "head", axis=1, tiled=True).astype(jnp.float32)
        * loss_weight[:, None]
    ).astype(jnp.bfloat16)
    pair_all = exchange_gather(jnp.concatenate([key_rows, value_rows], axis=1), "ctx")
    gram_part, pair_all = lax.optimization_barrier((gram_part, pair_all))
    hidden_gram = butterfly_sum(gram_part, "head")
    kv_width = key_rows.shape[1]
    keys_all, values_all = (pair_all[:, :kv_width], pair_all[:, kv_width:])
    tokens = keys_all.shape[0]
    block_rows = math.gcd(1024, tokens)

    def fetch(table, block_number):
        return lax.dynamic_slice_in_dim(table, block_number * block_rows, block_rows, 0)

    def column_pos(block_number):
        return block_number * block_rows + jnp.arange(block_rows, dtype=jnp.int32)

    buffer = jnp.zeros((tokens, 2 * local_groups * head_dim), jnp.float32)
    rows = query_rows.shape[0]
    row_pos = first_row + jnp.arange(rows, dtype=jnp.int32)
    needed = (first_row + rows - 1) // block_rows + 1
    query_heads = query_rows.reshape(rows, local_groups, group_size, head_dim)
    log_totals = []
    shared_head = 0
    query_group = query_heads[:, shared_head]

    def stats_step(block_number, carried):
        running_max, running_sum = carried
        key_block = fetch(keys_all, block_number)
        scores = block_scores(query_group, key_block, scaling, row_pos, column_pos(block_number))
        new_max = jnp.maximum(running_max, jnp.max(scores, axis=-1))
        running_sum = running_sum * jnp.exp(running_max - new_max) + jnp.sum(
            jnp.exp(scores - new_max[..., None]), axis=-1
        )
        return (new_max, running_sum)

    start_max = jnp.full((rows, group_size), NEGATIVE, jnp.float32)
    start_sum = jnp.zeros((rows, group_size), jnp.float32)
    running_max, running_sum = lax.fori_loop(0, needed, stats_step, (start_max, start_sum))
    log_total = running_max + jnp.log(running_sum)

    def value_step(block_number, accumulated):
        key_block = fetch(keys_all, block_number)
        value_block = fetch(values_all, block_number)
        scores = block_scores(query_group, key_block, scaling, row_pos, column_pos(block_number))
        rounded = jnp.exp(scores - log_total[..., None]).astype(jnp.bfloat16)
        return accumulated + jnp.einsum(
            "tgk,kd->tgd", rounded, value_block, preferred_element_type=jnp.float32
        )

    accumulated = lax.fori_loop(
        0, needed, value_step, jnp.zeros((rows, group_size, head_dim), jnp.float32)
    )
    log_totals.append(log_total)
    attended_list = [accumulated.astype(jnp.bfloat16)]
    attended_part = jnp.stack(attended_list, axis=1).reshape(
        rows, local_groups * group_size * head_dim
    )
    log_totals, attended = (log_totals, attended_part)
    grad_sum = lax.dot_general(
        piece_part, out_weight, (((1,), (1,)), ((), ())), preferred_element_type=jnp.float32
    )
    grad_sum, squares_out = (grad_sum, gram_squares(piece_part, attended, head_dim))
    grad_attended, squares_out = (grad_sum.astype(jnp.bfloat16), squares_out)
    hidden_gram, grad_attended = lax.optimization_barrier((hidden_gram, grad_attended))
    backward_buffer = buffer
    rows = query_rows.shape[0]
    backward_row_pos = first_row + jnp.arange(rows, dtype=jnp.int32)
    needed = (first_row + rows - 1) // block_rows + 1
    query_heads = query_rows.reshape(rows, local_groups, group_size, head_dim)
    grad_heads = grad_attended.reshape(rows, local_groups, group_size, head_dim)
    attended_heads = attended.reshape(rows, local_groups, group_size, head_dim)
    shared_head = 0
    backward_query_group = query_heads[:, shared_head]
    grad_group = grad_heads[:, shared_head]
    backward_log_total = log_totals[shared_head]
    row_dot = jnp.sum(
        grad_group.astype(jnp.float32) * attended_heads[:, shared_head].astype(jnp.float32), axis=-1
    )
    grad_query_part, backward_buffer = flash_backward(
        backward_query_group.reshape(rows, group_size * head_dim),
        grad_group.reshape(rows, group_size * head_dim),
        keys_all,
        values_all,
        backward_log_total,
        row_dot,
        first_row,
        head_dim,
        block_rows,
    )
    ctx_size = lax.axis_size("ctx")
    key_sums = exchange_reduce(
        backward_buffer.reshape((ctx_size, tokens // ctx_size) + backward_buffer.shape[1:]), "ctx"
    )
    grad_key = key_sums[:, : local_groups * head_dim].astype(jnp.bfloat16)
    grad_value = key_sums[:, local_groups * head_dim :].astype(jnp.bfloat16)
    squares_query = gram_pair_squares(hidden_gram, grad_query_part, head_dim)
    normal_size = D * head_dim * tok_dev
    fisher_q = jnp.log(squares_query / normal_size + EPSILON).reshape(1, -1)
    fisher_o = jnp.log(squares_out / normal_size + EPSILON).reshape(1, -1)
    return (grad_query_part, grad_key, grad_value, fisher_q, fisher_o)


def solution(mesh):
    return jax.shard_map(
        body,
        mesh=mesh,
        in_specs=(
            P("ctx", "head"),
            P("ctx", "head"),
            P("ctx", "head"),
            P("ctx", "head"),
            P("head", None),
            P("ctx", "head"),
            P("ctx"),
        ),
        out_specs=(
            P("ctx", "head"),
            P("ctx", "head"),
            P("ctx", "head"),
            P("ctx", "head"),
            P("ctx", "head"),
        ),
        check_vma=False,
    )
```
